128 devices in a mesh: head: 4 (over x_hi, core), blk: 32 (over y, x_lo, z).
Axes of the slice: x: 4 (x_hi: 2, x_lo: 2; x = x_hi * 2 + x_lo), y: 4, z: 4, core: 2. Of those that a mesh axis runs over, the one named last changes fastest.
Arguments:
- queries: bfloat16 [24576, 32, 128], P(('blk', 'head')), may hold values from -6 to 6
- rotated_keys: bfloat16 [24576, 8, 128], P(('blk', 'head')), may hold values from -6 to 6
- value_vectors: bfloat16 [24576, 8, 128], P(('blk', 'head')), may hold values from -6 to 6
- block_list: int32 [8, 192, 8], replicated, may hold values from 0 to 191, as said below
- grad_out: bfloat16 [24576, 32, 128], P(('blk', 'head')), may hold values from -6 to 6
Outputs:
- attn_out: bfloat16 [24576, 32, 128], P(('blk', 'head'))
- grad_queries: bfloat16 [24576, 32, 128], P(('blk', 'head'))
- key_gradient: bfloat16 [24576, 8, 128], P(('blk', 'head'))
- value_gradient: bfloat16 [24576, 8, 128], P(('blk', 'head'))
The draws below stay inside these ranges and needn't reach their ends.
Inputs may be any that keep to these rules, and one draw needn't show every extreme that they name: Slot 0 of block_list[g, b, :] is b itself; every other slot names a distinct block below b or repeats b. For one head g, the blocks listed by the 6 query blocks of a run (blocks r * 6 to (r + 1) * 6 - 1) lie in that run or, for each earlier run, in one single block of it; the last query block of every run but the first lists a block of the run before.
All inputs are finite; a program needn't handle non-finite values.
Results may differ from the reference program's by a relative error of at most 0.035.
Values may be sent and summed in bfloat16 or wider, within the bound.
No kernel may reach another device: no remote copies, remote signals or barrier semaphores. Data moves between devices by JAX's collectives and lax.ppermute only.
A program may use at most 192 MiB of HBM per device.

```python
import jax
import jax.numpy as jnp
from jax import lax

QUERY_HEADS = 32
KEY_HEADS = 8
HEAD_SIZE = 128
BLOCK_TOKENS = 128
TOPK = 8
SEQUENCE_TOKENS = 24576
RUN_BLOCKS = 6
SEQUENCE_BLOCKS = 192


def draw_queries(key, part):
    array_shape = (SEQUENCE_TOKENS, QUERY_HEADS, HEAD_SIZE)
    base_key = jax.random.fold_in(key, 11)
    base = jnp.clip(jax.random.normal(base_key, array_shape, jnp.float32), -5.0, 5.0)
    return base.astype(jnp.bfloat16)


def draw_rotated_keys(key, part):
    array_shape = (SEQUENCE_TOKENS, KEY_HEADS, HEAD_SIZE)
    base_key = jax.random.fold_in(key, 21)
    base = jnp.clip(jax.random.normal(base_key, array_shape, jnp.float32), -5.0, 5.0)
    return base.astype(jnp.bfloat16)


def draw_block_list(key, part):
    count_runs = SEQUENCE_BLOCKS // RUN_BLOCKS
    pool_random_key = jax.random.fold_in(key, 31)
    score_random_key = jax.random.fold_in(key, 32)
    run_index = jnp.arange(count_runs, dtype=jnp.int32)
    block_pool = run_index[None, None, :] * RUN_BLOCKS + jax.random.randint(pool_random_key, (KEY_HEADS, count_runs, count_runs), 0, RUN_BLOCKS)
    block_ids = jnp.arange(SEQUENCE_BLOCKS, dtype=jnp.int32)
    block_run = block_ids // RUN_BLOCKS
    pool_rows = block_pool[:, block_run, :]
    pool_hit = pool_rows[:, :, block_run] == block_ids[None, None, :]
    same_run = block_run[None, :] == block_run[:, None]
    valid = (block_ids[None, :] < block_ids[:, None])[None] & (same_run[None] | pool_hit)
    forced = ((block_ids % RUN_BLOCKS == RUN_BLOCKS - 1)[:, None] & (block_run[None, :] == block_run[:, None] - 1))[None] & pool_hit
    unsorted_draws = jax.random.randint(score_random_key, (KEY_HEADS, SEQUENCE_BLOCKS, SEQUENCE_BLOCKS), 0, 65536)
    score = jnp.where(forced, 2 ** 30, jnp.where(valid, unsorted_draws * SEQUENCE_BLOCKS + block_ids[None, None, :], -1))
    top_vals, picks = lax.top_k(score, TOPK - 1)
    chosen = jnp.where(top_vals >= 0, picks, block_ids[None, :, None])
    self_block = jnp.broadcast_to(block_ids[None, :, None], (KEY_HEADS, SEQUENCE_BLOCKS, 1))
    return jnp.concatenate([self_block, chosen], axis=-1).astype(jnp.int32)


def steps_of(key, extent, pieces, smallest, largest):
    gain = 1.0
    for dim, shards_of in pieces:
        draws = jax.random.uniform(jax.random.fold_in(jax.random.fold_in(key, 6), dim), (shards_of,), jnp.float32, smallest / len(pieces), largest / len(pieces))
        gain = gain * jnp.repeat(jnp.exp(draws), extent[dim] // shards_of).reshape((-1,) + (1,) * (len(extent) - 1 - dim))
    return gain


def scatter_about(rng, extent, width, bound, shards=(), kind=jnp.bfloat16):
    gain = steps_of(rng, extent, shards, -0.22, 0.18) if shards else 1.0
    array = jax.random.normal(rng, extent, jnp.float32) * width * gain
    return jnp.minimum(jnp.maximum(array, -bound), bound).astype(kind)


def setup_inputs(seed: int = 0) -> dict:
    splits = jax.random.split(jax.random.key(seed), 6)
    return {
        "queries": draw_queries(jax.random.fold_in(splits[5], 71), 0),
        "rotated_keys": draw_rotated_keys(jax.random.fold_in(splits[5], 71), 0),
        "value_vectors": scatter_about(splits[2], (SEQUENCE_TOKENS, KEY_HEADS, HEAD_SIZE), 1.0, 6.0, ((0, 128),)),
        "block_list": draw_block_list(jax.random.fold_in(splits[5], 71), 0),
        "grad_out": scatter_about(splits[4], (SEQUENCE_TOKENS, QUERY_HEADS, HEAD_SIZE), 1.0, 6.0, ((0, 128),)),
    }


def reference(queries, rotated_keys, value_vectors, block_list, grad_out):
    score_scale = HEAD_SIZE ** -0.5
    group_width = QUERY_HEADS // KEY_HEADS
    count_runs = SEQUENCE_BLOCKS // RUN_BLOCKS
    run_len = RUN_BLOCKS * BLOCK_TOKENS
    key_block_rows = rotated_keys.reshape(SEQUENCE_BLOCKS, BLOCK_TOKENS, KEY_HEADS, HEAD_SIZE)
    value_block_rows = value_vectors.reshape(SEQUENCE_BLOCKS, BLOCK_TOKENS, KEY_HEADS, HEAD_SIZE)
    group_index = jnp.arange(KEY_HEADS, dtype=jnp.int32)[:, None, None]
    slot_ids = jnp.arange(TOPK, dtype=jnp.int32)
    earlier = slot_ids[None, :] < slot_ids[:, None]
    offsets = jnp.arange(BLOCK_TOKENS, dtype=jnp.int32)

    def one_run(running_totals, run):
        key_total, value_total = running_totals
        first = (run * run_len).astype(jnp.int32)
        run_query = lax.dynamic_slice_in_dim(queries, first, run_len, 0).astype(jnp.float32)
        run_query = run_query.reshape(RUN_BLOCKS, BLOCK_TOKENS, KEY_HEADS, group_width, HEAD_SIZE)
        run_gradient = lax.dynamic_slice_in_dim(grad_out, first, run_len, 0).astype(jnp.float32)
        run_gradient = run_gradient.reshape(RUN_BLOCKS, BLOCK_TOKENS, KEY_HEADS, group_width, HEAD_SIZE)
        listed = lax.dynamic_slice_in_dim(block_list, (run * RUN_BLOCKS).astype(jnp.int32), RUN_BLOCKS, 1)
        keys_sel = key_block_rows[listed, :, group_index].astype(jnp.float32)
        values_sel = value_block_rows[listed, :, group_index].astype(jnp.float32)
        repeated = jnp.any((listed[..., :, None] == listed[..., None, :]) & earlier, axis=-1)
        query_pos = (run * RUN_BLOCKS + jnp.arange(RUN_BLOCKS, dtype=jnp.int32))[:, None] * BLOCK_TOKENS + offsets
        key_pos = listed[..., None] * BLOCK_TOKENS + offsets
        allowed = (key_pos[:, :, None, :, :] <= query_pos[None, :, :, None, None]) & jnp.logical_not(repeated)[:, :, None, :, None]
        scores = jnp.einsum('nqgjd,gnktd->gnqjkt', run_query, keys_sel) * score_scale
        scores = jnp.where(allowed[:, :, :, None], scores, -jnp.inf)
        row_max = jnp.max(scores, axis=(-2, -1), keepdims=True)
        log_total = row_max + jnp.log(jnp.sum(jnp.exp(scores - row_max), axis=(-2, -1), keepdims=True))
        probs = jnp.exp(scores - log_total)
        probs_b = lax.optimization_barrier(probs.astype(jnp.bfloat16)).astype(jnp.float32)
        output = jnp.einsum('gnqjkt,gnktd->nqgjd', probs_b, values_sel)
        output_b = output.astype(jnp.bfloat16)
        row_dot = jnp.sum(run_gradient * output_b.astype(jnp.float32), axis=-1)
        grad_probs = jnp.einsum('nqgjd,gnktd->gnqjkt', run_gradient, values_sel)
        grad_scores = probs * (grad_probs - jnp.transpose(row_dot, (2, 0, 1, 3))[..., None, None])
        grad_scores_b = lax.optimization_barrier(grad_scores.astype(jnp.bfloat16)).astype(jnp.float32)
        query_grad = (jnp.einsum('gnqjkt,gnktd->nqgjd', grad_scores_b, keys_sel) * score_scale).astype(jnp.bfloat16)
        key_slots = jnp.einsum('gnqjkt,nqgjd->gnktd', grad_scores_b, run_query) * score_scale
        value_slots = jnp.einsum('gnqjkt,nqgjd->gnktd', probs_b, run_gradient)
        complete_zeros = jnp.zeros((SEQUENCE_BLOCKS, KEY_HEADS, BLOCK_TOKENS, HEAD_SIZE), jnp.float32)
        key_part = complete_zeros.at[listed, group_index].add(key_slots)
        value_part = complete_zeros.at[listed, group_index].add(value_slots)
        key_part = lax.optimization_barrier(key_part.astype(jnp.bfloat16)).astype(jnp.float32)
        value_part = lax.optimization_barrier(value_part.astype(jnp.bfloat16)).astype(jnp.float32)
        return (key_total + key_part, value_total + value_part), (output_b.reshape(run_len, QUERY_HEADS, HEAD_SIZE), query_grad.reshape(run_len, QUERY_HEADS, HEAD_SIZE))

    initial_totals = (jnp.zeros((SEQUENCE_BLOCKS, KEY_HEADS, BLOCK_TOKENS, HEAD_SIZE), jnp.float32), jnp.zeros((SEQUENCE_BLOCKS, KEY_HEADS, BLOCK_TOKENS, HEAD_SIZE), jnp.float32))
    running_totals, results = lax.scan(one_run, initial_totals, jnp.arange(count_runs, dtype=jnp.int32))
    attn_out = results[0].reshape(SEQUENCE_TOKENS, QUERY_HEADS, HEAD_SIZE)
    grad_queries = results[1].reshape(SEQUENCE_TOKENS, QUERY_HEADS, HEAD_SIZE)
    key_gradient = jnp.transpose(running_totals[0], (0, 2, 1, 3)).reshape(SEQUENCE_TOKENS, KEY_HEADS, HEAD_SIZE).astype(jnp.bfloat16)
    value_gradient = jnp.transpose(running_totals[1], (0, 2, 1, 3)).reshape(SEQUENCE_TOKENS, KEY_HEADS, HEAD_SIZE).astype(jnp.bfloat16)
    return attn_out, grad_queries, key_gradient, value_gradient
```

```python
import jax
import jax.numpy as jnp
from jax import lax
from jax.sharding import PartitionSpec as P

BLOCK_TOKENS = 128
TOPK = 8


def to_heads(x):
    return lax.all_to_all(x, "head", split_axis=1, concat_axis=0, tiled=True)


def from_heads(x):
    return lax.all_to_all(x, "head", split_axis=0, concat_axis=1, tiled=True)


def split_exact(form, table, slots):
    upper = slots.astype(jnp.bfloat16)
    lower = (slots - upper.astype(jnp.float32)).astype(jnp.bfloat16)
    total = jnp.einsum(form, table, upper, preferred_element_type=jnp.float32)
    return total + jnp.einsum(form, table, lower, preferred_element_type=jnp.float32)


def on_device(queries, rotated_keys, value_vectors, block_list, grad_out):
    query_h = to_heads(queries)
    key_h = to_heads(rotated_keys)
    value_h = to_heads(value_vectors)
    grad_h = to_heads(grad_out)
    run_len, head_count, head_width = query_h.shape
    groups = key_h.shape[1]
    group_width = head_count // groups
    block_ids = run_len // BLOCK_TOKENS
    peers = lax.axis_size("blk")
    rank = lax.axis_index("blk")
    head_rank = lax.axis_index("head")
    score_scale = head_width ** (-0.5)
    offsets = jnp.arange(BLOCK_TOKENS, dtype=jnp.int32)
    block_range = jnp.arange(block_ids, dtype=jnp.int32)
    peer_range = jnp.arange(peers, dtype=jnp.int32)

    lists_here = lax.dynamic_slice_in_dim(block_list, head_rank * groups, groups, 0)
    lists_mine = lax.dynamic_slice_in_dim(lists_here, rank * block_ids, block_ids, 1)
    by_run = lists_here.reshape(groups, peers, block_ids * TOPK)
    in_mine = (by_run // block_ids) == rank
    named = jnp.max(jnp.where(in_mine, by_run % block_ids, -1), axis=-1)
    present = (named >= 0) & (peer_range != rank)[None, :]
    pick_send = (named[:, :, None] == block_range).astype(jnp.bfloat16)

    kv_h = jnp.concatenate([key_h, value_h], axis=1).reshape(
        block_ids, BLOCK_TOKENS, 2, groups, head_width
    )
    send = jnp.einsum(
        "grb,btkgd->rkgtd", pick_send, kv_h, preferred_element_type=jnp.float32
    ).astype(jnp.bfloat16)
    recv = lax.all_to_all(send, "blk", split_axis=0, concat_axis=0, tiled=True)

    owner = lists_mine // block_ids
    is_local = owner == rank
    local_pick = (
        is_local[..., None] & ((lists_mine % block_ids)[..., None] == block_range)
    ).astype(jnp.bfloat16)
    remote_pick = (
        jnp.logical_not(is_local)[..., None] & (owner[..., None] == peer_range)
    ).astype(jnp.bfloat16)
    picked = jnp.einsum(
        "gbsl,ltkgd->kgbstd", local_pick, kv_h, preferred_element_type=jnp.float32
    ) + jnp.einsum(
        "gbsr,rkgtd->kgbstd", remote_pick, recv, preferred_element_type=jnp.float32
    )
    picked = picked.astype(jnp.bfloat16)
    items = groups * block_ids
    key_items = picked[0].reshape(items, TOPK * BLOCK_TOKENS, head_width)
    value_items = picked[1].reshape(items, TOPK * BLOCK_TOKENS, head_width)

    query_items = jnp.transpose(
        query_h.reshape(block_ids, BLOCK_TOKENS, groups, group_width, head_width), (2, 0, 1, 3, 4)
    ).reshape(items, BLOCK_TOKENS * group_width, head_width)
    grad_items = jnp.transpose(
        grad_h.reshape(block_ids, BLOCK_TOKENS, groups, group_width, head_width), (2, 0, 1, 3, 4)
    ).reshape(items, BLOCK_TOKENS * group_width, head_width)

    slot_ids = jnp.arange(TOPK, dtype=jnp.int32)
    earlier = slot_ids[None, :] < slot_ids[:, None]
    repeated = jnp.any((lists_mine[..., :, None] == lists_mine[..., None, :]) & earlier, axis=-1)
    my_blocks = rank * block_ids + block_range
    query_pos = my_blocks[:, None] * BLOCK_TOKENS + offsets
    key_pos = lists_mine[..., None] * BLOCK_TOKENS + offsets
    allowed = (key_pos[:, :, None, :, :] <= query_pos[None, :, :, None, None]) & jnp.logical_not(
        repeated
    )[:, :, None, :, None]
    allowed = allowed.reshape(items, BLOCK_TOKENS, 1, TOPK * BLOCK_TOKENS)

    rows = BLOCK_TOKENS * group_width
    scores = (
        jnp.einsum("ird,icd->irc", query_items, key_items, preferred_element_type=jnp.float32)
        * score_scale
    )
    scores = jnp.where(
        allowed, scores.reshape(items, BLOCK_TOKENS, group_width, -1), -jnp.inf
    ).reshape(items, rows, -1)
    row_max = jnp.max(scores, axis=-1, keepdims=True)
    log_total = row_max + jnp.log(jnp.sum(jnp.exp(scores - row_max), axis=-1, keepdims=True))
    probs = jnp.exp(scores - log_total)
    probs_b = probs.astype(jnp.bfloat16)
    outputs = jnp.einsum(
        "irc,icd->ird", probs_b, value_items, preferred_element_type=jnp.float32
    ).astype(jnp.bfloat16)
    row_dot = jnp.sum(
        grad_items.astype(jnp.float32) * outputs.astype(jnp.float32), axis=-1, keepdims=True
    )
    grad_probs = jnp.einsum(
        "ird,icd->irc", grad_items, value_items, preferred_element_type=jnp.float32
    )
    grad_scores_b = (probs * (grad_probs - row_dot)).astype(jnp.bfloat16)
    query_grads = (
        jnp.einsum("irc,icd->ird", grad_scores_b, key_items, preferred_element_type=jnp.float32)
        * score_scale
    ).astype(jnp.bfloat16)
    key_slots = (
        jnp.einsum("irc,ird->icd", grad_scores_b, query_items, preferred_element_type=jnp.float32)
        * score_scale
    )
    value_slots = jnp.einsum(
        "irc,ird->icd", probs_b, grad_items, preferred_element_type=jnp.float32
    )

    def regroup(result):
        return jnp.transpose(
            result.reshape(groups, block_ids, BLOCK_TOKENS, group_width, head_width),
            (1, 2, 0, 3, 4),
        ).reshape(run_len, head_count, head_width)

    attn_h = regroup(outputs)
    query_grad_h = regroup(query_grads)

    slots_kv = jnp.stack([key_slots, value_slots]).reshape(
        2, groups, block_ids * TOPK, BLOCK_TOKENS, head_width
    )
    to_peer = remote_pick.reshape(groups, block_ids * TOPK, peers)
    to_local = local_pick.reshape(groups, block_ids * TOPK, block_ids)
    remote = split_exact("ger,kgetd->rkgtd", to_peer, slots_kv).astype(jnp.bfloat16)
    local = split_exact("gel,kgetd->ltkgd", to_local, slots_kv).astype(jnp.bfloat16)
    back = lax.all_to_all(remote, "blk", split_axis=0, concat_axis=0, tiled=True)
    take_back = (pick_send * present[..., None].astype(jnp.bfloat16))
    total = lax.optimization_barrier(local).astype(jnp.float32) + jnp.einsum(
        "grl,rkgtd->ltkgd", take_back, back, preferred_element_type=jnp.float32
    )
    total = total.astype(jnp.bfloat16)
    key_grad_h = total[:, :, 0].reshape(run_len, groups, head_width)
    value_grad_h = total[:, :, 1].reshape(run_len, groups, head_width)
    return (
        from_heads(attn_h),
        from_heads(query_grad_h),
        from_heads(key_grad_h),
        from_heads(value_grad_h),
    )


def solution(mesh):
    in_specs = (
        P(("blk", "head"), None, None),
        P(("blk", "head"), None, None),
        P(("blk", "head"), None, None),
        P(),
        P(("blk", "head"), None, None),
    )
    out_specs = (
        P(("blk", "head"), None, None),
        P(("blk", "head"), None, None),
        P(("blk", "head"), None, None),
        P(("blk", "head"), None, None),
    )
    return jax.shard_map(
        on_device, mesh=mesh, in_specs=in_specs, out_specs=out_specs, check_vma=False
    )
```

```python
import jax
import jax.numpy as jnp
from jax import lax
from jax.sharding import PartitionSpec as P
from jax.experimental import pallas as pl
from jax.experimental.pallas import tpu as pltpu

BLOCK_TOKENS = 128
TOPK = 8


def to_heads(x):
    return lax.all_to_all(x, "head", split_axis=1, concat_axis=0, tiled=True)


def from_heads(x):
    return lax.all_to_all(x, "head", split_axis=0, concat_axis=1, tiled=True)


def attention_kernel(src_ref, base_ref, *refs):
    k_refs = refs[:TOPK]
    v_refs = refs[TOPK:2 * TOPK]
    q_ref, do_ref, kpos_ref = refs[2 * TOPK:2 * TOPK + 3]
    o_ref, dq_ref, dk_ref, dv_ref = refs[2 * TOPK + 3:]
    g = pl.program_id(0)
    b = pl.program_id(1)
    blocks = pl.num_programs(1)

    @pl.when((g == 0) & (b == 0))
    def _():
        dk_ref[...] = jnp.zeros_like(dk_ref)
        dv_ref[...] = jnp.zeros_like(dv_ref)

    head_width = k_refs[0].shape[-1]
    group_width = q_ref.shape[-1] // head_width
    scale = head_width ** (-0.5)
    keys = jnp.concatenate([r[...] for r in k_refs], axis=0)
    values = jnp.concatenate([r[...] for r in v_refs], axis=0)
    query_pos = base_ref[b] + lax.broadcasted_iota(jnp.int32, (BLOCK_TOKENS, 1), 0)
    allowed = kpos_ref[...] <= query_pos
    nt = (((1,), (1,)), ((), ()))
    tn = (((0,), (0,)), ((), ()))
    dk = None
    dv = None
    for j in range(group_width):
        cols = slice(j * head_width, (j + 1) * head_width)
        qj = q_ref[:, cols]
        gj = do_ref[:, cols]
        s = lax.dot_general(qj, keys, nt, preferred_element_type=jnp.float32) * scale
        s = jnp.where(allowed, s, -jnp.inf)
        m = jnp.max(s, axis=-1, keepdims=True)
        lt = m + jnp.log(jnp.sum(jnp.exp(s - m), axis=-1, keepdims=True))
        p = jnp.exp(s - lt)
        pb = p.astype(jnp.bfloat16)
        o = jnp.dot(pb, values, preferred_element_type=jnp.float32).astype(jnp.bfloat16)
        o_ref[:, cols] = o
        rd = jnp.sum(gj.astype(jnp.float32) * o.astype(jnp.float32), axis=-1, keepdims=True)
        dp = lax.dot_general(gj, values, nt, preferred_element_type=jnp.float32)
        ds = (p * (dp - rd)).astype(jnp.bfloat16)
        dq = jnp.dot(ds, keys, preferred_element_type=jnp.float32) * scale
        dq_ref[:, cols] = dq.astype(jnp.bfloat16)
        dkj = lax.dot_general(ds, qj, tn, preferred_element_type=jnp.float32)
        dvj = lax.dot_general(pb, gj, tn, preferred_element_type=jnp.float32)
        dk = dkj if dk is None else dk + dkj
        dv = dvj if dv is None else dv + dvj
    dk = dk * scale
    row = (g * blocks + b) * TOPK
    for s in range(TOPK):
        t = src_ref[row + s]
        rows = slice(s * BLOCK_TOKENS, (s + 1) * BLOCK_TOKENS)
        dk_ref[t, g] = dk_ref[t, g] + dk[rows]
        dv_ref[t, g] = dv_ref[t, g] + dv[rows]


def attend(slot_src, query_base, table, q2, do2, key_pos):
    groups = table.shape[2]
    block_ids = q2.shape[0] // BLOCK_TOKENS
    targets = table.shape[0]
    head_width = table.shape[-1]
    row_width = q2.shape[1] // groups

    def slot_spec(s, kv):
        def index(g, b, src, base):
            return (src[(g * block_ids + b) * TOPK + s], kv, g, 0, 0)

        return pl.BlockSpec((None, None, None, BLOCK_TOKENS, head_width), index)

    row_spec = pl.BlockSpec((BLOCK_TOKENS, row_width), lambda g, b, src, base: (b, g))
    pos_spec = pl.BlockSpec((None, None, 1, TOPK * BLOCK_TOKENS), lambda g, b, src, base: (g, b, 0, 0))
    acc_spec = pl.BlockSpec(
        (targets, groups, BLOCK_TOKENS, head_width), lambda g, b, src, base: (0, 0, 0, 0)
    )
    in_specs = (
        [slot_spec(s, 0) for s in range(TOPK)]
        + [slot_spec(s, 1) for s in range(TOPK)]
        + [row_spec, row_spec, pos_spec]
    )
    out_shape = (
        jax.ShapeDtypeStruct(q2.shape, jnp.bfloat16),
        jax.ShapeDtypeStruct(q2.shape, jnp.bfloat16),
        jax.ShapeDtypeStruct((targets, groups, BLOCK_TOKENS, head_width), jnp.float32),
        jax.ShapeDtypeStruct((targets, groups, BLOCK_TOKENS, head_width), jnp.float32),
    )
    grid_spec = pltpu.PrefetchScalarGridSpec(
        num_scalar_prefetch=2,
        grid=(groups, block_ids),
        in_specs=in_specs,
        out_specs=(row_spec, row_spec, acc_spec, acc_spec),
    )
    return pl.pallas_call(
        attention_kernel,
        grid_spec=grid_spec,
        out_shape=out_shape,
        compiler_params=pltpu.CompilerParams(
            dimension_semantics=("arbitrary", "arbitrary"),
            vmem_limit_bytes=48 * 1024 * 1024,
        ),
    )(slot_src, query_base, *([table] * (2 * TOPK)), q2, do2, key_pos)


def on_device(queries, rotated_keys, value_vectors, block_list, grad_out):
    query_h = to_heads(queries)
    key_h = to_heads(rotated_keys)
    value_h = to_heads(value_vectors)
    grad_h = to_heads(grad_out)
    run_len, head_count, head_width = query_h.shape
    groups = key_h.shape[1]
    block_ids = run_len // BLOCK_TOKENS
    peers = lax.axis_size("blk")
    rank = lax.axis_index("blk")
    head_rank = lax.axis_index("head")
    offsets = jnp.arange(BLOCK_TOKENS, dtype=jnp.int32)
    block_range = jnp.arange(block_ids, dtype=jnp.int32)
    peer_range = jnp.arange(peers, dtype=jnp.int32)

    lists_here = lax.dynamic_slice_in_dim(block_list, head_rank * groups, groups, 0)
    lists_mine = lax.dynamic_slice_in_dim(lists_here, rank * block_ids, block_ids, 1)
    by_run = lists_here.reshape(groups, peers, block_ids * TOPK)
    in_mine = (by_run // block_ids) == rank
    named = jnp.max(jnp.where(in_mine, by_run % block_ids, -1), axis=-1)
    present = (named >= 0) & (peer_range != rank)[None, :]
    pick_send = (named[:, :, None] == block_range).astype(jnp.bfloat16)

    kv_local = jnp.transpose(
        jnp.stack([key_h, value_h]).reshape(2, block_ids, BLOCK_TOKENS, groups, head_width),
        (1, 0, 3, 2, 4),
    )
    send = jnp.einsum(
        "grb,bkgtd->rkgtd", pick_send, kv_local, preferred_element_type=jnp.float32
    ).astype(jnp.bfloat16)
    recv = lax.all_to_all(send, "blk", split_axis=0, concat_axis=0, tiled=True)
    table = jnp.concatenate([recv, kv_local], axis=0)

    owner = lists_mine // block_ids
    slot_src = jnp.where(owner == rank, peers + lists_mine % block_ids, owner)
    slot_ids = jnp.arange(TOPK, dtype=jnp.int32)
    earlier = slot_ids[None, :] < slot_ids[:, None]
    repeated = jnp.any((lists_mine[..., :, None] == lists_mine[..., None, :]) & earlier, axis=-1)
    key_pos = lists_mine[..., None] * BLOCK_TOKENS + offsets
    key_pos = jnp.where(repeated[..., None], jnp.int32(2**30), key_pos)
    key_pos = key_pos.reshape(groups, block_ids, 1, TOPK * BLOCK_TOKENS)
    query_base = (rank * block_ids + block_range) * BLOCK_TOKENS

    q2 = query_h.reshape(run_len, head_count * head_width)
    do2 = grad_h.reshape(run_len, head_count * head_width)
    o2, dq2, dk_acc, dv_acc = attend(
        slot_src.reshape(-1), query_base, table, q2, do2, key_pos
    )
    attn_h = o2.reshape(run_len, head_count, head_width)
    query_grad_h = dq2.reshape(run_len, head_count, head_width)

    acc = jnp.stack([dk_acc, dv_acc], axis=1)
    remote = acc[:peers].astype(jnp.bfloat16)
    local = acc[peers:].astype(jnp.bfloat16)
    back = lax.all_to_all(remote, "blk", split_axis=0, concat_axis=0, tiled=True)
    take_back = pick_send * present[..., None].astype(jnp.bfloat16)
    total = local.astype(jnp.float32) + jnp.einsum(
        "grl,rkgtd->lkgtd", take_back, back, preferred_element_type=jnp.float32
    )
    total = jnp.transpose(total.astype(jnp.bfloat16), (1, 0, 3, 2, 4))
    key_grad_h = total[0].reshape(run_len, groups, head_width)
    value_grad_h = total[1].reshape(run_len, groups, head_width)
    return (
        from_heads(attn_h),
        from_heads(query_grad_h),
        from_heads(key_grad_h),
        from_heads(value_grad_h),
    )


def solution(mesh):
    in_specs = (
        P(("blk", "head"), None, None),
        P(("blk", "head"), None, None),
        P(("blk", "head"), None, None),
        P(),
        P(("blk", "head"), None, None),
    )
    out_specs = (
        P(("blk", "head"), None, None),
        P(("blk", "head"), None, None),
        P(("blk", "head"), None, None),
        P(("blk", "head"), None, None),
    )
    return jax.shard_map(
        on_device, mesh=mesh, in_specs=in_specs, out_specs=out_specs, check_vma=False
    )
```

```python
import jax
import jax.numpy as jnp
from jax import lax
from jax.sharding import PartitionSpec as P
from jax.experimental import pallas as pl
from jax.experimental.pallas import tpu as pltpu

BLOCK_TOKENS = 128
TOPK = 8


def to_heads(x):
    return lax.all_to_all(x, "head", split_axis=1, concat_axis=0, tiled=True)


def from_heads(x):
    return lax.all_to_all(x, "head", split_axis=0, concat_axis=1, tiled=True)


def attention_kernel(src_ref, base_ref, *refs):
    k_refs = refs[:TOPK]
    v_refs = refs[TOPK:2 * TOPK]
    q_ref, do_ref, kpos_ref = refs[2 * TOPK:2 * TOPK + 3]
    o_ref, dq_ref, dk_ref, dv_ref = refs[2 * TOPK + 3:]
    b = pl.program_id(0)

    @pl.when(b == 0)
    def _():
        dk_ref[...] = jnp.zeros_like(dk_ref)
        dv_ref[...] = jnp.zeros_like(dv_ref)

    head_width = k_refs[0].shape[-1]
    group_width = q_ref.shape[-1] // head_width
    scale = head_width ** (-0.5)
    keys = jnp.concatenate([r[...] for r in k_refs], axis=0)
    values = jnp.concatenate([r[...] for r in v_refs], axis=0)
    query_pos = base_ref[b] + lax.broadcasted_iota(jnp.int32, (BLOCK_TOKENS, 1), 0)
    allowed = kpos_ref[...] <= query_pos
    nt = (((1,), (1,)), ((), ()))
    tn = (((0,), (0,)), ((), ()))
    dk = None
    dv = None
    for j in range(group_width):
        cols = slice(j * head_width, (j + 1) * head_width)
        qj = q_ref[:, cols]
        gj = do_ref[:, cols]
        s = lax.dot_general(qj, keys, nt, preferred_element_type=jnp.float32) * scale
        s = jnp.where(allowed, s, -jnp.inf)
        m = jnp.max(s, axis=-1, keepdims=True)
        lt = m + jnp.log(jnp.sum(jnp.exp(s - m), axis=-1, keepdims=True))
        p = jnp.exp(s - lt)
        pb = p.astype(jnp.bfloat16)
        o = jnp.dot(pb, values, preferred_element_type=jnp.float32).astype(jnp.bfloat16)
        o_ref[:, cols] = o
        rd = jnp.sum(gj.astype(jnp.float32) * o.astype(jnp.float32), axis=-1, keepdims=True)
        dp = lax.dot_general(gj, values, nt, preferred_element_type=jnp.float32)
        ds = (p * (dp - rd)).astype(jnp.bfloat16)
        dq = jnp.dot(ds, keys, preferred_element_type=jnp.float32) * scale
        dq_ref[:, cols] = dq.astype(jnp.bfloat16)
        dkj = lax.dot_general(ds, qj, tn, preferred_element_type=jnp.float32)
        dvj = lax.dot_general(pb, gj, tn, preferred_element_type=jnp.float32)
        dk = dkj if dk is None else dk + dkj
        dv = dvj if dv is None else dv + dvj
    dk = dk * scale
    for s in range(TOPK):
        t = src_ref[b * TOPK + s]
        rows = slice(s * BLOCK_TOKENS, (s + 1) * BLOCK_TOKENS)
        dk_ref[t] = dk_ref[t] + dk[rows]
        dv_ref[t] = dv_ref[t] + dv[rows]


def attend(slot_src, query_base, table, q2, do2, key_pos, group, groups):
    block_ids = q2.shape[0] // BLOCK_TOKENS
    targets = table.shape[0]
    head_width = table.shape[-1]
    row_width = q2.shape[1] // groups

    def slot_spec(s, kv):
        def index(b, src, base):
            return (src[b * TOPK + s], kv, 0, 0)

        return pl.BlockSpec((None, None, BLOCK_TOKENS, head_width), index)

    in_row = pl.BlockSpec((BLOCK_TOKENS, row_width), lambda b, src, base: (b, group))
    out_row = pl.BlockSpec((BLOCK_TOKENS, row_width), lambda b, src, base: (b, 0))
    pos_spec = pl.BlockSpec((None, 1, TOPK * BLOCK_TOKENS), lambda b, src, base: (b, 0, 0))
    acc_spec = pl.BlockSpec((targets, BLOCK_TOKENS, head_width), lambda b, src, base: (0, 0, 0))
    in_specs = (
        [slot_spec(s, 0) for s in range(TOPK)]
        + [slot_spec(s, 1) for s in range(TOPK)]
        + [in_row, in_row, pos_spec]
    )
    out_shape = (
        jax.ShapeDtypeStruct((q2.shape[0], row_width), jnp.bfloat16),
        jax.ShapeDtypeStruct((q2.shape[0], row_width), jnp.bfloat16),
        jax.ShapeDtypeStruct((targets, BLOCK_TOKENS, head_width), jnp.float32),
        jax.ShapeDtypeStruct((targets, BLOCK_TOKENS, head_width), jnp.float32),
    )
    grid_spec = pltpu.PrefetchScalarGridSpec(
        num_scalar_prefetch=2,
        grid=(block_ids,),
        in_specs=in_specs,
        out_specs=(out_row, out_row, acc_spec, acc_spec),
    )
    return pl.pallas_call(
        attention_kernel,
        grid_spec=grid_spec,
        out_shape=out_shape,
        compiler_params=pltpu.CompilerParams(
            dimension_semantics=("arbitrary",),
            vmem_limit_bytes=48 * 1024 * 1024,
        ),
    )(slot_src, query_base, *([table] * (2 * TOPK)), q2, do2, key_pos)


def on_device(queries, rotated_keys, value_vectors, block_list, grad_out):
    query_h = to_heads(queries)
    key_h = to_heads(rotated_keys)
    value_h = to_heads(value_vectors)
    grad_h = to_heads(grad_out)
    run_len, head_count, head_width = query_h.shape
    groups = key_h.shape[1]
    group_width = head_count // groups
    block_ids = run_len // BLOCK_TOKENS
    peers = lax.axis_size("blk")
    rank = lax.axis_index("blk")
    head_rank = lax.axis_index("head")
    offsets = jnp.arange(BLOCK_TOKENS, dtype=jnp.int32)
    block_range = jnp.arange(block_ids, dtype=jnp.int32)
    peer_range = jnp.arange(peers, dtype=jnp.int32)

    lists_here = lax.dynamic_slice_in_dim(block_list, head_rank * groups, groups, 0)
    lists_mine = lax.dynamic_slice_in_dim(lists_here, rank * block_ids, block_ids, 1)
    by_run = lists_here.reshape(groups, peers, block_ids * TOPK)
    in_mine = (by_run // block_ids) == rank
    named = jnp.max(jnp.where(in_mine, by_run % block_ids, -1), axis=-1)
    present = (named >= 0) & (peer_range != rank)[None, :]
    pick_send = (named[:, :, None] == block_range).astype(jnp.bfloat16)
    take_back = pick_send * present[..., None].astype(jnp.bfloat16)

    kv_local = jnp.transpose(
        jnp.stack([key_h, value_h]).reshape(2, block_ids, BLOCK_TOKENS, groups, head_width),
        (3, 1, 0, 2, 4),
    )
    owner = lists_mine // block_ids
    slot_src = jnp.where(owner == rank, peers + lists_mine % block_ids, owner)
    slot_ids = jnp.arange(TOPK, dtype=jnp.int32)
    earlier = slot_ids[None, :] < slot_ids[:, None]
    repeated = jnp.any((lists_mine[..., :, None] == lists_mine[..., None, :]) & earlier, axis=-1)
    key_pos = lists_mine[..., None] * BLOCK_TOKENS + offsets
    key_pos = jnp.where(repeated[..., None], jnp.int32(2**30), key_pos)
    key_pos = key_pos.reshape(groups, block_ids, 1, TOPK * BLOCK_TOKENS)
    query_base = (rank * block_ids + block_range) * BLOCK_TOKENS

    q2 = query_h.reshape(run_len, head_count * head_width)
    do2 = grad_h.reshape(run_len, head_count * head_width)
    outs, query_grads, key_grads, value_grads = [], [], [], []
    for g in range(groups):
        send = jnp.einsum(
            "rb,bktd->rktd", pick_send[g], kv_local[g], preferred_element_type=jnp.float32
        ).astype(jnp.bfloat16)
        recv = lax.all_to_all(send, "blk", split_axis=0, concat_axis=0, tiled=True)
        table = jnp.concatenate([recv, kv_local[g]], axis=0)
        o_g, dq_g, dk_acc, dv_acc = attend(
            slot_src[g].reshape(-1), query_base, table, q2, do2, key_pos[g], g, groups
        )
        outs.append(o_g)
        query_grads.append(dq_g)
        acc = jnp.stack([dk_acc, dv_acc], axis=1)
        remote = acc[:peers].astype(jnp.bfloat16)
        local = acc[peers:].astype(jnp.bfloat16)
        back = lax.all_to_all(remote, "blk", split_axis=0, concat_axis=0, tiled=True)
        total = local.astype(jnp.float32) + jnp.einsum(
            "rl,rktd->lktd", take_back[g], back, preferred_element_type=jnp.float32
        )
        total = total.astype(jnp.bfloat16)
        key_grads.append(total[:, 0])
        value_grads.append(total[:, 1])

    def heads_layout(parts):
        return jnp.concatenate(parts, axis=1).reshape(run_len, head_count, head_width)

    def group_layout(parts):
        return jnp.stack(parts, axis=2).reshape(run_len, groups, head_width)

    return (
        from_heads(heads_layout(outs)),
        from_heads(heads_layout(query_grads)),
        from_heads(group_layout(key_grads)),
        from_heads(group_layout(value_grads)),
    )


def solution(mesh):
    in_specs = (
        P(("blk", "head"), None, None),
        P(("blk", "head"), None, None),
        P(("blk", "head"), None, None),
        P(),
        P(("blk", "head"), None, None),
    )
    out_specs = (
        P(("blk", "head"), None, None),
        P(("blk", "head"), None, None),
        P(("blk", "head"), None, None),
        P(("blk", "head"), None, None),
    )
    return jax.shard_map(
        on_device, mesh=mesh, in_specs=in_specs, out_specs=out_specs, check_vma=False
    )
```

```python
import jax
import jax.numpy as jnp
from jax import lax
from jax.sharding import PartitionSpec as P
from jax.experimental import pallas as pl
from jax.experimental.pallas import tpu as pltpu

BLOCK_TOKENS = 128
TOPK = 8


def to_heads(*xs):
    return lax.all_to_all(jnp.stack(xs), "head", split_axis=2, concat_axis=1, tiled=True)


def from_heads(*xs):
    both = lax.all_to_all(jnp.stack(xs), "head", split_axis=1, concat_axis=2, tiled=True)
    return tuple(both[i] for i in range(len(xs)))


def attention_kernel(src_ref, base_ref, *refs):
    k_refs = refs[:TOPK]
    v_refs = refs[TOPK:2 * TOPK]
    q_ref, do_ref, kpos_ref = refs[2 * TOPK:2 * TOPK + 3]
    o_ref, dq_ref, dk_ref, dv_ref = refs[2 * TOPK + 3:]
    b = pl.program_id(0)

    @pl.when(b == 0)
    def _():
        dk_ref[...] = jnp.zeros_like(dk_ref)
        dv_ref[...] = jnp.zeros_like(dv_ref)

    head_width = k_refs[0].shape[-1]
    group_width = q_ref.shape[-1] // head_width
    scale = head_width ** (-0.5)
    keys = jnp.concatenate([r[...] for r in k_refs], axis=0)
    values = jnp.concatenate([r[...] for r in v_refs], axis=0)
    query_pos = base_ref[b] + lax.broadcasted_iota(jnp.int32, (BLOCK_TOKENS, 1), 0)
    allowed = kpos_ref[...] <= query_pos
    nt = (((1,), (1,)), ((), ()))
    tn = (((0,), (0,)), ((), ()))
    dk = None
    dv = None
    for j in range(group_width):
        cols = slice(j * head_width, (j + 1) * head_width)
        qj = q_ref[:, cols]
        gj = do_ref[:, cols]
        s = lax.dot_general(qj, keys, nt, preferred_element_type=jnp.float32) * scale
        s = jnp.where(allowed, s, -jnp.inf)
        m = jnp.max(s, axis=-1, keepdims=True)
        lt = m + jnp.log(jnp.sum(jnp.exp(s - m), axis=-1, keepdims=True))
        p = jnp.exp(s - lt)
        pb = p.astype(jnp.bfloat16)
        o = jnp.dot(pb, values, preferred_element_type=jnp.float32).astype(jnp.bfloat16)
        o_ref[:, cols] = o
        rd = jnp.sum(gj.astype(jnp.float32) * o.astype(jnp.float32), axis=-1, keepdims=True)
        dp = lax.dot_general(gj, values, nt, preferred_element_type=jnp.float32)
        ds = (p * (dp - rd)).astype(jnp.bfloat16)
        dq = jnp.dot(ds, keys, preferred_element_type=jnp.float32) * scale
        dq_ref[:, cols] = dq.astype(jnp.bfloat16)
        dkj = lax.dot_general(ds, qj, tn, preferred_element_type=jnp.float32)
        dvj = lax.dot_general(pb, gj, tn, preferred_element_type=jnp.float32)
        dk = dkj if dk is None else dk + dkj
        dv = dvj if dv is None else dv + dvj
    dk = dk * scale
    for s in range(TOPK):
        t = src_ref[b * TOPK + s]
        rows = slice(s * BLOCK_TOKENS, (s + 1) * BLOCK_TOKENS)
        dk_ref[t] = dk_ref[t] + dk[rows]
        dv_ref[t] = dv_ref[t] + dv[rows]


def attend(slot_src, query_base, table, qg2, key_pos, group, groups):
    run_len = qg2.shape[1]
    block_ids = run_len // BLOCK_TOKENS
    targets = table.shape[0]
    head_width = table.shape[-1]
    row_width = qg2.shape[2] // groups

    def slot_spec(s, kv):
        def index(b, src, base):
            return (src[b * TOPK + s], kv, 0, 0)

        return pl.BlockSpec((None, None, BLOCK_TOKENS, head_width), index)

    q_row = pl.BlockSpec((None, BLOCK_TOKENS, row_width), lambda b, src, base: (0, b, group))
    do_row = pl.BlockSpec((None, BLOCK_TOKENS, row_width), lambda b, src, base: (1, b, group))
    out_row = pl.BlockSpec((BLOCK_TOKENS, row_width), lambda b, src, base: (b, 0))
    pos_spec = pl.BlockSpec((None, 1, TOPK * BLOCK_TOKENS), lambda b, src, base: (b, 0, 0))
    acc_spec = pl.BlockSpec((targets, BLOCK_TOKENS, head_width), lambda b, src, base: (0, 0, 0))
    in_specs = (
        [slot_spec(s, 0) for s in range(TOPK)]
        + [slot_spec(s, 1) for s in range(TOPK)]
        + [q_row, do_row, pos_spec]
    )
    out_shape = (
        jax.ShapeDtypeStruct((run_len, row_width), jnp.bfloat16),
        jax.ShapeDtypeStruct((run_len, row_width), jnp.bfloat16),
        jax.ShapeDtypeStruct((targets, BLOCK_TOKENS, head_width), jnp.float32),
        jax.ShapeDtypeStruct((targets, BLOCK_TOKENS, head_width), jnp.float32),
    )
    grid_spec = pltpu.PrefetchScalarGridSpec(
        num_scalar_prefetch=2,
        grid=(block_ids,),
        in_specs=in_specs,
        out_specs=(out_row, out_row, acc_spec, acc_spec),
    )
    return pl.pallas_call(
        attention_kernel,
        grid_spec=grid_spec,
        out_shape=out_shape,
        compiler_params=pltpu.CompilerParams(
            dimension_semantics=("arbitrary",),
            vmem_limit_bytes=48 * 1024 * 1024,
        ),
    )(slot_src, query_base, *([table] * (2 * TOPK)), qg2, qg2, key_pos)


def on_device(queries, rotated_keys, value_vectors, block_list, grad_out):
    kv_h = to_heads(rotated_keys, value_vectors)
    qg_h = to_heads(queries, grad_out)
    _, run_len, head_count, head_width = qg_h.shape
    groups = kv_h.shape[2]
    group_width = head_count // groups
    block_ids = run_len // BLOCK_TOKENS
    peers = lax.axis_size("blk")
    rank = lax.axis_index("blk")
    head_rank = lax.axis_index("head")
    offsets = jnp.arange(BLOCK_TOKENS, dtype=jnp.int32)
    block_range = jnp.arange(block_ids, dtype=jnp.int32)
    peer_range = jnp.arange(peers, dtype=jnp.int32)

    lists_here = lax.dynamic_slice_in_dim(block_list, head_rank * groups, groups, 0)
    lists_mine = lax.dynamic_slice_in_dim(lists_here, rank * block_ids, block_ids, 1)
    by_run = lists_here.reshape(groups, peers, block_ids * TOPK)
    in_mine = (by_run // block_ids) == rank
    named = jnp.max(jnp.where(in_mine, by_run % block_ids, -1), axis=-1)
    present = (named >= 0) & (peer_range != rank)[None, :]
    pick_send = (named[:, :, None] == block_range).astype(jnp.bfloat16)
    take_back = pick_send * present[..., None].astype(jnp.bfloat16)

    kv_local = jnp.transpose(
        kv_h.reshape(2, block_ids, BLOCK_TOKENS, groups, head_width), (3, 1, 0, 2, 4)
    )
    owner = lists_mine // block_ids
    slot_src = jnp.where(owner == rank, peers + lists_mine % block_ids, owner)
    slot_ids = jnp.arange(TOPK, dtype=jnp.int32)
    earlier = slot_ids[None, :] < slot_ids[:, None]
    repeated = jnp.any((lists_mine[..., :, None] == lists_mine[..., None, :]) & earlier, axis=-1)
    key_pos = lists_mine[..., None] * BLOCK_TOKENS + offsets
    key_pos = jnp.where(repeated[..., None], jnp.int32(2**30), key_pos)
    key_pos = key_pos.reshape(groups, block_ids, 1, TOPK * BLOCK_TOKENS)
    query_base = (rank * block_ids + block_range) * BLOCK_TOKENS

    qg2 = qg_h.reshape(2, run_len, head_count * head_width)
    outs, query_grads, key_grads, value_grads = [], [], [], []
    for g in range(groups):
        send = jnp.einsum(
            "rb,bktd->rktd", pick_send[g], kv_local[g], preferred_element_type=jnp.float32
        ).astype(jnp.bfloat16)
        recv = lax.all_to_all(send, "blk", split_axis=0, concat_axis=0, tiled=True)
        table = jnp.concatenate([recv, kv_local[g]], axis=0)
        o_g, dq_g, dk_acc, dv_acc = attend(
            slot_src[g].reshape(-1), query_base, table, qg2, key_pos[g], g, groups
        )
        outs.append(o_g)
        query_grads.append(dq_g)
        acc = jnp.stack([dk_acc, dv_acc], axis=1)
        remote = acc[:peers].astype(jnp.bfloat16)
        local = acc[peers:].astype(jnp.bfloat16)
        back = lax.all_to_all(remote, "blk", split_axis=0, concat_axis=0, tiled=True)
        total = local.astype(jnp.float32) + jnp.einsum(
            "rl,rktd->lktd", take_back[g], back, preferred_element_type=jnp.float32
        )
        total = total.astype(jnp.bfloat16)
        key_grads.append(total[:, 0])
        value_grads.append(total[:, 1])

    def heads_layout(parts):
        return jnp.concatenate(parts, axis=1).reshape(run_len, head_count, head_width)

    def group_layout(parts):
        return jnp.stack(parts, axis=2).reshape(run_len, groups, head_width)

    attn_out, grad_queries = from_heads(heads_layout(outs), heads_layout(query_grads))
    key_gradient, value_gradient = from_heads(group_layout(key_grads), group_layout(value_grads))
    return attn_out, grad_queries, key_gradient, value_gradient


def solution(mesh):
    in_specs = (
        P(("blk", "head"), None, None),
        P(("blk", "head"), None, None),
        P(("blk", "head"), None, None),
        P(),
        P(("blk", "head"), None, None),
    )
    out_specs = (
        P(("blk", "head"), None, None),
        P(("blk", "head"), None, None),
        P(("blk", "head"), None, None),
        P(("blk", "head"), None, None),
    )
    return jax.shard_map(
        on_device, mesh=mesh, in_specs=in_specs, out_specs=out_specs, check_vma=False
    )
```

```python
import jax
import jax.numpy as jnp
from jax import lax
from jax.sharding import PartitionSpec as P
from jax.experimental import pallas as pl
from jax.experimental.pallas import tpu as pltpu

BLOCK_TOKENS = 128
TOPK = 8


def exchange(x, part_axis, out_axis):
    size = lax.axis_size("head")
    here = lax.axis_index("head")
    pieces = []
    for k in range(size):
        piece = lax.dynamic_index_in_dim(x, (here + k) % size, axis=part_axis, keepdims=False)
        if k:
            piece = lax.ppermute(piece, "head", [(i, (i + k) % size) for i in range(size)])
        pieces.append(piece)
    ordered = jnp.stack([pieces[(-s) % size] for s in range(size)], axis=out_axis)
    return jnp.roll(ordered, here, axis=out_axis)


def to_heads(*xs):
    size = lax.axis_size("head")
    x = jnp.stack(xs)
    n, tok, heads, d = x.shape
    x = x.reshape(n, tok, size, heads // size, d)
    return exchange(x, 2, 1).reshape(n, size * tok, heads // size, d)


def from_heads(*xs):
    size = lax.axis_size("head")
    x = jnp.stack(xs)
    n, run, part, d = x.shape
    x = x.reshape(n, size, run // size, part, d)
    both = exchange(x, 1, 2).reshape(n, run // size, size * part, d)
    return tuple(both[i] for i in range(len(xs)))


def attention_kernel(src_ref, base_ref, *refs):
    k_refs = refs[:TOPK]
    v_refs = refs[TOPK:2 * TOPK]
    q_ref, do_ref, kpos_ref = refs[2 * TOPK:2 * TOPK + 3]
    o_ref, dq_ref, dk_ref, dv_ref = refs[2 * TOPK + 3:]
    b = pl.program_id(0)

    @pl.when(b == 0)
    def _():
        dk_ref[...] = jnp.zeros_like(dk_ref)
        dv_ref[...] = jnp.zeros_like(dv_ref)

    head_width = k_refs[0].shape[-1]
    group_width = q_ref.shape[-1] // head_width
    scale = head_width ** (-0.5)
    keys = jnp.concatenate([r[...] for r in k_refs], axis=0)
    values = jnp.concatenate([r[...] for r in v_refs], axis=0)
    query_pos = base_ref[b] + lax.broadcasted_iota(jnp.int32, (BLOCK_TOKENS, 1), 0)
    allowed = kpos_ref[...] <= query_pos
    nt = (((1,), (1,)), ((), ()))
    tn = (((0,), (0,)), ((), ()))
    dk = None
    dv = None
    for j in range(group_width):
        cols = slice(j * head_width, (j + 1) * head_width)
        qj = q_ref[:, cols]
        gj = do_ref[:, cols]
        s = lax.dot_general(qj, keys, nt, preferred_element_type=jnp.float32) * scale
        s = jnp.where(allowed, s, -jnp.inf)
        m = jnp.max(s, axis=-1, keepdims=True)
        lt = m + jnp.log(jnp.sum(jnp.exp(s - m), axis=-1, keepdims=True))
        p = jnp.exp(s - lt)
        pb = p.astype(jnp.bfloat16)
        o = jnp.dot(pb, values, preferred_element_type=jnp.float32).astype(jnp.bfloat16)
        o_ref[:, cols] = o
        rd = jnp.sum(gj.astype(jnp.float32) * o.astype(jnp.float32), axis=-1, keepdims=True)
        dp = lax.dot_general(gj, values, nt, preferred_element_type=jnp.float32)
        ds = (p * (dp - rd)).astype(jnp.bfloat16)
        dq = jnp.dot(ds, keys, preferred_element_type=jnp.float32) * scale
        dq_ref[:, cols] = dq.astype(jnp.bfloat16)
        dkj = lax.dot_general(ds, qj, tn, preferred_element_type=jnp.float32)
        dvj = lax.dot_general(pb, gj, tn, preferred_element_type=jnp.float32)
        dk = dkj if dk is None else dk + dkj
        dv = dvj if dv is None else dv + dvj
    dk = dk * scale
    for s in range(TOPK):
        t = src_ref[b * TOPK + s]
        rows = slice(s * BLOCK_TOKENS, (s + 1) * BLOCK_TOKENS)
        dk_ref[t] = dk_ref[t] + dk[rows]
        dv_ref[t] = dv_ref[t] + dv[rows]


def attend(slot_src, query_base, table, qg2, key_pos, group, groups):
    run_len = qg2.shape[1]
    block_ids = run_len // BLOCK_TOKENS
    targets = table.shape[0]
    head_width = table.shape[-1]
    row_width = qg2.shape[2] // groups

    def slot_spec(s, kv):
        def index(b, src, base):
            return (src[b * TOPK + s], kv, 0, 0)

        return pl.BlockSpec((None, None, BLOCK_TOKENS, head_width), index)

    q_row = pl.BlockSpec((None, BLOCK_TOKENS, row_width), lambda b, src, base: (0, b, group))
    do_row = pl.BlockSpec((None, BLOCK_TOKENS, row_width), lambda b, src, base: (1, b, group))
    out_row = pl.BlockSpec((BLOCK_TOKENS, row_width), lambda b, src, base: (b, 0))
    pos_spec = pl.BlockSpec((None, 1, TOPK * BLOCK_TOKENS), lambda b, src, base: (b, 0, 0))
    acc_spec = pl.BlockSpec((targets, BLOCK_TOKENS, head_width), lambda b, src, base: (0, 0, 0))
    in_specs = (
        [slot_spec(s, 0) for s in range(TOPK)]
        + [slot_spec(s, 1) for s in range(TOPK)]
        + [q_row, do_row, pos_spec]
    )
    out_shape = (
        jax.ShapeDtypeStruct((run_len, row_width), jnp.bfloat16),
        jax.ShapeDtypeStruct((run_len, row_width), jnp.bfloat16),
        jax.ShapeDtypeStruct((targets, BLOCK_TOKENS, head_width), jnp.float32),
        jax.ShapeDtypeStruct((targets, BLOCK_TOKENS, head_width), jnp.float32),
    )
    grid_spec = pltpu.PrefetchScalarGridSpec(
        num_scalar_prefetch=2,
        grid=(block_ids,),
        in_specs=in_specs,
        out_specs=(out_row, out_row, acc_spec, acc_spec),
    )
    return pl.pallas_call(
        attention_kernel,
        grid_spec=grid_spec,
        out_shape=out_shape,
        compiler_params=pltpu.CompilerParams(
            dimension_semantics=("arbitrary",),
            vmem_limit_bytes=48 * 1024 * 1024,
        ),
    )(slot_src, query_base, *([table] * (2 * TOPK)), qg2, qg2, key_pos)


def on_device(queries, rotated_keys, value_vectors, block_list, grad_out):
    kv_h = to_heads(rotated_keys, value_vectors)
    qg_h = to_heads(queries, grad_out)
    _, run_len, head_count, head_width = qg_h.shape
    groups = kv_h.shape[2]
    group_width = head_count // groups
    block_ids = run_len // BLOCK_TOKENS
    peers = lax.axis_size("blk")
    rank = lax.axis_index("blk")
    head_rank = lax.axis_index("head")
    offsets = jnp.arange(BLOCK_TOKENS, dtype=jnp.int32)
    block_range = jnp.arange(block_ids, dtype=jnp.int32)
    peer_range = jnp.arange(peers, dtype=jnp.int32)

    lists_here = lax.dynamic_slice_in_dim(block_list, head_rank * groups, groups, 0)
    lists_mine = lax.dynamic_slice_in_dim(lists_here, rank * block_ids, block_ids, 1)
    by_run = lists_here.reshape(groups, peers, block_ids * TOPK)
    in_mine = (by_run // block_ids) == rank
    named = jnp.max(jnp.where(in_mine, by_run % block_ids, -1), axis=-1)
    present = (named >= 0) & (peer_range != rank)[None, :]
    pick_send = (named[:, :, None] == block_range).astype(jnp.bfloat16)
    take_back = pick_send * present[..., None].astype(jnp.bfloat16)

    kv_local = jnp.transpose(
        kv_h.reshape(2, block_ids, BLOCK_TOKENS, groups, head_width), (3, 1, 0, 2, 4)
    )
    owner = lists_mine // block_ids
    slot_src = jnp.where(owner == rank, peers + lists_mine % block_ids, owner)
    slot_ids = jnp.arange(TOPK, dtype=jnp.int32)
    earlier = slot_ids[None, :] < slot_ids[:, None]
    repeated = jnp.any((lists_mine[..., :, None] == lists_mine[..., None, :]) & earlier, axis=-1)
    key_pos = lists_mine[..., None] * BLOCK_TOKENS + offsets
    key_pos = jnp.where(repeated[..., None], jnp.int32(2**30), key_pos)
    key_pos = key_pos.reshape(groups, block_ids, 1, TOPK * BLOCK_TOKENS)
    query_base = (rank * block_ids + block_range) * BLOCK_TOKENS

    qg2 = qg_h.reshape(2, run_len, head_count * head_width)
    outs, query_grads, key_grads, value_grads = [], [], [], []
    for g in range(groups):
        send = jnp.einsum(
            "rb,bktd->rktd", pick_send[g], kv_local[g], preferred_element_type=jnp.float32
        ).astype(jnp.bfloat16)
        recv = lax.all_to_all(send, "blk", split_axis=0, concat_axis=0, tiled=True)
        table = jnp.concatenate([recv, kv_local[g]], axis=0)
        o_g, dq_g, dk_acc, dv_acc = attend(
            slot_src[g].reshape(-1), query_base, table, qg2, key_pos[g], g, groups
        )
        outs.append(o_g)
        query_grads.append(dq_g)
        acc = jnp.stack([dk_acc, dv_acc], axis=1)
        remote = acc[:peers].astype(jnp.bfloat16)
        local = acc[peers:].astype(jnp.bfloat16)
        back = lax.all_to_all(remote, "blk", split_axis=0, concat_axis=0, tiled=True)
        total = local.astype(jnp.float32) + jnp.einsum(
            "rl,rktd->lktd", take_back[g], back, preferred_element_type=jnp.float32
        )
        total = total.astype(jnp.bfloat16)
        key_grads.append(total[:, 0])
        value_grads.append(total[:, 1])

    def heads_layout(parts):
        return jnp.concatenate(parts, axis=1).reshape(run_len, head_count, head_width)

    def group_layout(parts):
        return jnp.stack(parts, axis=2).reshape(run_len, groups, head_width)

    attn_out, grad_queries = from_heads(heads_layout(outs), heads_layout(query_grads))
    key_gradient, value_gradient = from_heads(group_layout(key_grads), group_layout(value_grads))
    return attn_out, grad_queries, key_gradient, value_gradient


def solution(mesh):
    in_specs = (
        P(("blk", "head"), None, None),
        P(("blk", "head"), None, None),
        P(("blk", "head"), None, None),
        P(),
        P(("blk", "head"), None, None),
    )
    out_specs = (
        P(("blk", "head"), None, None),
        P(("blk", "head"), None, None),
        P(("blk", "head"), None, None),
        P(("blk", "head"), None, None),
    )
    return jax.shard_map(
        on_device, mesh=mesh, in_specs=in_specs, out_specs=out_specs, check_vma=False
    )
```

```python
import jax
import jax.numpy as jnp
from jax import lax
from jax.sharding import PartitionSpec as P
from jax.experimental import pallas as pl
from jax.experimental.pallas import tpu as pltpu

BLOCK_TOKENS = 128
TOPK = 8


def exchange(x, part_axis, out_axis):
    size = lax.axis_size("head")
    here = lax.axis_index("head")
    pieces = []
    for k in range(size):
        piece = lax.dynamic_index_in_dim(x, (here + k) % size, axis=part_axis, keepdims=False)
        if k:
            piece = lax.ppermute(piece, "head", [(i, (i + k) % size) for i in range(size)])
        pieces.append(piece)
    ordered = jnp.stack([pieces[(-s) % size] for s in range(size)], axis=out_axis)
    return jnp.roll(ordered, here, axis=out_axis)


def to_heads(*xs):
    size = lax.axis_size("head")
    x = jnp.stack(xs)
    n, tok, heads, d = x.shape
    x = x.reshape(n, tok, size, heads // size, d)
    return exchange(x, 2, 1).reshape(n, size * tok, heads // size, d)


def from_heads(*xs):
    size = lax.axis_size("head")
    x = jnp.stack(xs)
    n, run, part, d = x.shape
    x = x.reshape(n, size, run // size, part, d)
    both = exchange(x, 1, 2).reshape(n, run // size, size * part, d)
    return tuple(both[i] for i in range(len(xs)))


def attention_kernel(src_ref, base_ref, *refs):
    k_refs = refs[:TOPK]
    v_refs = refs[TOPK:2 * TOPK]
    q_ref, do_ref, kpos_ref = refs[2 * TOPK:2 * TOPK + 3]
    o_ref, dq_ref, dk_ref, dv_ref = refs[2 * TOPK + 3:]
    b = pl.program_id(0)

    @pl.when(b == 0)
    def _():
        dk_ref[...] = jnp.zeros_like(dk_ref)
        dv_ref[...] = jnp.zeros_like(dv_ref)

    head_width = k_refs[0].shape[-1]
    group_width = q_ref.shape[-1] // head_width
    scale = head_width ** (-0.5)
    keys = jnp.concatenate([r[...] for r in k_refs], axis=0)
    values = jnp.concatenate([r[...] for r in v_refs], axis=0)
    query_pos = base_ref[b] + lax.broadcasted_iota(jnp.int32, (BLOCK_TOKENS, 1), 0)
    allowed = kpos_ref[...] <= query_pos
    nt = (((1,), (1,)), ((), ()))
    tn = (((0,), (0,)), ((), ()))
    dk = None
    dv = None
    for j in range(group_width):
        cols = slice(j * head_width, (j + 1) * head_width)
        qj = q_ref[:, cols]
        gj = do_ref[:, cols]
        s = lax.dot_general(qj, keys, nt, preferred_element_type=jnp.float32) * scale
        s = jnp.where(allowed, s, -jnp.inf)
        m = jnp.max(s, axis=-1, keepdims=True)
        lt = m + jnp.log(jnp.sum(jnp.exp(s - m), axis=-1, keepdims=True))
        p = jnp.exp(s - lt)
        pb = p.astype(jnp.bfloat16)
        o = jnp.dot(pb, values, preferred_element_type=jnp.float32).astype(jnp.bfloat16)
        o_ref[:, cols] = o
        rd = jnp.sum(gj.astype(jnp.float32) * o.astype(jnp.float32), axis=-1, keepdims=True)
        dp = lax.dot_general(gj, values, nt, preferred_element_type=jnp.float32)
        ds = (p * (dp - rd)).astype(jnp.bfloat16)
        dq = jnp.dot(ds, keys, preferred_element_type=jnp.float32) * scale
        dq_ref[:, cols] = dq.astype(jnp.bfloat16)
        dkj = lax.dot_general(ds, qj, tn, preferred_element_type=jnp.float32)
        dvj = lax.dot_general(pb, gj, tn, preferred_element_type=jnp.float32)
        dk = dkj if dk is None else dk + dkj
        dv = dvj if dv is None else dv + dvj
    dk = dk * scale
    for s in range(TOPK):
        t = src_ref[b * TOPK + s]
        rows = slice(s * BLOCK_TOKENS, (s + 1) * BLOCK_TOKENS)
        dk_ref[t] = dk_ref[t] + dk[rows]
        dv_ref[t] = dv_ref[t] + dv[rows]


def attend(slot_src, query_base, table, qg2, key_pos, group, groups):
    run_len = qg2.shape[1]
    block_ids = run_len // BLOCK_TOKENS
    targets = table.shape[0]
    head_width = table.shape[-1]
    row_width = qg2.shape[2] // groups

    def slot_spec(s, kv):
        def index(b, src, base):
            return (src[b * TOPK + s], kv, 0, 0)

        return pl.BlockSpec((None, None, BLOCK_TOKENS, head_width), index)

    q_row = pl.BlockSpec((None, BLOCK_TOKENS, row_width), lambda b, src, base: (0, b, group))
    do_row = pl.BlockSpec((None, BLOCK_TOKENS, row_width), lambda b, src, base: (1, b, group))
    out_row = pl.BlockSpec((BLOCK_TOKENS, row_width), lambda b, src, base: (b, 0))
    pos_spec = pl.BlockSpec((None, 1, TOPK * BLOCK_TOKENS), lambda b, src, base: (b, 0, 0))
    acc_spec = pl.BlockSpec((targets, BLOCK_TOKENS, head_width), lambda b, src, base: (0, 0, 0))
    in_specs = (
        [slot_spec(s, 0) for s in range(TOPK)]
        + [slot_spec(s, 1) for s in range(TOPK)]
        + [q_row, do_row, pos_spec]
    )
    out_shape = (
        jax.ShapeDtypeStruct((run_len, row_width), jnp.bfloat16),
        jax.ShapeDtypeStruct((run_len, row_width), jnp.bfloat16),
        jax.ShapeDtypeStruct((targets, BLOCK_TOKENS, head_width), jnp.float32),
        jax.ShapeDtypeStruct((targets, BLOCK_TOKENS, head_width), jnp.float32),
    )
    grid_spec = pltpu.PrefetchScalarGridSpec(
        num_scalar_prefetch=2,
        grid=(block_ids,),
        in_specs=in_specs,
        out_specs=(out_row, out_row, acc_spec, acc_spec),
    )
    return pl.pallas_call(
        attention_kernel,
        grid_spec=grid_spec,
        out_shape=out_shape,
        compiler_params=pltpu.CompilerParams(
            dimension_semantics=("arbitrary",),
            vmem_limit_bytes=48 * 1024 * 1024,
        ),
    )(slot_src, query_base, *([table] * (2 * TOPK)), qg2, qg2, key_pos)


def on_device(queries, rotated_keys, value_vectors, block_list, grad_out):
    kv_h = to_heads(rotated_keys, value_vectors)
    qg_h = to_heads(queries, grad_out)
    _, run_len, head_count, head_width = qg_h.shape
    groups = kv_h.shape[2]
    group_width = head_count // groups
    block_ids = run_len // BLOCK_TOKENS
    peers = lax.axis_size("blk")
    rank = lax.axis_index("blk")
    head_rank = lax.axis_index("head")
    offsets = jnp.arange(BLOCK_TOKENS, dtype=jnp.int32)
    block_range = jnp.arange(block_ids, dtype=jnp.int32)
    peer_range = jnp.arange(peers, dtype=jnp.int32)

    lists_here = lax.dynamic_slice_in_dim(block_list, head_rank * groups, groups, 0)
    lists_mine = lax.dynamic_slice_in_dim(lists_here, rank * block_ids, block_ids, 1)
    by_run = lists_here.reshape(groups, peers, block_ids * TOPK)
    in_mine = (by_run // block_ids) == rank
    named = jnp.max(jnp.where(in_mine, by_run % block_ids, -1), axis=-1)
    present = (named >= 0) & (peer_range != rank)[None, :]
    pick_send = (named[:, :, None] == block_range).astype(jnp.bfloat16)
    take_back = pick_send * present[..., None].astype(jnp.bfloat16)

    kv_local = jnp.transpose(
        kv_h.reshape(2, block_ids, BLOCK_TOKENS, groups, head_width), (3, 1, 0, 2, 4)
    )
    owner = lists_mine // block_ids
    slot_src = jnp.where(owner == rank, peers + lists_mine % block_ids, owner)
    slot_ids = jnp.arange(TOPK, dtype=jnp.int32)
    earlier = slot_ids[None, :] < slot_ids[:, None]
    repeated = jnp.any((lists_mine[..., :, None] == lists_mine[..., None, :]) & earlier, axis=-1)
    key_pos = lists_mine[..., None] * BLOCK_TOKENS + offsets
    key_pos = jnp.where(repeated[..., None], jnp.int32(2**30), key_pos)
    key_pos = key_pos.reshape(groups, block_ids, 1, TOPK * BLOCK_TOKENS)
    query_base = (rank * block_ids + block_range) * BLOCK_TOKENS

    qg2 = qg_h.reshape(2, run_len, head_count * head_width)
    outs, query_grads, backs, locals_ = [], [], [], []
    for g in range(groups):
        send = jnp.einsum(
            "rb,bktd->rktd", pick_send[g], kv_local[g], preferred_element_type=jnp.float32
        ).astype(jnp.bfloat16)
        recv = lax.all_to_all(send, "blk", split_axis=0, concat_axis=0, tiled=True)
        table = jnp.concatenate([recv, kv_local[g]], axis=0)
        o_g, dq_g, dk_acc, dv_acc = attend(
            slot_src[g].reshape(-1), query_base, table, qg2, key_pos[g], g, groups
        )
        outs.append(o_g)
        query_grads.append(dq_g)
        acc = jnp.stack([dk_acc, dv_acc], axis=1)
        remote = acc[:peers].astype(jnp.bfloat16)
        local = acc[peers:].astype(jnp.bfloat16)
        backs.append(lax.all_to_all(remote, "blk", split_axis=0, concat_axis=0, tiled=True))
        locals_.append(local)

    def heads_layout(parts):
        return jnp.concatenate(parts, axis=1).reshape(run_len, head_count, head_width)

    def group_layout(parts):
        return jnp.stack(parts, axis=2).reshape(run_len, groups, head_width)

    attn_all, query_grad_all, backs[-1] = lax.optimization_barrier(
        (heads_layout(outs), heads_layout(query_grads), backs[-1])
    )
    key_grads, value_grads = [], []
    for g in range(groups):
        total = locals_[g].astype(jnp.float32) + jnp.einsum(
            "rl,rktd->lktd", take_back[g], backs[g], preferred_element_type=jnp.float32
        )
        total = total.astype(jnp.bfloat16)
        key_grads.append(total[:, 0])
        value_grads.append(total[:, 1])
    attn_out, grad_queries = from_heads(attn_all, query_grad_all)
    key_gradient, value_gradient = from_heads(group_layout(key_grads), group_layout(value_grads))
    return attn_out, grad_queries, key_gradient, value_gradient


def solution(mesh):
    in_specs = (
        P(("blk", "head"), None, None),
        P(("blk", "head"), None, None),
        P(("blk", "head"), None, None),
        P(),
        P(("blk", "head"), None, None),
    )
    out_specs = (
        P(("blk", "head"), None, None),
        P(("blk", "head"), None, None),
        P(("blk", "head"), None, None),
        P(("blk", "head"), None, None),
    )
    return jax.shard_map(
        on_device, mesh=mesh, in_specs=in_specs, out_specs=out_specs, check_vma=False
    )
```

```python
import jax
import jax.numpy as jnp
from jax import lax
from jax.sharding import PartitionSpec as P
from jax.experimental import pallas as pl
from jax.experimental.pallas import tpu as pltpu

BLOCK_TOKENS = 128
TOPK = 8


def exchange(x, part_axis, out_axis):
    size = lax.axis_size("head")
    here = lax.axis_index("head")
    pieces = []
    for k in range(size):
        piece = lax.dynamic_index_in_dim(x, (here + k) % size, axis=part_axis, keepdims=False)
        if k:
            piece = lax.ppermute(piece, "head", [(i, (i + k) % size) for i in range(size)])
        pieces.append(piece)
    ordered = jnp.stack([pieces[(-s) % size] for s in range(size)], axis=out_axis)
    return jnp.roll(ordered, here, axis=out_axis)


def to_heads(*xs):
    size = lax.axis_size("head")
    x = jnp.stack(xs)
    n, tok, heads, d = x.shape
    x = x.reshape(n, tok, size, heads // size, d)
    return exchange(x, 2, 1).reshape(n, size * tok, heads // size, d)


def from_heads(*xs):
    size = lax.axis_size("head")
    x = jnp.stack(xs)
    n, run, part, d = x.shape
    x = x.reshape(n, size, run // size, part, d)
    both = exchange(x, 1, 2).reshape(n, run // size, size * part, d)
    return tuple(both[i] for i in range(len(xs)))


def attention_kernel(src_ref, base_ref, peer_ref, *refs):
    k_refs = refs[:TOPK]
    v_refs = refs[TOPK:2 * TOPK]
    q_lo, q_hi, do_lo, do_hi, kpos_ref = refs[2 * TOPK:2 * TOPK + 5]
    o_ref, dq_ref, dk_ref, dv_ref = refs[2 * TOPK + 5:]
    b = pl.program_id(0)

    @pl.when(b == 0)
    def _():
        dk_ref[...] = jnp.zeros_like(dk_ref)
        dv_ref[...] = jnp.zeros_like(dv_ref)

    head_width = k_refs[0].shape[-1]
    group_width = q_lo.shape[-1] // head_width
    scale = head_width ** (-0.5)
    keys = jnp.concatenate([r[...] for r in k_refs], axis=0)
    values = jnp.concatenate([r[...] for r in v_refs], axis=0)
    query_pos = base_ref[b] + lax.broadcasted_iota(jnp.int32, (BLOCK_TOKENS, 1), 0)
    allowed = kpos_ref[...] <= query_pos
    nt = (((1,), (1,)), ((), ()))
    tn = (((0,), (0,)), ((), ()))
    dk = None
    dv = None
    for j in range(group_width):
        cols = slice(j * head_width, (j + 1) * head_width)
        qj = jnp.concatenate([q_lo[:, cols], q_hi[:, cols]], axis=0)
        gj = jnp.concatenate([do_lo[:, cols], do_hi[:, cols]], axis=0)
        s = lax.dot_general(qj, keys, nt, preferred_element_type=jnp.float32) * scale
        s = jnp.where(allowed, s, -jnp.inf)
        m = jnp.max(s, axis=-1, keepdims=True)
        lt = m + jnp.log(jnp.sum(jnp.exp(s - m), axis=-1, keepdims=True))
        p = jnp.exp(s - lt)
        pb = p.astype(jnp.bfloat16)
        o = jnp.dot(pb, values, preferred_element_type=jnp.float32).astype(jnp.bfloat16)
        o_ref[:, cols] = o
        rd = jnp.sum(gj.astype(jnp.float32) * o.astype(jnp.float32), axis=-1, keepdims=True)
        dp = lax.dot_general(gj, values, nt, preferred_element_type=jnp.float32)
        ds = (p * (dp - rd)).astype(jnp.bfloat16)
        dq = jnp.dot(ds, keys, preferred_element_type=jnp.float32) * scale
        dq_ref[:, cols] = dq.astype(jnp.bfloat16)
        dkj = lax.dot_general(ds, qj, tn, preferred_element_type=jnp.float32)
        dvj = lax.dot_general(pb, gj, tn, preferred_element_type=jnp.float32)
        dk = dkj if dk is None else dk + dkj
        dv = dvj if dv is None else dv + dvj
    dk = dk * scale
    for s in range(TOPK):
        t = src_ref[b * TOPK + s]
        rows = slice(s * BLOCK_TOKENS, (s + 1) * BLOCK_TOKENS)
        dk_ref[t] = dk_ref[t] + dk[rows]
        dv_ref[t] = dv_ref[t] + dv[rows]


def attend(slot_src, query_base, peer_of, table, pieces, key_pos, group, groups):
    piece_len = pieces.shape[2]
    run_len = pieces.shape[0] * piece_len
    block_ids = run_len // BLOCK_TOKENS
    targets = table.shape[0]
    head_width = table.shape[-1]
    row_width = pieces.shape[-1] // groups
    half = BLOCK_TOKENS // 2
    per_piece = piece_len // half

    def half_spec(which, part):
        def index(b, src, base, peer):
            i = 2 * b + part
            return (peer[i // per_piece], which, i % per_piece, group)

        return pl.BlockSpec((None, None, half, row_width), index)

    def slot_spec(s, kv):
        def index(b, src, base, peer):
            return (src[b * TOPK + s], kv, 0, 0)

        return pl.BlockSpec((None, None, BLOCK_TOKENS, head_width), index)

    out_row = pl.BlockSpec((BLOCK_TOKENS, row_width), lambda b, src, base, peer: (b, 0))
    pos_spec = pl.BlockSpec((None, 1, TOPK * BLOCK_TOKENS), lambda b, src, base, peer: (b, 0, 0))
    acc_spec = pl.BlockSpec((targets, BLOCK_TOKENS, head_width), lambda b, src, base, peer: (0, 0, 0))
    in_specs = (
        [slot_spec(s, 0) for s in range(TOPK)]
        + [slot_spec(s, 1) for s in range(TOPK)]
        + [half_spec(0, 0), half_spec(0, 1), half_spec(1, 0), half_spec(1, 1), pos_spec]
    )
    out_shape = (
        jax.ShapeDtypeStruct((run_len, row_width), jnp.bfloat16),
        jax.ShapeDtypeStruct((run_len, row_width), jnp.bfloat16),
        jax.ShapeDtypeStruct((targets, BLOCK_TOKENS, head_width), jnp.float32),
        jax.ShapeDtypeStruct((targets, BLOCK_TOKENS, head_width), jnp.float32),
    )
    grid_spec = pltpu.PrefetchScalarGridSpec(
        num_scalar_prefetch=3,
        grid=(block_ids,),
        in_specs=in_specs,
        out_specs=(out_row, out_row, acc_spec, acc_spec),
    )
    return pl.pallas_call(
        attention_kernel,
        grid_spec=grid_spec,
        out_shape=out_shape,
        compiler_params=pltpu.CompilerParams(
            dimension_semantics=("arbitrary",),
            vmem_limit_bytes=48 * 1024 * 1024,
        ),
    )(slot_src, query_base, peer_of, *([table] * (2 * TOPK)), *([pieces] * 4), key_pos)


def on_device(queries, rotated_keys, value_vectors, block_list, grad_out):
    kv_h = to_heads(rotated_keys, value_vectors)
    size = lax.axis_size("head")
    here = lax.axis_index("head")
    tok, head_count, head_width = queries.shape
    run_len = size * tok
    groups = kv_h.shape[2]
    group_width = head_count // size // groups
    qg = jnp.stack([queries, grad_out]).reshape(2, tok, size, head_count // size * head_width)
    qg = jnp.transpose(qg, (2, 0, 1, 3))
    pieces = []
    for k in range(size):
        piece = lax.dynamic_index_in_dim(qg, (here + k) % size, axis=0, keepdims=False)
        if k:
            piece = lax.ppermute(piece, "head", [(i, (i + k) % size) for i in range(size)])
        pieces.append(piece)
    qg_pieces = jnp.stack(pieces)
    peer_of = (here - jnp.arange(size, dtype=jnp.int32)) % size
    head_count = head_count // size
    block_ids = run_len // BLOCK_TOKENS
    peers = lax.axis_size("blk")
    rank = lax.axis_index("blk")
    head_rank = lax.axis_index("head")
    offsets = jnp.arange(BLOCK_TOKENS, dtype=jnp.int32)
    block_range = jnp.arange(block_ids, dtype=jnp.int32)
    peer_range = jnp.arange(peers, dtype=jnp.int32)

    lists_here = lax.dynamic_slice_in_dim(block_list, head_rank * groups, groups, 0)
    lists_mine = lax.dynamic_slice_in_dim(lists_here, rank * block_ids, block_ids, 1)
    by_run = lists_here.reshape(groups, peers, block_ids * TOPK)
    in_mine = (by_run // block_ids) == rank
    named = jnp.max(jnp.where(in_mine, by_run % block_ids, -1), axis=-1)
    present = (named >= 0) & (peer_range != rank)[None, :]
    pick_send = (named[:, :, None] == block_range).astype(jnp.bfloat16)
    take_back = pick_send * present[..., None].astype(jnp.bfloat16)

    kv_local = jnp.transpose(
        kv_h.reshape(2, block_ids, BLOCK_TOKENS, groups, head_width), (3, 1, 0, 2, 4)
    )
    owner = lists_mine // block_ids
    slot_src = jnp.where(owner == rank, peers + lists_mine % block_ids, owner)
    slot_ids = jnp.arange(TOPK, dtype=jnp.int32)
    earlier = slot_ids[None, :] < slot_ids[:, None]
    repeated = jnp.any((lists_mine[..., :, None] == lists_mine[..., None, :]) & earlier, axis=-1)
    key_pos = lists_mine[..., None] * BLOCK_TOKENS + offsets
    key_pos = jnp.where(repeated[..., None], jnp.int32(2**30), key_pos)
    key_pos = key_pos.reshape(groups, block_ids, 1, TOPK * BLOCK_TOKENS)
    query_base = (rank * block_ids + block_range) * BLOCK_TOKENS

    outs, query_grads, backs, locals_ = [], [], [], []
    for g in range(groups):
        send = jnp.einsum(
            "rb,bktd->rktd", pick_send[g], kv_local[g], preferred_element_type=jnp.float32
        ).astype(jnp.bfloat16)
        recv = lax.all_to_all(send, "blk", split_axis=0, concat_axis=0, tiled=True)
        table = jnp.concatenate([recv, kv_local[g]], axis=0)
        o_g, dq_g, dk_acc, dv_acc = attend(
            slot_src[g].reshape(-1), query_base, peer_of, table, qg_pieces, key_pos[g], g, groups
        )
        outs.append(o_g)
        query_grads.append(dq_g)
        acc = jnp.stack([dk_acc, dv_acc], axis=1)
        remote = acc[:peers].astype(jnp.bfloat16)
        local = acc[peers:].astype(jnp.bfloat16)
        backs.append(lax.all_to_all(remote, "blk", split_axis=0, concat_axis=0, tiled=True))
        locals_.append(local)

    def heads_layout(parts):
        return jnp.concatenate(parts, axis=1).reshape(run_len, head_count, head_width)

    def group_layout(parts):
        return jnp.stack(parts, axis=2).reshape(run_len, groups, head_width)

    attn_all, query_grad_all, backs[-1] = lax.optimization_barrier(
        (heads_layout(outs), heads_layout(query_grads), backs[-1])
    )
    key_grads, value_grads = [], []
    for g in range(groups):
        total = locals_[g].astype(jnp.float32) + jnp.einsum(
            "rl,rktd->lktd", take_back[g], backs[g], preferred_element_type=jnp.float32
        )
        total = total.astype(jnp.bfloat16)
        key_grads.append(total[:, 0])
        value_grads.append(total[:, 1])
    attn_out, grad_queries = from_heads(attn_all, query_grad_all)
    key_gradient, value_gradient = from_heads(group_layout(key_grads), group_layout(value_grads))
    return attn_out, grad_queries, key_gradient, value_gradient


def solution(mesh):
    in_specs = (
        P(("blk", "head"), None, None),
        P(("blk", "head"), None, None),
        P(("blk", "head"), None, None),
        P(),
        P(("blk", "head"), None, None),
    )
    out_specs = (
        P(("blk", "head"), None, None),
        P(("blk", "head"), None, None),
        P(("blk", "head"), None, None),
        P(("blk", "head"), None, None),
    )
    return jax.shard_map(
        on_device, mesh=mesh, in_specs=in_specs, out_specs=out_specs, check_vma=False
    )
```

```python
import jax
import jax.numpy as jnp
from jax import lax
from jax.sharding import PartitionSpec as P
from jax.experimental import pallas as pl
from jax.experimental.pallas import tpu as pltpu

BLOCK_TOKENS = 128
TOPK = 8


def exchange(x, part_axis, out_axis):
    size = lax.axis_size("head")
    here = lax.axis_index("head")
    pieces = []
    for k in range(size):
        piece = lax.dynamic_index_in_dim(x, (here + k) % size, axis=part_axis, keepdims=False)
        if k:
            piece = lax.ppermute(piece, "head", [(i, (i + k) % size) for i in range(size)])
        pieces.append(piece)
    ordered = jnp.stack([pieces[(-s) % size] for s in range(size)], axis=out_axis)
    return jnp.roll(ordered, here, axis=out_axis)


def to_heads(x):
    size = lax.axis_size("head")
    n, tok, heads, d = x.shape
    x = x.reshape(n, tok, size, heads // size, d)
    return exchange(x, 2, 1).reshape(n, size * tok, heads // size, d)


def from_heads(*xs):
    size = lax.axis_size("head")
    x = jnp.stack(xs)
    n, run, part, d = x.shape
    x = x.reshape(n, size, run // size, part, d)
    both = exchange(x, 1, 2).reshape(n, run // size, size * part, d)
    return tuple(both[i] for i in range(len(xs)))


def attention_kernel(src_ref, base_ref, peer_ref, *refs):
    k_refs = refs[:TOPK]
    v_refs = refs[TOPK:2 * TOPK]
    q_lo, q_hi, do_lo, do_hi, kpos_ref = refs[2 * TOPK:2 * TOPK + 5]
    o_ref, dq_ref, dk_ref, dv_ref = refs[2 * TOPK + 5:]
    b = pl.program_id(0)

    @pl.when(b == 0)
    def _():
        dk_ref[...] = jnp.zeros_like(dk_ref)
        dv_ref[...] = jnp.zeros_like(dv_ref)

    head_width = k_refs[0].shape[-1]
    group_width = q_lo.shape[-1] // head_width
    scale = head_width ** (-0.5)
    keys = jnp.concatenate([r[...] for r in k_refs], axis=0)
    values = jnp.concatenate([r[...] for r in v_refs], axis=0)
    query_pos = base_ref[b] + lax.broadcasted_iota(jnp.int32, (BLOCK_TOKENS, 1), 0)
    allowed = kpos_ref[...] <= query_pos
    nt = (((1,), (1,)), ((), ()))
    tn = (((0,), (0,)), ((), ()))
    dk = None
    dv = None
    for j in range(group_width):
        cols = slice(j * head_width, (j + 1) * head_width)
        qj = jnp.concatenate([q_lo[:, cols], q_hi[:, cols]], axis=0)
        gj = jnp.concatenate([do_lo[:, cols], do_hi[:, cols]], axis=0)
        s = lax.dot_general(qj, keys, nt, preferred_element_type=jnp.float32) * scale
        s = jnp.where(allowed, s, -jnp.inf)
        m = jnp.max(s, axis=-1, keepdims=True)
        lt = m + jnp.log(jnp.sum(jnp.exp(s - m), axis=-1, keepdims=True))
        p = jnp.exp(s - lt)
        pb = p.astype(jnp.bfloat16)
        o = jnp.dot(pb, values, preferred_element_type=jnp.float32).astype(jnp.bfloat16)
        o_ref[:, cols] = o
        rd = jnp.sum(gj.astype(jnp.float32) * o.astype(jnp.float32), axis=-1, keepdims=True)
        dp = lax.dot_general(gj, values, nt, preferred_element_type=jnp.float32)
        ds = (p * (dp - rd)).astype(jnp.bfloat16)
        dq = jnp.dot(ds, keys, preferred_element_type=jnp.float32) * scale
        dq_ref[:, cols] = dq.astype(jnp.bfloat16)
        dkj = lax.dot_general(ds, qj, tn, preferred_element_type=jnp.float32)
        dvj = lax.dot_general(pb, gj, tn, preferred_element_type=jnp.float32)
        dk = dkj if dk is None else dk + dkj
        dv = dvj if dv is None else dv + dvj
    dk = dk * scale
    for s in range(TOPK):
        t = src_ref[b * TOPK + s]
        rows = slice(s * BLOCK_TOKENS, (s + 1) * BLOCK_TOKENS)
        dk_ref[t] = dk_ref[t] + dk[rows]
        dv_ref[t] = dv_ref[t] + dv[rows]


def attend(slot_src, query_base, peer_of, table, pieces, key_pos, group, groups):
    piece_len = pieces.shape[2]
    run_len = pieces.shape[0] * piece_len
    block_ids = run_len // BLOCK_TOKENS
    targets = table.shape[0]
    head_width = table.shape[-1]
    row_width = pieces.shape[-1] // groups
    half = BLOCK_TOKENS // 2
    per_piece = piece_len // half

    def half_spec(which, part):
        def index(b, src, base, peer):
            i = 2 * b + part
            return (peer[i // per_piece], which, i % per_piece, group)

        return pl.BlockSpec((None, None, half, row_width), index)

    def slot_spec(s, kv):
        def index(b, src, base, peer):
            return (src[b * TOPK + s], kv, 0, 0)

        return pl.BlockSpec((None, None, BLOCK_TOKENS, head_width), index)

    out_row = pl.BlockSpec((BLOCK_TOKENS, row_width), lambda b, src, base, peer: (b, 0))
    pos_spec = pl.BlockSpec((None, 1, TOPK * BLOCK_TOKENS), lambda b, src, base, peer: (b, 0, 0))
    acc_spec = pl.BlockSpec((targets, BLOCK_TOKENS, head_width), lambda b, src, base, peer: (0, 0, 0))
    in_specs = (
        [slot_spec(s, 0) for s in range(TOPK)]
        + [slot_spec(s, 1) for s in range(TOPK)]
        + [half_spec(0, 0), half_spec(0, 1), half_spec(1, 0), half_spec(1, 1), pos_spec]
    )
    out_shape = (
        jax.ShapeDtypeStruct((run_len, row_width), jnp.bfloat16),
        jax.ShapeDtypeStruct((run_len, row_width), jnp.bfloat16),
        jax.ShapeDtypeStruct((targets, BLOCK_TOKENS, head_width), jnp.float32),
        jax.ShapeDtypeStruct((targets, BLOCK_TOKENS, head_width), jnp.float32),
    )
    grid_spec = pltpu.PrefetchScalarGridSpec(
        num_scalar_prefetch=3,
        grid=(block_ids,),
        in_specs=in_specs,
        out_specs=(out_row, out_row, acc_spec, acc_spec),
    )
    return pl.pallas_call(
        attention_kernel,
        grid_spec=grid_spec,
        out_shape=out_shape,
        compiler_params=pltpu.CompilerParams(
            dimension_semantics=("arbitrary",),
            vmem_limit_bytes=48 * 1024 * 1024,
        ),
    )(slot_src, query_base, peer_of, *([table] * (2 * TOPK)), *([pieces] * 4), key_pos)


def on_device(queries, rotated_keys, value_vectors, block_list, grad_out):
    size = lax.axis_size("head")
    here = lax.axis_index("head")
    tok, head_count, head_width = queries.shape
    run_len = size * tok
    groups = rotated_keys.shape[1] // size
    group_width = head_count // size // groups
    qg = jnp.stack([queries, grad_out]).reshape(2, tok, size, head_count // size * head_width)
    qg = jnp.transpose(qg, (2, 0, 1, 3))
    kv, qg = lax.optimization_barrier((jnp.stack([rotated_keys, value_vectors]), qg))
    kv_h = to_heads(kv)
    pieces = []
    for k in range(size):
        piece = lax.dynamic_index_in_dim(qg, (here + k) % size, axis=0, keepdims=False)
        if k:
            piece = lax.ppermute(piece, "head", [(i, (i + k) % size) for i in range(size)])
        pieces.append(piece)
    qg_pieces = jnp.stack(pieces)
    peer_of = (here - jnp.arange(size, dtype=jnp.int32)) % size
    head_count = head_count // size
    block_ids = run_len // BLOCK_TOKENS
    peers = lax.axis_size("blk")
    rank = lax.axis_index("blk")
    head_rank = lax.axis_index("head")
    offsets = jnp.arange(BLOCK_TOKENS, dtype=jnp.int32)
    block_range = jnp.arange(block_ids, dtype=jnp.int32)
    peer_range = jnp.arange(peers, dtype=jnp.int32)

    lists_here = lax.dynamic_slice_in_dim(block_list, head_rank * groups, groups, 0)
    lists_mine = lax.dynamic_slice_in_dim(lists_here, rank * block_ids, block_ids, 1)
    by_run = lists_here.reshape(groups, peers, block_ids * TOPK)
    in_mine = (by_run // block_ids) == rank
    named = jnp.max(jnp.where(in_mine, by_run % block_ids, -1), axis=-1)
    present = (named >= 0) & (peer_range != rank)[None, :]
    pick_send = (named[:, :, None] == block_range).astype(jnp.bfloat16)
    take_back = pick_send * present[..., None].astype(jnp.bfloat16)

    kv_local = jnp.transpose(
        kv_h.reshape(2, block_ids, BLOCK_TOKENS, groups, head_width), (3, 1, 0, 2, 4)
    )
    owner = lists_mine // block_ids
    slot_src = jnp.where(owner == rank, peers + lists_mine % block_ids, owner)
    slot_ids = jnp.arange(TOPK, dtype=jnp.int32)
    earlier = slot_ids[None, :] < slot_ids[:, None]
    repeated = jnp.any((lists_mine[..., :, None] == lists_mine[..., None, :]) & earlier, axis=-1)
    key_pos = lists_mine[..., None] * BLOCK_TOKENS + offsets
    key_pos = jnp.where(repeated[..., None], jnp.int32(2**30), key_pos)
    key_pos = key_pos.reshape(groups, block_ids, 1, TOPK * BLOCK_TOKENS)
    query_base = (rank * block_ids + block_range) * BLOCK_TOKENS

    outs, query_grads, backs, locals_ = [], [], [], []
    for g in range(groups):
        send = jnp.einsum(
            "rb,bktd->rktd", pick_send[g], kv_local[g], preferred_element_type=jnp.float32
        ).astype(jnp.bfloat16)
        recv = lax.all_to_all(send, "blk", split_axis=0, concat_axis=0, tiled=True)
        table = jnp.concatenate([recv, kv_local[g]], axis=0)
        o_g, dq_g, dk_acc, dv_acc = attend(
            slot_src[g].reshape(-1), query_base, peer_of, table, qg_pieces, key_pos[g], g, groups
        )
        outs.append(o_g)
        query_grads.append(dq_g)
        acc = jnp.stack([dk_acc, dv_acc], axis=1)
        remote = acc[:peers].astype(jnp.bfloat16)
        local = acc[peers:].astype(jnp.bfloat16)
        backs.append(lax.all_to_all(remote, "blk", split_axis=0, concat_axis=0, tiled=True))
        locals_.append(local)

    def heads_layout(parts):
        return jnp.concatenate(parts, axis=1).reshape(run_len, head_count, head_width)

    def group_layout(parts):
        return jnp.stack(parts, axis=2).reshape(run_len, groups, head_width)

    attn_all, query_grad_all, backs[-1] = lax.optimization_barrier(
        (heads_layout(outs), heads_layout(query_grads), backs[-1])
    )
    key_grads, value_grads = [], []
    for g in range(groups):
        total = locals_[g].astype(jnp.float32) + jnp.einsum(
            "rl,rktd->lktd", take_back[g], backs[g], preferred_element_type=jnp.float32
        )
        total = total.astype(jnp.bfloat16)
        key_grads.append(total[:, 0])
        value_grads.append(total[:, 1])
    attn_out, grad_queries = from_heads(attn_all, query_grad_all)
    key_gradient, value_gradient = from_heads(group_layout(key_grads), group_layout(value_grads))
    return attn_out, grad_queries, key_gradient, value_gradient


def solution(mesh):
    in_specs = (
        P(("blk", "head"), None, None),
        P(("blk", "head"), None, None),
        P(("blk", "head"), None, None),
        P(),
        P(("blk", "head"), None, None),
    )
    out_specs = (
        P(("blk", "head"), None, None),
        P(("blk", "head"), None, None),
        P(("blk", "head"), None, None),
        P(("blk", "head"), None, None),
    )
    return jax.shard_map(
        on_device, mesh=mesh, in_specs=in_specs, out_specs=out_specs, check_vma=False
    )
```

```python
import jax
import jax.numpy as jnp
from jax import lax
from jax.sharding import PartitionSpec as P
from jax.experimental import pallas as pl
from jax.experimental.pallas import tpu as pltpu

BLOCK_TOKENS = 128
TOPK = 8


def exchange(x, part_axis, out_axis):
    size = lax.axis_size("head")
    here = lax.axis_index("head")
    pieces = []
    for k in range(size):
        piece = lax.dynamic_index_in_dim(x, (here + k) % size, axis=part_axis, keepdims=False)
        if k:
            piece = lax.ppermute(piece, "head", [(i, (i + k) % size) for i in range(size)])
        pieces.append(piece)
    ordered = jnp.stack([pieces[(-s) % size] for s in range(size)], axis=out_axis)
    return jnp.roll(ordered, here, axis=out_axis)


def to_heads(*xs):
    size = lax.axis_size("head")
    x = jnp.stack(xs)
    n, tok, heads, d = x.shape
    x = x.reshape(n, tok, size, heads // size, d)
    return exchange(x, 2, 1).reshape(n, size * tok, heads // size, d)


def from_heads(*xs):
    size = lax.axis_size("head")
    x = jnp.stack(xs)
    n, run, part, d = x.shape
    x = x.reshape(n, size, run // size, part, d)
    both = exchange(x, 1, 2).reshape(n, run // size, size * part, d)
    return tuple(both[i] for i in range(len(xs)))


def attention_kernel(src_ref, base_ref, peer_ref, *refs):
    k_refs = refs[:TOPK]
    v_refs = refs[TOPK:2 * TOPK]
    q_lo, q_hi, do_lo, do_hi, kpos_ref = refs[2 * TOPK:2 * TOPK + 5]
    o_ref, dq_ref, dk_ref, dv_ref = refs[2 * TOPK + 5:]
    b = pl.program_id(0)

    @pl.when(b == 0)
    def _():
        dk_ref[...] = jnp.zeros_like(dk_ref)
        dv_ref[...] = jnp.zeros_like(dv_ref)

    head_width = k_refs[0].shape[-1]
    group_width = q_lo.shape[-1] // head_width
    scale = head_width ** (-0.5)
    keys = jnp.concatenate([r[...] for r in k_refs], axis=0)
    values = jnp.concatenate([r[...] for r in v_refs], axis=0)
    query_pos = base_ref[b] + lax.broadcasted_iota(jnp.int32, (BLOCK_TOKENS, 1), 0)
    allowed = kpos_ref[...] <= query_pos
    nt = (((1,), (1,)), ((), ()))
    tn = (((0,), (0,)), ((), ()))
    dk = None
    dv = None
    for j in range(group_width):
        cols = slice(j * head_width, (j + 1) * head_width)
        qj = jnp.concatenate([q_lo[:, cols], q_hi[:, cols]], axis=0)
        gj = jnp.concatenate([do_lo[:, cols], do_hi[:, cols]], axis=0)
        s = lax.dot_general(qj, keys, nt, preferred_element_type=jnp.float32)
        s = jnp.where(allowed, s, -jnp.inf)
        m = jnp.max(s, axis=-1, keepdims=True)
        e = jnp.exp((s - m) * scale)
        p = e * (1.0 / jnp.sum(e, axis=-1, keepdims=True))
        pb = p.astype(jnp.bfloat16)
        o = jnp.dot(pb, values, preferred_element_type=jnp.float32).astype(jnp.bfloat16)
        o_ref[:, cols] = o
        rd = jnp.sum(gj.astype(jnp.float32) * o.astype(jnp.float32), axis=-1, keepdims=True)
        dp = lax.dot_general(gj, values, nt, preferred_element_type=jnp.float32)
        ds = (p * (dp - rd)).astype(jnp.bfloat16)
        dq = jnp.dot(ds, keys, preferred_element_type=jnp.float32) * scale
        dq_ref[:, cols] = dq.astype(jnp.bfloat16)
        dkj = lax.dot_general(ds, qj, tn, preferred_element_type=jnp.float32)
        dvj = lax.dot_general(pb, gj, tn, preferred_element_type=jnp.float32)
        dk = dkj if dk is None else dk + dkj
        dv = dvj if dv is None else dv + dvj
    dk = dk * scale
    for s in range(TOPK):
        t = src_ref[b * TOPK + s]
        rows = slice(s * BLOCK_TOKENS, (s + 1) * BLOCK_TOKENS)
        dk_ref[t] = dk_ref[t] + dk[rows]
        dv_ref[t] = dv_ref[t] + dv[rows]


def attend(slot_src, query_base, peer_of, table, pieces, key_pos, group, groups):
    piece_len = pieces.shape[2]
    run_len = pieces.shape[0] * piece_len
    block_ids = run_len // BLOCK_TOKENS
    targets = table.shape[0]
    head_width = table.shape[-1]
    row_width = pieces.shape[-1] // groups
    half = BLOCK_TOKENS // 2
    per_piece = piece_len // half

    def half_spec(which, part):
        def index(b, src, base, peer):
            i = 2 * b + part
            return (peer[i // per_piece], which, i % per_piece, group)

        return pl.BlockSpec((None, None, half, row_width), index)

    def slot_spec(s, kv):
        def index(b, src, base, peer):
            return (src[b * TOPK + s], kv, 0, 0)

        return pl.BlockSpec((None, None, BLOCK_TOKENS, head_width), index)

    out_row = pl.BlockSpec((BLOCK_TOKENS, row_width), lambda b, src, base, peer: (b, 0))
    pos_spec = pl.BlockSpec((None, 1, TOPK * BLOCK_TOKENS), lambda b, src, base, peer: (b, 0, 0))
    acc_spec = pl.BlockSpec((targets, BLOCK_TOKENS, head_width), lambda b, src, base, peer: (0, 0, 0))
    in_specs = (
        [slot_spec(s, 0) for s in range(TOPK)]
        + [slot_spec(s, 1) for s in range(TOPK)]
        + [half_spec(0, 0), half_spec(0, 1), half_spec(1, 0), half_spec(1, 1), pos_spec]
    )
    out_shape = (
        jax.ShapeDtypeStruct((run_len, row_width), jnp.bfloat16),
        jax.ShapeDtypeStruct((run_len, row_width), jnp.bfloat16),
        jax.ShapeDtypeStruct((targets, BLOCK_TOKENS, head_width), jnp.float32),
        jax.ShapeDtypeStruct((targets, BLOCK_TOKENS, head_width), jnp.float32),
    )
    grid_spec = pltpu.PrefetchScalarGridSpec(
        num_scalar_prefetch=3,
        grid=(block_ids,),
        in_specs=in_specs,
        out_specs=(out_row, out_row, acc_spec, acc_spec),
    )
    return pl.pallas_call(
        attention_kernel,
        grid_spec=grid_spec,
        out_shape=out_shape,
        compiler_params=pltpu.CompilerParams(
            dimension_semantics=("arbitrary",),
            vmem_limit_bytes=48 * 1024 * 1024,
        ),
    )(slot_src, query_base, peer_of, *([table] * (2 * TOPK)), *([pieces] * 4), key_pos)


def on_device(queries, rotated_keys, value_vectors, block_list, grad_out):
    kv_h = to_heads(rotated_keys, value_vectors)
    size = lax.axis_size("head")
    here = lax.axis_index("head")
    tok, head_count, head_width = queries.shape
    run_len = size * tok
    groups = kv_h.shape[2]
    group_width = head_count // size // groups
    qg = jnp.stack([queries, grad_out]).reshape(2, tok, size, head_count // size * head_width)
    qg = jnp.transpose(qg, (2, 0, 1, 3))
    pieces = []
    for k in range(size):
        piece = lax.dynamic_index_in_dim(qg, (here + k) % size, axis=0, keepdims=False)
        if k:
            piece = lax.ppermute(piece, "head", [(i, (i + k) % size) for i in range(size)])
        pieces.append(piece)
    qg_pieces = jnp.stack(pieces)
    peer_of = (here - jnp.arange(size, dtype=jnp.int32)) % size
    head_count = head_count // size
    block_ids = run_len // BLOCK_TOKENS
    peers = lax.axis_size("blk")
    rank = lax.axis_index("blk")
    head_rank = lax.axis_index("head")
    offsets = jnp.arange(BLOCK_TOKENS, dtype=jnp.int32)
    block_range = jnp.arange(block_ids, dtype=jnp.int32)
    peer_range = jnp.arange(peers, dtype=jnp.int32)

    lists_here = lax.dynamic_slice_in_dim(block_list, head_rank * groups, groups, 0)
    lists_mine = lax.dynamic_slice_in_dim(lists_here, rank * block_ids, block_ids, 1)
    by_run = lists_here.reshape(groups, peers, block_ids * TOPK)
    in_mine = (by_run // block_ids) == rank
    named = jnp.max(jnp.where(in_mine, by_run % block_ids, -1), axis=-1)
    present = (named >= 0) & (peer_range != rank)[None, :]
    pick_send = (named[:, :, None] == block_range).astype(jnp.bfloat16)
    take_back = pick_send * present[..., None].astype(jnp.bfloat16)

    kv_local = jnp.transpose(
        kv_h.reshape(2, block_ids, BLOCK_TOKENS, groups, head_width), (3, 1, 0, 2, 4)
    )
    owner = lists_mine // block_ids
    slot_src = jnp.where(owner == rank, peers + lists_mine % block_ids, owner)
    slot_ids = jnp.arange(TOPK, dtype=jnp.int32)
    earlier = slot_ids[None, :] < slot_ids[:, None]
    repeated = jnp.any((lists_mine[..., :, None] == lists_mine[..., None, :]) & earlier, axis=-1)
    key_pos = lists_mine[..., None] * BLOCK_TOKENS + offsets
    key_pos = jnp.where(repeated[..., None], jnp.int32(2**30), key_pos)
    key_pos = key_pos.reshape(groups, block_ids, 1, TOPK * BLOCK_TOKENS)
    query_base = (rank * block_ids + block_range) * BLOCK_TOKENS

    outs, query_grads, backs, locals_ = [], [], [], []
    for g in range(groups):
        send = jnp.einsum(
            "rb,bktd->rktd", pick_send[g], kv_local[g], preferred_element_type=jnp.float32
        ).astype(jnp.bfloat16)
        recv = lax.all_to_all(send, "blk", split_axis=0, concat_axis=0, tiled=True)
        table = jnp.concatenate([recv, kv_local[g]], axis=0)
        o_g, dq_g, dk_acc, dv_acc = attend(
            slot_src[g].reshape(-1), query_base, peer_of, table, qg_pieces, key_pos[g], g, groups
        )
        outs.append(o_g)
        query_grads.append(dq_g)
        acc = jnp.stack([dk_acc, dv_acc], axis=1)
        remote = acc[:peers].astype(jnp.bfloat16)
        local = acc[peers:].astype(jnp.bfloat16)
        backs.append(lax.all_to_all(remote, "blk", split_axis=0, concat_axis=0, tiled=True))
        locals_.append(local)

    def heads_layout(parts):
        return jnp.concatenate(parts, axis=1).reshape(run_len, head_count, head_width)

    def group_layout(parts):
        return jnp.stack(parts, axis=2).reshape(run_len, groups, head_width)

    attn_all, query_grad_all, backs[-1] = lax.optimization_barrier(
        (heads_layout(outs), heads_layout(query_grads), backs[-1])
    )
    key_grads, value_grads = [], []
    for g in range(groups):
        total = locals_[g].astype(jnp.float32) + jnp.einsum(
            "rl,rktd->lktd", take_back[g], backs[g], preferred_element_type=jnp.float32
        )
        total = total.astype(jnp.bfloat16)
        key_grads.append(total[:, 0])
        value_grads.append(total[:, 1])
    attn_out, grad_queries = from_heads(attn_all, query_grad_all)
    key_gradient, value_gradient = from_heads(group_layout(key_grads), group_layout(value_grads))
    return attn_out, grad_queries, key_gradient, value_gradient


def solution(mesh):
    in_specs = (
        P(("blk", "head"), None, None),
        P(("blk", "head"), None, None),
        P(("blk", "head"), None, None),
        P(),
        P(("blk", "head"), None, None),
    )
    out_specs = (
        P(("blk", "head"), None, None),
        P(("blk", "head"), None, None),
        P(("blk", "head"), None, None),
        P(("blk", "head"), None, None),
    )
    return jax.shard_map(
        on_device, mesh=mesh, in_specs=in_specs, out_specs=out_specs, check_vma=False
    )
```

```python
import jax
import jax.numpy as jnp
from jax import lax
from jax.sharding import PartitionSpec as P
from jax.experimental import pallas as pl
from jax.experimental.pallas import tpu as pltpu

BLOCK_TOKENS = 128
TOPK = 8


def exchange(x, part_axis, out_axis):
    size = lax.axis_size("head")
    here = lax.axis_index("head")
    pieces = []
    for k in range(size):
        piece = lax.dynamic_index_in_dim(x, (here + k) % size, axis=part_axis, keepdims=False)
        if k:
            piece = lax.ppermute(piece, "head", [(i, (i + k) % size) for i in range(size)])
        pieces.append(piece)
    ordered = jnp.stack([pieces[(-s) % size] for s in range(size)], axis=out_axis)
    return jnp.roll(ordered, here, axis=out_axis)


def to_heads(*xs):
    size = lax.axis_size("head")
    x = jnp.stack(xs)
    n, tok, heads, d = x.shape
    x = x.reshape(n, tok, size, heads // size, d)
    return exchange(x, 2, 1).reshape(n, size * tok, heads // size, d)


def from_heads(*xs):
    size = lax.axis_size("head")
    x = jnp.stack(xs)
    n, run, part, d = x.shape
    x = x.reshape(n, size, run // size, part, d)
    both = exchange(x, 1, 2).reshape(n, run // size, size * part, d)
    return tuple(both[i] for i in range(len(xs)))


def attention_kernel(src_ref, base_ref, peer_ref, *refs):
    k_refs = refs[:TOPK]
    v_refs = refs[TOPK:2 * TOPK]
    q_lo, q_hi, do_lo, do_hi, kpos_ref = refs[2 * TOPK:2 * TOPK + 5]
    o_ref, dq_ref, dk_ref, dv_ref = refs[2 * TOPK + 5:]
    b = pl.program_id(0)

    @pl.when(b == 0)
    def _():
        dk_ref[...] = jnp.zeros_like(dk_ref)
        dv_ref[...] = jnp.zeros_like(dv_ref)

    head_width = k_refs[0].shape[-1]
    group_width = q_lo.shape[-1] // head_width
    scale = head_width ** (-0.5)
    keys = jnp.concatenate([r[...] for r in k_refs], axis=0)
    values = jnp.concatenate([r[...] for r in v_refs], axis=0)
    query_pos = base_ref[b] + lax.broadcasted_iota(jnp.int32, (BLOCK_TOKENS, 1), 0)
    allowed = kpos_ref[...] <= query_pos
    nt = (((1,), (1,)), ((), ()))
    tn = (((0,), (0,)), ((), ()))
    dk = None
    dv = None
    for j in range(group_width):
        cols = slice(j * head_width, (j + 1) * head_width)
        qj = jnp.concatenate([q_lo[:, cols], q_hi[:, cols]], axis=0)
        gj = jnp.concatenate([do_lo[:, cols], do_hi[:, cols]], axis=0)
        s = lax.dot_general(qj, keys, nt, preferred_element_type=jnp.float32)
        s = jnp.where(allowed, s, -jnp.inf)
        m = jnp.max(s, axis=-1, keepdims=True)
        e = jnp.exp((s - m) * scale)
        p = e * (1.0 / jnp.sum(e, axis=-1, keepdims=True))
        pb = p.astype(jnp.bfloat16)
        o = jnp.dot(pb, values, preferred_element_type=jnp.float32).astype(jnp.bfloat16)
        o_ref[:, cols] = o
        rd = jnp.sum(gj.astype(jnp.float32) * o.astype(jnp.float32), axis=-1, keepdims=True)
        dp = lax.dot_general(gj, values, nt, preferred_element_type=jnp.float32)
        ds = (p * (dp - rd)).astype(jnp.bfloat16)
        dq = jnp.dot(ds, keys, preferred_element_type=jnp.float32) * scale
        dq_ref[:, cols] = dq.astype(jnp.bfloat16)
        dkj = lax.dot_general(ds, qj, tn, preferred_element_type=jnp.float32)
        dvj = lax.dot_general(pb, gj, tn, preferred_element_type=jnp.float32)
        dk = dkj if dk is None else dk + dkj
        dv = dvj if dv is None else dv + dvj
    dk = dk * scale
    for s in range(TOPK):
        t = src_ref[b * TOPK + s]
        rows = slice(s * BLOCK_TOKENS, (s + 1) * BLOCK_TOKENS)
        dk_ref[t] = dk_ref[t] + dk[rows]
        dv_ref[t] = dv_ref[t] + dv[rows]


def attend(slot_src, query_base, peer_of, table, pieces, key_pos, group, groups):
    piece_len = pieces.shape[2]
    run_len = pieces.shape[0] * piece_len
    block_ids = run_len // BLOCK_TOKENS
    targets = table.shape[0]
    head_width = table.shape[-1]
    row_width = pieces.shape[-1] // groups
    half = BLOCK_TOKENS // 2
    per_piece = piece_len // half

    def half_spec(which, part):
        def index(b, src, base, peer):
            i = 2 * b + part
            return (peer[i // per_piece], which, i % per_piece, group)

        return pl.BlockSpec((None, None, half, row_width), index)

    def slot_spec(s, kv):
        def index(b, src, base, peer):
            return (src[b * TOPK + s], kv, 0, 0)

        return pl.BlockSpec((None, None, BLOCK_TOKENS, head_width), index)

    out_row = pl.BlockSpec((BLOCK_TOKENS, row_width), lambda b, src, base, peer: (b, 0))
    pos_spec = pl.BlockSpec((None, 1, TOPK * BLOCK_TOKENS), lambda b, src, base, peer: (b, 0, 0))
    acc_spec = pl.BlockSpec((targets, BLOCK_TOKENS, head_width), lambda b, src, base, peer: (0, 0, 0))
    in_specs = (
        [slot_spec(s, 0) for s in range(TOPK)]
        + [slot_spec(s, 1) for s in range(TOPK)]
        + [half_spec(0, 0), half_spec(0, 1), half_spec(1, 0), half_spec(1, 1), pos_spec]
    )
    out_shape = (
        jax.ShapeDtypeStruct((run_len, row_width), jnp.bfloat16),
        jax.ShapeDtypeStruct((run_len, row_width), jnp.bfloat16),
        jax.ShapeDtypeStruct((targets, BLOCK_TOKENS, head_width), jnp.float32),
        jax.ShapeDtypeStruct((targets, BLOCK_TOKENS, head_width), jnp.float32),
    )
    grid_spec = pltpu.PrefetchScalarGridSpec(
        num_scalar_prefetch=3,
        grid=(block_ids,),
        in_specs=in_specs,
        out_specs=(out_row, out_row, acc_spec, acc_spec),
    )
    return pl.pallas_call(
        attention_kernel,
        grid_spec=grid_spec,
        out_shape=out_shape,
        compiler_params=pltpu.CompilerParams(
            dimension_semantics=("arbitrary",),
            vmem_limit_bytes=48 * 1024 * 1024,
        ),
    )(slot_src, query_base, peer_of, *([table] * (2 * TOPK)), *([pieces] * 4), key_pos)


def on_device(queries, rotated_keys, value_vectors, block_list, grad_out):
    kv_h = to_heads(rotated_keys, value_vectors)
    size = lax.axis_size("head")
    here = lax.axis_index("head")
    tok, head_count, head_width = queries.shape
    run_len = size * tok
    groups = kv_h.shape[2]
    group_width = head_count // size // groups
    qg = jnp.stack([queries, grad_out]).reshape(2, tok, size, head_count // size * head_width)
    qg = jnp.transpose(qg, (2, 0, 1, 3))
    pieces = []
    for k in range(size):
        piece = lax.dynamic_index_in_dim(qg, (here + k) % size, axis=0, keepdims=False)
        if k:
            piece = lax.ppermute(piece, "head", [(i, (i + k) % size) for i in range(size)])
        pieces.append(piece)
    qg_pieces = jnp.stack(pieces)
    peer_of = (here - jnp.arange(size, dtype=jnp.int32)) % size
    head_count = head_count // size
    block_ids = run_len // BLOCK_TOKENS
    peers = lax.axis_size("blk")
    rank = lax.axis_index("blk")
    head_rank = lax.axis_index("head")
    offsets = jnp.arange(BLOCK_TOKENS, dtype=jnp.int32)
    block_range = jnp.arange(block_ids, dtype=jnp.int32)
    peer_range = jnp.arange(peers, dtype=jnp.int32)

    lists_here = lax.dynamic_slice_in_dim(block_list, head_rank * groups, groups, 0)
    lists_mine = lax.dynamic_slice_in_dim(lists_here, rank * block_ids, block_ids, 1)
    by_run = lists_here.reshape(groups, peers, block_ids * TOPK)
    in_mine = (by_run // block_ids) == rank
    named = jnp.max(jnp.where(in_mine, by_run % block_ids, -1), axis=-1)
    present = (named >= 0) & (peer_range != rank)[None, :]
    pick_send = (named[:, :, None] == block_range).astype(jnp.bfloat16)
    take_back = pick_send * present[..., None].astype(jnp.bfloat16)

    kv_local = jnp.transpose(
        kv_h.reshape(2, block_ids, BLOCK_TOKENS, groups, head_width), (3, 1, 0, 2, 4)
    )
    owner = lists_mine // block_ids
    slot_src = jnp.where(owner == rank, peers + lists_mine % block_ids, owner)
    slot_ids = jnp.arange(TOPK, dtype=jnp.int32)
    earlier = slot_ids[None, :] < slot_ids[:, None]
    repeated = jnp.any((lists_mine[..., :, None] == lists_mine[..., None, :]) & earlier, axis=-1)
    key_pos = lists_mine[..., None] * BLOCK_TOKENS + offsets
    key_pos = jnp.where(repeated[..., None], jnp.int32(2**30), key_pos)
    key_pos = key_pos.reshape(groups, block_ids, 1, TOPK * BLOCK_TOKENS)
    query_base = (rank * block_ids + block_range) * BLOCK_TOKENS

    outs, backs, locals_ = [], [], []
    for g in range(groups):
        send = jnp.einsum(
            "rb,bktd->rktd", pick_send[g], kv_local[g], preferred_element_type=jnp.float32
        ).astype(jnp.bfloat16)
        recv = lax.all_to_all(send, "blk", split_axis=0, concat_axis=0, tiled=True)
        table = jnp.concatenate([recv, kv_local[g]], axis=0)
        o_g, dq_g, dk_acc, dv_acc = attend(
            slot_src[g].reshape(-1), query_base, peer_of, table, qg_pieces, key_pos[g], g, groups
        )
        size_ = lax.axis_size("head")
        pair = jnp.stack([o_g, dq_g]).reshape(2, size_, run_len // size_, o_g.shape[-1])
        outs.append(exchange(pair, 1, 1))
        acc = jnp.stack([dk_acc, dv_acc], axis=1)
        remote = acc[:peers].astype(jnp.bfloat16)
        local = acc[peers:].astype(jnp.bfloat16)
        backs.append(lax.all_to_all(remote, "blk", split_axis=0, concat_axis=0, tiled=True))
        locals_.append(local)

    def group_layout(parts):
        return jnp.stack(parts, axis=2).reshape(run_len, groups, head_width)

    key_grads, value_grads = [], []
    for g in range(groups):
        total = locals_[g].astype(jnp.float32) + jnp.einsum(
            "rl,rktd->lktd", take_back[g], backs[g], preferred_element_type=jnp.float32
        )
        total = total.astype(jnp.bfloat16)
        key_grads.append(total[:, 0])
        value_grads.append(total[:, 1])
    both = jnp.transpose(jnp.stack(outs), (1, 3, 2, 0, 4))
    both = both.reshape(2, run_len // size, size * head_count, head_width)
    attn_out, grad_queries = both[0], both[1]
    key_gradient, value_gradient = from_heads(group_layout(key_grads), group_layout(value_grads))
    return attn_out, grad_queries, key_gradient, value_gradient


def solution(mesh):
    in_specs = (
        P(("blk", "head"), None, None),
        P(("blk", "head"), None, None),
        P(("blk", "head"), None, None),
        P(),
        P(("blk", "head"), None, None),
    )
    out_specs = (
        P(("blk", "head"), None, None),
        P(("blk", "head"), None, None),
        P(("blk", "head"), None, None),
        P(("blk", "head"), None, None),
    )
    return jax.shard_map(
        on_device, mesh=mesh, in_specs=in_specs, out_specs=out_specs, check_vma=False
    )
```

```python
import jax
import jax.numpy as jnp
from jax import lax
from jax.sharding import PartitionSpec as P
from jax.experimental import pallas as pl
from jax.experimental.pallas import tpu as pltpu

BLOCK_TOKENS = 128
TOPK = 8


def exchange(x, part_axis, out_axis):
    size = lax.axis_size("head")
    here = lax.axis_index("head")
    pieces = []
    for k in range(size):
        piece = lax.dynamic_index_in_dim(x, (here + k) % size, axis=part_axis, keepdims=False)
        if k:
            piece = lax.ppermute(piece, "head", [(i, (i + k) % size) for i in range(size)])
        pieces.append(piece)
    ordered = jnp.stack([pieces[(-s) % size] for s in range(size)], axis=out_axis)
    return jnp.roll(ordered, here, axis=out_axis)


def to_heads(*xs):
    size = lax.axis_size("head")
    x = jnp.stack(xs)
    n, tok, heads, d = x.shape
    x = x.reshape(n, tok, size, heads // size, d)
    return exchange(x, 2, 1).reshape(n, size * tok, heads // size, d)


def from_heads(*xs):
    size = lax.axis_size("head")
    x = jnp.stack(xs)
    n, run, part, d = x.shape
    x = x.reshape(n, size, run // size, part, d)
    both = exchange(x, 1, 2).reshape(n, run // size, size * part, d)
    return tuple(both[i] for i in range(len(xs)))


def attention_kernel(src_ref, base_ref, peer_ref, *refs):
    table_ref, q_lo, q_hi, do_lo, do_hi, kpos_ref = refs[:6]
    o_ref, dq_ref, dk_ref, dv_ref = refs[6:]
    b = pl.program_id(0)

    @pl.when(b == 0)
    def _():
        dk_ref[...] = jnp.zeros_like(dk_ref)
        dv_ref[...] = jnp.zeros_like(dv_ref)

    head_width = table_ref.shape[-1]
    group_width = q_lo.shape[-1] // head_width
    scale = head_width ** (-0.5)
    slots = [src_ref[b * TOPK + s] for s in range(TOPK)]
    keys = jnp.concatenate([table_ref[t, 0] for t in slots], axis=0)
    values = jnp.concatenate([table_ref[t, 1] for t in slots], axis=0)
    query_pos = base_ref[b] + lax.broadcasted_iota(jnp.int32, (BLOCK_TOKENS, 1), 0)
    allowed = kpos_ref[...] <= query_pos
    nt = (((1,), (1,)), ((), ()))
    tn = (((0,), (0,)), ((), ()))
    dk = None
    dv = None
    for j in range(group_width):
        cols = slice(j * head_width, (j + 1) * head_width)
        qj = jnp.concatenate([q_lo[:, cols], q_hi[:, cols]], axis=0)
        gj = jnp.concatenate([do_lo[:, cols], do_hi[:, cols]], axis=0)
        s = lax.dot_general(qj, keys, nt, preferred_element_type=jnp.float32) * scale
        s = jnp.where(allowed, s, -jnp.inf)
        m = jnp.max(s, axis=-1, keepdims=True)
        lt = m + jnp.log(jnp.sum(jnp.exp(s - m), axis=-1, keepdims=True))
        p = jnp.exp(s - lt)
        pb = p.astype(jnp.bfloat16)
        o = jnp.dot(pb, values, preferred_element_type=jnp.float32).astype(jnp.bfloat16)
        o_ref[:, cols] = o
        rd = jnp.sum(gj.astype(jnp.float32) * o.astype(jnp.float32), axis=-1, keepdims=True)
        dp = lax.dot_general(gj, values, nt, preferred_element_type=jnp.float32)
        ds = (p * (dp - rd)).astype(jnp.bfloat16)
        dq = jnp.dot(ds, keys, preferred_element_type=jnp.float32) * scale
        dq_ref[:, cols] = dq.astype(jnp.bfloat16)
        dkj = lax.dot_general(ds, qj, tn, preferred_element_type=jnp.float32)
        dvj = lax.dot_general(pb, gj, tn, preferred_element_type=jnp.float32)
        dk = dkj if dk is None else dk + dkj
        dv = dvj if dv is None else dv + dvj
    dk = dk * scale
    for s in range(TOPK):
        t = src_ref[b * TOPK + s]
        rows = slice(s * BLOCK_TOKENS, (s + 1) * BLOCK_TOKENS)
        dk_ref[t] = dk_ref[t] + dk[rows]
        dv_ref[t] = dv_ref[t] + dv[rows]


def attend(slot_src, query_base, peer_of, table, pieces, key_pos, group, groups):
    piece_len = pieces.shape[2]
    run_len = pieces.shape[0] * piece_len
    block_ids = run_len // BLOCK_TOKENS
    targets = table.shape[0]
    head_width = table.shape[-1]
    row_width = pieces.shape[-1] // groups
    half = BLOCK_TOKENS // 2
    per_piece = piece_len // half

    def half_spec(which, part):
        def index(b, src, base, peer):
            i = 2 * b + part
            return (peer[i // per_piece], which, i % per_piece, group)

        return pl.BlockSpec((None, None, half, row_width), index)

    table_spec = pl.BlockSpec(table.shape, lambda b, src, base, peer: (0, 0, 0, 0))

    out_row = pl.BlockSpec((BLOCK_TOKENS, row_width), lambda b, src, base, peer: (b, 0))
    pos_spec = pl.BlockSpec((None, 1, TOPK * BLOCK_TOKENS), lambda b, src, base, peer: (b, 0, 0))
    acc_spec = pl.BlockSpec((targets, BLOCK_TOKENS, head_width), lambda b, src, base, peer: (0, 0, 0))
    in_specs = (
        [table_spec]
        + [half_spec(0, 0), half_spec(0, 1), half_spec(1, 0), half_spec(1, 1), pos_spec]
    )
    out_shape = (
        jax.ShapeDtypeStruct((run_len, row_width), jnp.bfloat16),
        jax.ShapeDtypeStruct((run_len, row_width), jnp.bfloat16),
        jax.ShapeDtypeStruct((targets, BLOCK_TOKENS, head_width), jnp.float32),
        jax.ShapeDtypeStruct((targets, BLOCK_TOKENS, head_width), jnp.float32),
    )
    grid_spec = pltpu.PrefetchScalarGridSpec(
        num_scalar_prefetch=3,
        grid=(block_ids,),
        in_specs=in_specs,
        out_specs=(out_row, out_row, acc_spec, acc_spec),
    )
    return pl.pallas_call(
        attention_kernel,
        grid_spec=grid_spec,
        out_shape=out_shape,
        compiler_params=pltpu.CompilerParams(
            dimension_semantics=("arbitrary",),
            vmem_limit_bytes=48 * 1024 * 1024,
        ),
    )(slot_src, query_base, peer_of, table, *([pieces] * 4), key_pos)


def on_device(queries, rotated_keys, value_vectors, block_list, grad_out):
    kv_h = to_heads(rotated_keys, value_vectors)
    size = lax.axis_size("head")
    here = lax.axis_index("head")
    tok, head_count, head_width = queries.shape
    run_len = size * tok
    groups = kv_h.shape[2]
    group_width = head_count // size // groups
    qg = jnp.stack([queries, grad_out]).reshape(2, tok, size, head_count // size * head_width)
    qg = jnp.transpose(qg, (2, 0, 1, 3))
    pieces = []
    for k in range(size):
        piece = lax.dynamic_index_in_dim(qg, (here + k) % size, axis=0, keepdims=False)
        if k:
            piece = lax.ppermute(piece, "head", [(i, (i + k) % size) for i in range(size)])
        pieces.append(piece)
    qg_pieces = jnp.stack(pieces)
    peer_of = (here - jnp.arange(size, dtype=jnp.int32)) % size
    head_count = head_count // size
    block_ids = run_len // BLOCK_TOKENS
    peers = lax.axis_size("blk")
    rank = lax.axis_index("blk")
    head_rank = lax.axis_index("head")
    offsets = jnp.arange(BLOCK_TOKENS, dtype=jnp.int32)
    block_range = jnp.arange(block_ids, dtype=jnp.int32)
    peer_range = jnp.arange(peers, dtype=jnp.int32)

    lists_here = lax.dynamic_slice_in_dim(block_list, head_rank * groups, groups, 0)
    lists_mine = lax.dynamic_slice_in_dim(lists_here, rank * block_ids, block_ids, 1)
    by_run = lists_here.reshape(groups, peers, block_ids * TOPK)
    in_mine = (by_run // block_ids) == rank
    named = jnp.max(jnp.where(in_mine, by_run % block_ids, -1), axis=-1)
    present = (named >= 0) & (peer_range != rank)[None, :]
    pick_send = (named[:, :, None] == block_range).astype(jnp.bfloat16)
    take_back = pick_send * present[..., None].astype(jnp.bfloat16)

    kv_local = jnp.transpose(
        kv_h.reshape(2, block_ids, BLOCK_TOKENS, groups, head_width), (3, 1, 0, 2, 4)
    )
    owner = lists_mine // block_ids
    slot_src = jnp.where(owner == rank, peers + lists_mine % block_ids, owner)
    slot_ids = jnp.arange(TOPK, dtype=jnp.int32)
    earlier = slot_ids[None, :] < slot_ids[:, None]
    repeated = jnp.any((lists_mine[..., :, None] == lists_mine[..., None, :]) & earlier, axis=-1)
    key_pos = lists_mine[..., None] * BLOCK_TOKENS + offsets
    key_pos = jnp.where(repeated[..., None], jnp.int32(2**30), key_pos)
    key_pos = key_pos.reshape(groups, block_ids, 1, TOPK * BLOCK_TOKENS)
    query_base = (rank * block_ids + block_range) * BLOCK_TOKENS

    outs, query_grads, backs, locals_ = [], [], [], []
    for g in range(groups):
        send = jnp.einsum(
            "rb,bktd->rktd", pick_send[g], kv_local[g], preferred_element_type=jnp.float32
        ).astype(jnp.bfloat16)
        recv = lax.all_to_all(send, "blk", split_axis=0, concat_axis=0, tiled=True)
        table = jnp.concatenate([recv, kv_local[g]], axis=0)
        o_g, dq_g, dk_acc, dv_acc = attend(
            slot_src[g].reshape(-1), query_base, peer_of, table, qg_pieces, key_pos[g], g, groups
        )
        outs.append(o_g)
        query_grads.append(dq_g)
        acc = jnp.stack([dk_acc, dv_acc], axis=1)
        remote = acc[:peers].astype(jnp.bfloat16)
        local = acc[peers:].astype(jnp.bfloat16)
        backs.append(lax.all_to_all(remote, "blk", split_axis=0, concat_axis=0, tiled=True))
        locals_.append(local)

    def heads_layout(parts):
        return jnp.concatenate(parts, axis=1).reshape(run_len, head_count, head_width)

    def group_layout(parts):
        return jnp.stack(parts, axis=2).reshape(run_len, groups, head_width)

    attn_all, query_grad_all, backs[-1] = lax.optimization_barrier(
        (heads_layout(outs), heads_layout(query_grads), backs[-1])
    )
    key_grads, value_grads = [], []
    for g in range(groups):
        total = locals_[g].astype(jnp.float32) + jnp.einsum(
            "rl,rktd->lktd", take_back[g], backs[g], preferred_element_type=jnp.float32
        )
        total = total.astype(jnp.bfloat16)
        key_grads.append(total[:, 0])
        value_grads.append(total[:, 1])
    attn_out, grad_queries = from_heads(attn_all, query_grad_all)
    key_gradient, value_gradient = from_heads(group_layout(key_grads), group_layout(value_grads))
    return attn_out, grad_queries, key_gradient, value_gradient


def solution(mesh):
    in_specs = (
        P(("blk", "head"), None, None),
        P(("blk", "head"), None, None),
        P(("blk", "head"), None, None),
        P(),
        P(("blk", "head"), None, None),
    )
    out_specs = (
        P(("blk", "head"), None, None),
        P(("blk", "head"), None, None),
        P(("blk", "head"), None, None),
        P(("blk", "head"), None, None),
    )
    return jax.shard_map(
        on_device, mesh=mesh, in_specs=in_specs, out_specs=out_specs, check_vma=False
    )
```

```python
import jax
import jax.numpy as jnp
from jax import lax
from jax.sharding import PartitionSpec as P
from jax.experimental import pallas as pl
from jax.experimental.pallas import tpu as pltpu

BLOCK_TOKENS = 128
TOPK = 8


def exchange(x, part_axis, out_axis):
    size = lax.axis_size("head")
    here = lax.axis_index("head")
    pieces = []
    for k in range(size):
        piece = lax.dynamic_index_in_dim(x, (here + k) % size, axis=part_axis, keepdims=False)
        if k:
            piece = lax.ppermute(piece, "head", [(i, (i + k) % size) for i in range(size)])
        pieces.append(piece)
    ordered = jnp.stack([pieces[(-s) % size] for s in range(size)], axis=out_axis)
    return jnp.roll(ordered, here, axis=out_axis)


def to_heads(*xs):
    size = lax.axis_size("head")
    x = jnp.stack(xs)
    n, tok, heads, d = x.shape
    x = x.reshape(n, tok, size, heads // size, d)
    return exchange(x, 2, 1).reshape(n, size * tok, heads // size, d)


def from_heads(*xs):
    size = lax.axis_size("head")
    x = jnp.stack(xs)
    n, run, part, d = x.shape
    x = x.reshape(n, size, run // size, part, d)
    both = exchange(x, 1, 2).reshape(n, run // size, size * part, d)
    return tuple(both[i] for i in range(len(xs)))


def attention_kernel(src_ref, base_ref, peer_ref, *refs):
    table_ref, q_lo, q_hi, do_lo, do_hi, kpos_ref = refs[:6]
    o_ref, dq_ref, dk_ref, dv_ref = refs[6:]
    b = pl.program_id(0)

    @pl.when(b == 0)
    def _():
        dk_ref[...] = jnp.zeros_like(dk_ref)
        dv_ref[...] = jnp.zeros_like(dv_ref)

    head_width = table_ref.shape[-1]
    group_width = q_lo.shape[-1] // head_width
    scale = head_width ** (-0.5)
    slots = [src_ref[b * TOPK + s] for s in range(TOPK)]
    keys = jnp.concatenate([table_ref[t, 0] for t in slots], axis=0)
    values = jnp.concatenate([table_ref[t, 1] for t in slots], axis=0)
    query_pos = base_ref[b] + lax.broadcasted_iota(jnp.int32, (BLOCK_TOKENS, 1), 0)
    allowed = kpos_ref[...] <= query_pos
    nt = (((1,), (1,)), ((), ()))
    dk = None
    dv = None
    for j in range(group_width):
        cols = slice(j * head_width, (j + 1) * head_width)
        qj = jnp.concatenate([q_lo[:, cols], q_hi[:, cols]], axis=0)
        gj = jnp.concatenate([do_lo[:, cols], do_hi[:, cols]], axis=0)
        s = lax.dot_general(qj, keys, nt, preferred_element_type=jnp.float32) * scale
        s = jnp.where(allowed, s, -jnp.inf)
        m = jnp.max(s, axis=-1, keepdims=True)
        lt = m + jnp.log(jnp.sum(jnp.exp(s - m), axis=-1, keepdims=True))
        p = jnp.exp(s - lt)
        pb = p.astype(jnp.bfloat16)
        o = jnp.dot(pb, values, preferred_element_type=jnp.float32).astype(jnp.bfloat16)
        o_ref[:, cols] = o
        rd = jnp.sum(gj.astype(jnp.float32) * o.astype(jnp.float32), axis=-1, keepdims=True)
        dp = lax.dot_general(gj, values, nt, preferred_element_type=jnp.float32)
        ds = (p * (dp - rd)).astype(jnp.bfloat16)
        dq = jnp.dot(ds, keys, preferred_element_type=jnp.float32) * scale
        dq_ref[:, cols] = dq.astype(jnp.bfloat16)
        dkj = jnp.dot(qj.T, ds, preferred_element_type=jnp.float32)
        dvj = jnp.dot(gj.T, pb, preferred_element_type=jnp.float32)
        dk = dkj if dk is None else dk + dkj
        dv = dvj if dv is None else dv + dvj
    dk = dk * scale
    for s in range(TOPK):
        t = src_ref[b * TOPK + s]
        cols = slice(s * BLOCK_TOKENS, (s + 1) * BLOCK_TOKENS)
        dk_ref[t] = dk_ref[t] + dk[:, cols]
        dv_ref[t] = dv_ref[t] + dv[:, cols]


def attend(slot_src, query_base, peer_of, table, pieces, key_pos, group, groups):
    piece_len = pieces.shape[2]
    run_len = pieces.shape[0] * piece_len
    block_ids = run_len // BLOCK_TOKENS
    targets = table.shape[0]
    head_width = table.shape[-1]
    row_width = pieces.shape[-1] // groups
    half = BLOCK_TOKENS // 2
    per_piece = piece_len // half

    def half_spec(which, part):
        def index(b, src, base, peer):
            i = 2 * b + part
            return (peer[i // per_piece], which, i % per_piece, group)

        return pl.BlockSpec((None, None, half, row_width), index)

    table_spec = pl.BlockSpec(table.shape, lambda b, src, base, peer: (0, 0, 0, 0))

    out_row = pl.BlockSpec((BLOCK_TOKENS, row_width), lambda b, src, base, peer: (b, 0))
    pos_spec = pl.BlockSpec((None, 1, TOPK * BLOCK_TOKENS), lambda b, src, base, peer: (b, 0, 0))
    acc_spec = pl.BlockSpec((targets, BLOCK_TOKENS, head_width), lambda b, src, base, peer: (0, 0, 0))
    in_specs = (
        [table_spec]
        + [half_spec(0, 0), half_spec(0, 1), half_spec(1, 0), half_spec(1, 1), pos_spec]
    )
    out_shape = (
        jax.ShapeDtypeStruct((run_len, row_width), jnp.bfloat16),
        jax.ShapeDtypeStruct((run_len, row_width), jnp.bfloat16),
        jax.ShapeDtypeStruct((targets, BLOCK_TOKENS, head_width), jnp.float32),
        jax.ShapeDtypeStruct((targets, BLOCK_TOKENS, head_width), jnp.float32),
    )
    grid_spec = pltpu.PrefetchScalarGridSpec(
        num_scalar_prefetch=3,
        grid=(block_ids,),
        in_specs=in_specs,
        out_specs=(out_row, out_row, acc_spec, acc_spec),
    )
    return pl.pallas_call(
        attention_kernel,
        grid_spec=grid_spec,
        out_shape=out_shape,
        compiler_params=pltpu.CompilerParams(
            dimension_semantics=("arbitrary",),
            vmem_limit_bytes=48 * 1024 * 1024,
        ),
    )(slot_src, query_base, peer_of, table, *([pieces] * 4), key_pos)


def on_device(queries, rotated_keys, value_vectors, block_list, grad_out):
    kv_h = to_heads(rotated_keys, value_vectors)
    size = lax.axis_size("head")
    here = lax.axis_index("head")
    tok, head_count, head_width = queries.shape
    run_len = size * tok
    groups = kv_h.shape[2]
    group_width = head_count // size // groups
    qg = jnp.stack([queries, grad_out]).reshape(2, tok, size, head_count // size * head_width)
    qg = jnp.transpose(qg, (2, 0, 1, 3))
    pieces = []
    for k in range(size):
        piece = lax.dynamic_index_in_dim(qg, (here + k) % size, axis=0, keepdims=False)
        if k:
            piece = lax.ppermute(piece, "head", [(i, (i + k) % size) for i in range(size)])
        pieces.append(piece)
    qg_pieces = jnp.stack(pieces)
    peer_of = (here - jnp.arange(size, dtype=jnp.int32)) % size
    head_count = head_count // size
    block_ids = run_len // BLOCK_TOKENS
    peers = lax.axis_size("blk")
    rank = lax.axis_index("blk")
    head_rank = lax.axis_index("head")
    offsets = jnp.arange(BLOCK_TOKENS, dtype=jnp.int32)
    block_range = jnp.arange(block_ids, dtype=jnp.int32)
    peer_range = jnp.arange(peers, dtype=jnp.int32)

    lists_here = lax.dynamic_slice_in_dim(block_list, head_rank * groups, groups, 0)
    lists_mine = lax.dynamic_slice_in_dim(lists_here, rank * block_ids, block_ids, 1)
    by_run = lists_here.reshape(groups, peers, block_ids * TOPK)
    in_mine = (by_run // block_ids) == rank
    named = jnp.max(jnp.where(in_mine, by_run % block_ids, -1), axis=-1)
    present = (named >= 0) & (peer_range != rank)[None, :]
    pick_send = (named[:, :, None] == block_range).astype(jnp.bfloat16)
    take_back = pick_send * present[..., None].astype(jnp.bfloat16)

    kv_local = jnp.transpose(
        kv_h.reshape(2, block_ids, BLOCK_TOKENS, groups, head_width), (3, 1, 0, 2, 4)
    )
    owner = lists_mine // block_ids
    slot_src = jnp.where(owner == rank, peers + lists_mine % block_ids, owner)
    slot_ids = jnp.arange(TOPK, dtype=jnp.int32)
    earlier = slot_ids[None, :] < slot_ids[:, None]
    repeated = jnp.any((lists_mine[..., :, None] == lists_mine[..., None, :]) & earlier, axis=-1)
    key_pos = lists_mine[..., None] * BLOCK_TOKENS + offsets
    key_pos = jnp.where(repeated[..., None], jnp.int32(2**30), key_pos)
    key_pos = key_pos.reshape(groups, block_ids, 1, TOPK * BLOCK_TOKENS)
    query_base = (rank * block_ids + block_range) * BLOCK_TOKENS

    outs, query_grads, backs, locals_ = [], [], [], []
    for g in range(groups):
        send = jnp.einsum(
            "rb,bktd->rktd", pick_send[g], kv_local[g], preferred_element_type=jnp.float32
        ).astype(jnp.bfloat16)
        recv = lax.all_to_all(send, "blk", split_axis=0, concat_axis=0, tiled=True)
        table = jnp.concatenate([recv, kv_local[g]], axis=0)
        o_g, dq_g, dk_acc, dv_acc = attend(
            slot_src[g].reshape(-1), query_base, peer_of, table, qg_pieces, key_pos[g], g, groups
        )
        outs.append(o_g)
        query_grads.append(dq_g)
        acc = jnp.swapaxes(jnp.stack([dk_acc, dv_acc], axis=1), 2, 3)
        remote = acc[:peers].astype(jnp.bfloat16)
        local = acc[peers:].astype(jnp.bfloat16)
        backs.append(lax.all_to_all(remote, "blk", split_axis=0, concat_axis=0, tiled=True))
        locals_.append(local)

    def heads_layout(parts):
        return jnp.concatenate(parts, axis=1).reshape(run_len, head_count, head_width)

    def group_layout(parts):
        return jnp.stack(parts, axis=2).reshape(run_len, groups, head_width)

    attn_all, query_grad_all, backs[-1] = lax.optimization_barrier(
        (heads_layout(outs), heads_layout(query_grads), backs[-1])
    )
    key_grads, value_grads = [], []
    for g in range(groups):
        total = locals_[g].astype(jnp.float32) + jnp.einsum(
            "rl,rktd->lktd", take_back[g], backs[g], preferred_element_type=jnp.float32
        )
        total = total.astype(jnp.bfloat16)
        key_grads.append(total[:, 0])
        value_grads.append(total[:, 1])
    attn_out, grad_queries = from_heads(attn_all, query_grad_all)
    key_gradient, value_gradient = from_heads(group_layout(key_grads), group_layout(value_grads))
    return attn_out, grad_queries, key_gradient, value_gradient


def solution(mesh):
    in_specs = (
        P(("blk", "head"), None, None),
        P(("blk", "head"), None, None),
        P(("blk", "head"), None, None),
        P(),
        P(("blk", "head"), None, None),
    )
    out_specs = (
        P(("blk", "head"), None, None),
        P(("blk", "head"), None, None),
        P(("blk", "head"), None, None),
        P(("blk", "head"), None, None),
    )
    return jax.shard_map(
        on_device, mesh=mesh, in_specs=in_specs, out_specs=out_specs, check_vma=False
    )
```

```python
import jax
import jax.numpy as jnp
from jax import lax
from jax.sharding import PartitionSpec as P
from jax.experimental import pallas as pl
from jax.experimental.pallas import tpu as pltpu

BLOCK_TOKENS = 128
TOPK = 8


def exchange(x, part_axis, out_axis):
    size = lax.axis_size("head")
    here = lax.axis_index("head")
    pieces = []
    for k in range(size):
        piece = lax.dynamic_index_in_dim(x, (here + k) % size, axis=part_axis, keepdims=False)
        if k:
            piece = lax.ppermute(piece, "head", [(i, (i + k) % size) for i in range(size)])
        pieces.append(piece)
    ordered = jnp.stack([pieces[(-s) % size] for s in range(size)], axis=out_axis)
    return jnp.roll(ordered, here, axis=out_axis)


def to_heads(*xs):
    size = lax.axis_size("head")
    x = jnp.stack(xs)
    n, tok, heads, d = x.shape
    x = x.reshape(n, tok, size, heads // size, d)
    return exchange(x, 2, 1).reshape(n, size * tok, heads // size, d)


def from_heads(*xs):
    size = lax.axis_size("head")
    x = jnp.stack(xs)
    n, run, part, d = x.shape
    x = x.reshape(n, size, run // size, part, d)
    both = exchange(x, 1, 2).reshape(n, run // size, size * part, d)
    return tuple(both[i] for i in range(len(xs)))


def attention_kernel(src_ref, base_ref, peer_ref, *refs):
    table_ref, q_lo, q_hi, do_lo, do_hi, kpos_ref = refs[:6]
    o_ref, dq_ref, dk_ref, dv_ref = refs[6:]
    b = pl.program_id(0)

    @pl.when(b == 0)
    def _():
        dk_ref[...] = jnp.zeros_like(dk_ref)
        dv_ref[...] = jnp.zeros_like(dv_ref)

    head_width = table_ref.shape[-1]
    group_width = q_lo.shape[-1] // head_width
    scale = head_width ** (-0.5)
    slots = [src_ref[b * TOPK + s] for s in range(TOPK)]
    keys = jnp.concatenate([table_ref[t, 0] for t in slots], axis=0)
    values = jnp.concatenate([table_ref[t, 1] for t in slots], axis=0)
    query_pos = base_ref[b] + lax.broadcasted_iota(jnp.int32, (BLOCK_TOKENS, 1), 0)
    allowed = kpos_ref[...] <= query_pos
    nt = (((1,), (1,)), ((), ()))
    tn = (((0,), (0,)), ((), ()))
    dk = None
    dv = None
    for j in range(group_width):
        cols = slice(j * head_width, (j + 1) * head_width)
        qj = jnp.concatenate([q_lo[:, cols], q_hi[:, cols]], axis=0)
        gj = jnp.concatenate([do_lo[:, cols], do_hi[:, cols]], axis=0)
        s = lax.dot_general(qj, keys, nt, preferred_element_type=jnp.float32) * scale
        s = jnp.where(allowed, s, -jnp.inf)
        m = jnp.max(s, axis=-1, keepdims=True)
        lt = m + jnp.log(jnp.sum(jnp.exp(s - m), axis=-1, keepdims=True))
        p = jnp.exp(s - lt)
        pb = p.astype(jnp.bfloat16)
        o = jnp.dot(pb, values, preferred_element_type=jnp.float32).astype(jnp.bfloat16)
        o_ref[:, cols] = o
        rd = jnp.sum(gj.astype(jnp.float32) * o.astype(jnp.float32), axis=-1, keepdims=True)
        dp = lax.dot_general(gj, values, nt, preferred_element_type=jnp.float32)
        ds = (p * (dp - rd)).astype(jnp.bfloat16)
        dq = jnp.dot(ds, keys, preferred_element_type=jnp.float32) * scale
        dq_ref[:, cols] = dq.astype(jnp.bfloat16)
        dkj = lax.dot_general(ds, qj, tn, preferred_element_type=jnp.float32)
        dvj = lax.dot_general(pb, gj, tn, preferred_element_type=jnp.float32)
        dk = dkj if dk is None else dk + dkj
        dv = dvj if dv is None else dv + dvj
    dk = dk * scale
    for s in range(TOPK):
        t = src_ref[b * TOPK + s]
        rows = slice(s * BLOCK_TOKENS, (s + 1) * BLOCK_TOKENS)
        dk_ref[t] = dk_ref[t] + dk[rows]
        dv_ref[t] = dv_ref[t] + dv[rows]


def attend(slot_src, query_base, peer_of, table, pieces, key_pos, group, groups):
    piece_len = pieces.shape[2]
    run_len = pieces.shape[0] * piece_len
    block_ids = run_len // BLOCK_TOKENS
    targets = table.shape[0]
    head_width = table.shape[-1]
    row_width = pieces.shape[-1] // groups
    half = BLOCK_TOKENS // 2
    per_piece = piece_len // half

    def half_spec(which, part):
        def index(b, src, base, peer):
            i = 2 * b + part
            return (peer[i // per_piece], which, i % per_piece, group)

        return pl.BlockSpec((None, None, half, row_width), index)

    table_spec = pl.BlockSpec(table.shape, lambda b, src, base, peer: (0, 0, 0, 0))

    out_row = pl.BlockSpec((BLOCK_TOKENS, row_width), lambda b, src, base, peer: (b, 0))
    pos_spec = pl.BlockSpec((None, 1, TOPK * BLOCK_TOKENS), lambda b, src, base, peer: (b, 0, 0))
    acc_spec = pl.BlockSpec((targets, BLOCK_TOKENS, head_width), lambda b, src, base, peer: (0, 0, 0))
    in_specs = (
        [table_spec]
        + [half_spec(0, 0), half_spec(0, 1), half_spec(1, 0), half_spec(1, 1), pos_spec]
    )
    out_shape = (
        jax.ShapeDtypeStruct((run_len, row_width), jnp.bfloat16),
        jax.ShapeDtypeStruct((run_len, row_width), jnp.bfloat16),
        jax.ShapeDtypeStruct((targets, BLOCK_TOKENS, head_width), jnp.float32),
        jax.ShapeDtypeStruct((targets, BLOCK_TOKENS, head_width), jnp.float32),
    )
    grid_spec = pltpu.PrefetchScalarGridSpec(
        num_scalar_prefetch=3,
        grid=(block_ids,),
        in_specs=in_specs,
        out_specs=(out_row, out_row, acc_spec, acc_spec),
    )
    return pl.pallas_call(
        attention_kernel,
        grid_spec=grid_spec,
        out_shape=out_shape,
        compiler_params=pltpu.CompilerParams(
            dimension_semantics=("arbitrary",),
            vmem_limit_bytes=48 * 1024 * 1024,
        ),
    )(slot_src, query_base, peer_of, table, *([pieces] * 4), key_pos)


def on_device(queries, rotated_keys, value_vectors, block_list, grad_out):
    kv_h = to_heads(rotated_keys, value_vectors)
    size = lax.axis_size("head")
    here = lax.axis_index("head")
    tok, head_count, head_width = queries.shape
    run_len = size * tok
    groups = kv_h.shape[2]
    group_width = head_count // size // groups
    qg = jnp.stack([queries, grad_out]).reshape(2, tok, size, head_count // size * head_width)
    qg = jnp.transpose(qg, (2, 0, 1, 3))
    pieces = []
    for k in range(size):
        piece = lax.dynamic_index_in_dim(qg, (here + k) % size, axis=0, keepdims=False)
        if k:
            piece = lax.ppermute(piece, "head", [(i, (i + k) % size) for i in range(size)])
        pieces.append(piece)
    qg_pieces = jnp.stack(pieces)
    peer_of = (here - jnp.arange(size, dtype=jnp.int32)) % size
    head_count = head_count // size
    block_ids = run_len // BLOCK_TOKENS
    peers = lax.axis_size("blk")
    rank = lax.axis_index("blk")
    head_rank = lax.axis_index("head")
    offsets = jnp.arange(BLOCK_TOKENS, dtype=jnp.int32)
    block_range = jnp.arange(block_ids, dtype=jnp.int32)
    peer_range = jnp.arange(peers, dtype=jnp.int32)

    lists_here = lax.dynamic_slice_in_dim(block_list, head_rank * groups, groups, 0)
    lists_mine = lax.dynamic_slice_in_dim(lists_here, rank * block_ids, block_ids, 1)
    by_run = lists_here.reshape(groups, peers, block_ids * TOPK)
    in_mine = (by_run // block_ids) == rank
    named = jnp.max(jnp.where(in_mine, by_run % block_ids, -1), axis=-1)
    present = (named >= 0) & (peer_range != rank)[None, :]
    pick_send = (named[:, :, None] == block_range).astype(jnp.bfloat16)
    take_back = pick_send * present[..., None].astype(jnp.bfloat16)

    kv_local = jnp.transpose(
        kv_h.reshape(2, block_ids, BLOCK_TOKENS, groups, head_width), (3, 1, 0, 2, 4)
    )
    owner = lists_mine // block_ids
    slot_src = jnp.where(owner == rank, peers + lists_mine % block_ids, owner)
    slot_ids = jnp.arange(TOPK, dtype=jnp.int32)
    earlier = slot_ids[None, :] < slot_ids[:, None]
    repeated = jnp.any((lists_mine[..., :, None] == lists_mine[..., None, :]) & earlier, axis=-1)
    key_pos = lists_mine[..., None] * BLOCK_TOKENS + offsets
    key_pos = jnp.where(repeated[..., None], jnp.int32(2**30), key_pos)
    key_pos = key_pos.reshape(groups, block_ids, 1, TOPK * BLOCK_TOKENS)
    query_base = (rank * block_ids + block_range) * BLOCK_TOKENS

    outs, query_grads, backs, locals_ = [], [], [], []

    def heads_layout(parts):
        return jnp.concatenate(parts, axis=1).reshape(run_len, head_count, head_width)

    for g in range(groups):
        send = jnp.einsum(
            "rb,bktd->rktd", pick_send[g], kv_local[g], preferred_element_type=jnp.float32
        ).astype(jnp.bfloat16)
        recv = lax.all_to_all(send, "blk", split_axis=0, concat_axis=0, tiled=True)
        table = jnp.concatenate([recv, kv_local[g]], axis=0)
        o_g, dq_g, dk_acc, dv_acc = attend(
            slot_src[g].reshape(-1), query_base, peer_of, table, qg_pieces, key_pos[g], g, groups
        )
        outs.append(o_g)
        query_grads.append(dq_g)
        acc = jnp.stack([dk_acc, dv_acc], axis=1)
        remote = acc[:peers].astype(jnp.bfloat16)
        local = acc[peers:].astype(jnp.bfloat16)
        if g == groups - 1:
            attn_all, query_grad_all, remote, backs[0] = lax.optimization_barrier(
                (heads_layout(outs), heads_layout(query_grads), remote, backs[0])
            )
        backs.append(lax.all_to_all(remote, "blk", split_axis=0, concat_axis=0, tiled=True))
        locals_.append(local)

    def group_layout(parts):
        return jnp.stack(parts, axis=2).reshape(run_len, groups, head_width)

    key_grads, value_grads = [], []
    for g in range(groups):
        total = locals_[g].astype(jnp.float32) + jnp.einsum(
            "rl,rktd->lktd", take_back[g], backs[g], preferred_element_type=jnp.float32
        )
        total = total.astype(jnp.bfloat16)
        key_grads.append(total[:, 0])
        value_grads.append(total[:, 1])
    attn_out, grad_queries = from_heads(attn_all, query_grad_all)
    key_gradient, value_gradient = from_heads(group_layout(key_grads), group_layout(value_grads))
    return attn_out, grad_queries, key_gradient, value_gradient


def solution(mesh):
    in_specs = (
        P(("blk", "head"), None, None),
        P(("blk", "head"), None, None),
        P(("blk", "head"), None, None),
        P(),
        P(("blk", "head"), None, None),
    )
    out_specs = (
        P(("blk", "head"), None, None),
        P(("blk", "head"), None, None),
        P(("blk", "head"), None, None),
        P(("blk", "head"), None, None),
    )
    return jax.shard_map(
        on_device, mesh=mesh, in_specs=in_specs, out_specs=out_specs, check_vma=False
    )
```

```python
import jax
import jax.numpy as jnp
from jax import lax
from jax.sharding import PartitionSpec as P
from jax.experimental import pallas as pl
from jax.experimental.pallas import tpu as pltpu

BLOCK_TOKENS = 128
TOPK = 8


def exchange(x, part_axis, out_axis):
    size = lax.axis_size("head")
    here = lax.axis_index("head")
    pieces = []
    for k in range(size):
        piece = lax.dynamic_index_in_dim(x, (here + k) % size, axis=part_axis, keepdims=False)
        if k:
            piece = lax.ppermute(piece, "head", [(i, (i + k) % size) for i in range(size)])
        pieces.append(piece)
    ordered = jnp.stack([pieces[(-s) % size] for s in range(size)], axis=out_axis)
    return jnp.roll(ordered, here, axis=out_axis)


def to_heads(*xs):
    size = lax.axis_size("head")
    x = jnp.stack(xs)
    n, tok, heads, d = x.shape
    return lax.all_to_all(x, "head", split_axis=2, concat_axis=1, tiled=True)


def from_heads(*xs):
    size = lax.axis_size("head")
    x = jnp.stack(xs)
    n, run, part, d = x.shape
    x = x.reshape(n, size, run // size, part, d)
    both = exchange(x, 1, 2).reshape(n, run // size, size * part, d)
    return tuple(both[i] for i in range(len(xs)))


def attention_kernel(src_ref, base_ref, peer_ref, *refs):
    table_ref, q_lo, q_hi, do_lo, do_hi, kpos_ref = refs[:6]
    o_ref, dq_ref, dk_ref, dv_ref = refs[6:]
    b = pl.program_id(0)

    @pl.when(b == 0)
    def _():
        dk_ref[...] = jnp.zeros_like(dk_ref)
        dv_ref[...] = jnp.zeros_like(dv_ref)

    head_width = table_ref.shape[-1]
    group_width = q_lo.shape[-1] // head_width
    scale = head_width ** (-0.5)
    slots = [src_ref[b * TOPK + s] for s in range(TOPK)]
    keys = jnp.concatenate([table_ref[t, 0] for t in slots], axis=0)
    values = jnp.concatenate([table_ref[t, 1] for t in slots], axis=0)
    query_pos = base_ref[b] + lax.broadcasted_iota(jnp.int32, (BLOCK_TOKENS, 1), 0)
    allowed = kpos_ref[...] <= query_pos
    nt = (((1,), (1,)), ((), ()))
    tn = (((0,), (0,)), ((), ()))
    dk = None
    dv = None
    for j in range(group_width):
        cols = slice(j * head_width, (j + 1) * head_width)
        qj = jnp.concatenate([q_lo[:, cols], q_hi[:, cols]], axis=0)
        gj = jnp.concatenate([do_lo[:, cols], do_hi[:, cols]], axis=0)
        s = lax.dot_general(qj, keys, nt, preferred_element_type=jnp.float32) * scale
        s = jnp.where(allowed, s, -jnp.inf)
        m = jnp.max(s, axis=-1, keepdims=True)
        lt = m + jnp.log(jnp.sum(jnp.exp(s - m), axis=-1, keepdims=True))
        p = jnp.exp(s - lt)
        pb = p.astype(jnp.bfloat16)
        o = jnp.dot(pb, values, preferred_element_type=jnp.float32).astype(jnp.bfloat16)
        o_ref[:, cols] = o
        rd = jnp.sum(gj.astype(jnp.float32) * o.astype(jnp.float32), axis=-1, keepdims=True)
        dp = lax.dot_general(gj, values, nt, preferred_element_type=jnp.float32)
        ds = (p * (dp - rd)).astype(jnp.bfloat16)
        dq = jnp.dot(ds, keys, preferred_element_type=jnp.float32) * scale
        dq_ref[:, cols] = dq.astype(jnp.bfloat16)
        dkj = lax.dot_general(ds, qj, tn, preferred_element_type=jnp.float32)
        dvj = lax.dot_general(pb, gj, tn, preferred_element_type=jnp.float32)
        dk = dkj if dk is None else dk + dkj
        dv = dvj if dv is None else dv + dvj
    dk = dk * scale
    for s in range(TOPK):
        t = src_ref[b * TOPK + s]
        rows = slice(s * BLOCK_TOKENS, (s + 1) * BLOCK_TOKENS)
        dk_ref[t] = dk_ref[t] + dk[rows]
        dv_ref[t] = dv_ref[t] + dv[rows]


def attend(slot_src, query_base, peer_of, table, pieces, key_pos, group, groups):
    piece_len = pieces.shape[2]
    run_len = pieces.shape[0] * piece_len
    block_ids = run_len // BLOCK_TOKENS
    targets = table.shape[0]
    head_width = table.shape[-1]
    row_width = pieces.shape[-1] // groups
    half = BLOCK_TOKENS // 2
    per_piece = piece_len // half

    def half_spec(which, part):
        def index(b, src, base, peer):
            i = 2 * b + part
            return (peer[i // per_piece], which, i % per_piece, group)

        return pl.BlockSpec((None, None, half, row_width), index)

    table_spec = pl.BlockSpec(table.shape, lambda b, src, base, peer: (0, 0, 0, 0))

    out_row = pl.BlockSpec((BLOCK_TOKENS, row_width), lambda b, src, base, peer: (b, 0))
    pos_spec = pl.BlockSpec((None, 1, TOPK * BLOCK_TOKENS), lambda b, src, base, peer: (b, 0, 0))
    acc_spec = pl.BlockSpec((targets, BLOCK_TOKENS, head_width), lambda b, src, base, peer: (0, 0, 0))
    in_specs = (
        [table_spec]
        + [half_spec(0, 0), half_spec(0, 1), half_spec(1, 0), half_spec(1, 1), pos_spec]
    )
    out_shape = (
        jax.ShapeDtypeStruct((run_len, row_width), jnp.bfloat16),
        jax.ShapeDtypeStruct((run_len, row_width), jnp.bfloat16),
        jax.ShapeDtypeStruct((targets, BLOCK_TOKENS, head_width), jnp.float32),
        jax.ShapeDtypeStruct((targets, BLOCK_TOKENS, head_width), jnp.float32),
    )
    grid_spec = pltpu.PrefetchScalarGridSpec(
        num_scalar_prefetch=3,
        grid=(block_ids,),
        in_specs=in_specs,
        out_specs=(out_row, out_row, acc_spec, acc_spec),
    )
    return pl.pallas_call(
        attention_kernel,
        grid_spec=grid_spec,
        out_shape=out_shape,
        compiler_params=pltpu.CompilerParams(
            dimension_semantics=("arbitrary",),
            vmem_limit_bytes=48 * 1024 * 1024,
        ),
    )(slot_src, query_base, peer_of, table, *([pieces] * 4), key_pos)


def on_device(queries, rotated_keys, value_vectors, block_list, grad_out):
    kv_h = to_heads(rotated_keys, value_vectors)
    size = lax.axis_size("head")
    here = lax.axis_index("head")
    tok, head_count, head_width = queries.shape
    run_len = size * tok
    groups = kv_h.shape[2]
    group_width = head_count // size // groups
    qg = jnp.stack([queries, grad_out]).reshape(2, tok, size, head_count // size * head_width)
    qg = jnp.transpose(qg, (2, 0, 1, 3))
    pieces = []
    for k in range(size):
        piece = lax.dynamic_index_in_dim(qg, (here + k) % size, axis=0, keepdims=False)
        if k:
            piece = lax.ppermute(piece, "head", [(i, (i + k) % size) for i in range(size)])
        pieces.append(piece)
    qg_pieces = jnp.stack(pieces)
    peer_of = (here - jnp.arange(size, dtype=jnp.int32)) % size
    head_count = head_count // size
    block_ids = run_len // BLOCK_TOKENS
    peers = lax.axis_size("blk")
    rank = lax.axis_index("blk")
    head_rank = lax.axis_index("head")
    offsets = jnp.arange(BLOCK_TOKENS, dtype=jnp.int32)
    block_range = jnp.arange(block_ids, dtype=jnp.int32)
    peer_range = jnp.arange(peers, dtype=jnp.int32)

    lists_here = lax.dynamic_slice_in_dim(block_list, head_rank * groups, groups, 0)
    lists_mine = lax.dynamic_slice_in_dim(lists_here, rank * block_ids, block_ids, 1)
    by_run = lists_here.reshape(groups, peers, block_ids * TOPK)
    in_mine = (by_run // block_ids) == rank
    named = jnp.max(jnp.where(in_mine, by_run % block_ids, -1), axis=-1)
    present = (named >= 0) & (peer_range != rank)[None, :]
    pick_send = (named[:, :, None] == block_range).astype(jnp.bfloat16)
    take_back = pick_send * present[..., None].astype(jnp.bfloat16)

    kv_local = jnp.transpose(
        kv_h.reshape(2, block_ids, BLOCK_TOKENS, groups, head_width), (3, 1, 0, 2, 4)
    )
    owner = lists_mine // block_ids
    slot_src = jnp.where(owner == rank, peers + lists_mine % block_ids, owner)
    slot_ids = jnp.arange(TOPK, dtype=jnp.int32)
    earlier = slot_ids[None, :] < slot_ids[:, None]
    repeated = jnp.any((lists_mine[..., :, None] == lists_mine[..., None, :]) & earlier, axis=-1)
    key_pos = lists_mine[..., None] * BLOCK_TOKENS + offsets
    key_pos = jnp.where(repeated[..., None], jnp.int32(2**30), key_pos)
    key_pos = key_pos.reshape(groups, block_ids, 1, TOPK * BLOCK_TOKENS)
    query_base = (rank * block_ids + block_range) * BLOCK_TOKENS

    outs, query_grads, backs, locals_ = [], [], [], []

    def heads_layout(parts):
        return jnp.concatenate(parts, axis=1).reshape(run_len, head_count, head_width)

    for g in range(groups):
        send = jnp.einsum(
            "rb,bktd->rktd", pick_send[g], kv_local[g], preferred_element_type=jnp.float32
        ).astype(jnp.bfloat16)
        recv = lax.all_to_all(send, "blk", split_axis=0, concat_axis=0, tiled=True)
        table = jnp.concatenate([recv, kv_local[g]], axis=0)
        o_g, dq_g, dk_acc, dv_acc = attend(
            slot_src[g].reshape(-1), query_base, peer_of, table, qg_pieces, key_pos[g], g, groups
        )
        outs.append(o_g)
        query_grads.append(dq_g)
        acc = jnp.stack([dk_acc, dv_acc], axis=1)
        remote = acc[:peers].astype(jnp.bfloat16)
        local = acc[peers:].astype(jnp.bfloat16)
        if g == groups - 1:
            attn_all, query_grad_all, remote, backs[0] = lax.optimization_barrier(
                (heads_layout(outs), heads_layout(query_grads), remote, backs[0])
            )
        backs.append(lax.all_to_all(remote, "blk", split_axis=0, concat_axis=0, tiled=True))
        locals_.append(local)

    def group_layout(parts):
        return jnp.stack(parts, axis=2).reshape(run_len, groups, head_width)

    key_grads, value_grads = [], []
    for g in range(groups):
        total = locals_[g].astype(jnp.float32) + jnp.einsum(
            "rl,rktd->lktd", take_back[g], backs[g], preferred_element_type=jnp.float32
        )
        total = total.astype(jnp.bfloat16)
        key_grads.append(total[:, 0])
        value_grads.append(total[:, 1])
    attn_out, grad_queries = from_heads(attn_all, query_grad_all)
    key_gradient, value_gradient = from_heads(group_layout(key_grads), group_layout(value_grads))
    return attn_out, grad_queries, key_gradient, value_gradient


def solution(mesh):
    in_specs = (
        P(("blk", "head"), None, None),
        P(("blk", "head"), None, None),
        P(("blk", "head"), None, None),
        P(),
        P(("blk", "head"), None, None),
    )
    out_specs = (
        P(("blk", "head"), None, None),
        P(("blk", "head"), None, None),
        P(("blk", "head"), None, None),
        P(("blk", "head"), None, None),
    )
    return jax.shard_map(
        on_device, mesh=mesh, in_specs=in_specs, out_specs=out_specs, check_vma=False
    )
```

```python
import jax
import jax.numpy as jnp
from jax import lax
from jax.sharding import PartitionSpec as P
from jax.experimental import pallas as pl
from jax.experimental.pallas import tpu as pltpu

BLOCK_TOKENS = 128
TOPK = 8


def exchange(x, part_axis, out_axis):
    size = lax.axis_size("head")
    here = lax.axis_index("head")
    pieces = []
    for k in range(size):
        piece = lax.dynamic_index_in_dim(x, (here + k) % size, axis=part_axis, keepdims=False)
        if k:
            piece = lax.ppermute(piece, "head", [(i, (i + k) % size) for i in range(size)])
        pieces.append(piece)
    ordered = jnp.stack([pieces[(-s) % size] for s in range(size)], axis=out_axis)
    return jnp.roll(ordered, here, axis=out_axis)


def to_heads(*xs):
    size = lax.axis_size("head")
    x = jnp.stack(xs)
    n, tok, heads, d = x.shape
    return lax.all_to_all(x, "head", split_axis=2, concat_axis=1, tiled=True)


def from_heads(*xs):
    size = lax.axis_size("head")
    x = jnp.stack(xs)
    n, run, part, d = x.shape
    x = x.reshape(n, size, run // size, part, d)
    both = exchange(x, 1, 2).reshape(n, run // size, size * part, d)
    return tuple(both[i] for i in range(len(xs)))


def attention_kernel(src_ref, base_ref, peer_ref, *refs):
    table_ref, q_lo, q_hi, do_lo, do_hi, kpos_ref = refs[:6]
    o_ref, dq_ref, dk_ref, dv_ref = refs[6:]
    b = pl.program_id(0)

    @pl.when(b == 0)
    def _():
        dk_ref[...] = jnp.zeros_like(dk_ref)
        dv_ref[...] = jnp.zeros_like(dv_ref)

    head_width = table_ref.shape[-1]
    group_width = q_lo.shape[-1] // head_width
    scale = head_width ** (-0.5)
    slots = [src_ref[b * TOPK + s] for s in range(TOPK)]
    keys = jnp.concatenate([table_ref[t, 0] for t in slots], axis=0)
    values = jnp.concatenate([table_ref[t, 1] for t in slots], axis=0)
    query_pos = base_ref[b] + lax.broadcasted_iota(jnp.int32, (BLOCK_TOKENS, 1), 0)
    allowed = kpos_ref[...] <= query_pos
    nt = (((1,), (1,)), ((), ()))
    tn = (((0,), (0,)), ((), ()))
    dk = None
    dv = None
    for j in range(group_width):
        cols = slice(j * head_width, (j + 1) * head_width)
        qj = jnp.concatenate([q_lo[:, cols], q_hi[:, cols]], axis=0)
        gj = jnp.concatenate([do_lo[:, cols], do_hi[:, cols]], axis=0)
        s = lax.dot_general(qj, keys, nt, preferred_element_type=jnp.float32) * scale
        s = jnp.where(allowed, s, -jnp.inf)
        m = jnp.max(s, axis=-1, keepdims=True)
        lt = m + jnp.log(jnp.sum(jnp.exp(s - m), axis=-1, keepdims=True))
        p = jnp.exp(s - lt)
        pb = p.astype(jnp.bfloat16)
        o = jnp.dot(pb, values, preferred_element_type=jnp.float32).astype(jnp.bfloat16)
        o_ref[:, cols] = o
        rd = jnp.sum(gj.astype(jnp.float32) * o.astype(jnp.float32), axis=-1, keepdims=True)
        dp = lax.dot_general(gj, values, nt, preferred_element_type=jnp.float32)
        ds = (p * (dp - rd)).astype(jnp.bfloat16)
        dq = jnp.dot(ds, keys, preferred_element_type=jnp.float32) * scale
        dq_ref[:, cols] = dq.astype(jnp.bfloat16)
        dkj = lax.dot_general(ds, qj, tn, preferred_element_type=jnp.float32)
        dvj = lax.dot_general(pb, gj, tn, preferred_element_type=jnp.float32)
        dk = dkj if dk is None else dk + dkj
        dv = dvj if dv is None else dv + dvj
    dk = dk * scale
    for s in range(TOPK):
        t = src_ref[b * TOPK + s]
        rows = slice(s * BLOCK_TOKENS, (s + 1) * BLOCK_TOKENS)
        dk_ref[t] = dk_ref[t] + dk[rows]
        dv_ref[t] = dv_ref[t] + dv[rows]


def attend(slot_src, query_base, peer_of, table, pieces, key_pos, group, groups):
    piece_len = pieces.shape[2]
    run_len = pieces.shape[0] * piece_len
    block_ids = run_len // BLOCK_TOKENS
    targets = table.shape[0]
    head_width = table.shape[-1]
    row_width = pieces.shape[-1] // groups
    half = BLOCK_TOKENS // 2
    per_piece = piece_len // half

    def half_spec(which, part):
        def index(b, src, base, peer):
            i = 2 * b + part
            return (peer[i // per_piece], which, i % per_piece, group)

        return pl.BlockSpec((None, None, half, row_width), index)

    table_spec = pl.BlockSpec(table.shape, lambda b, src, base, peer: (0, 0, 0, 0))

    out_row = pl.BlockSpec((BLOCK_TOKENS, row_width), lambda b, src, base, peer: (b, 0))
    pos_spec = pl.BlockSpec((None, 1, TOPK * BLOCK_TOKENS), lambda b, src, base, peer: (b, 0, 0))
    acc_spec = pl.BlockSpec((targets, BLOCK_TOKENS, head_width), lambda b, src, base, peer: (0, 0, 0))
    in_specs = (
        [table_spec]
        + [half_spec(0, 0), half_spec(0, 1), half_spec(1, 0), half_spec(1, 1), pos_spec]
    )
    out_shape = (
        jax.ShapeDtypeStruct((run_len, row_width), jnp.bfloat16),
        jax.ShapeDtypeStruct((run_len, row_width), jnp.bfloat16),
        jax.ShapeDtypeStruct((targets, BLOCK_TOKENS, head_width), jnp.float32),
        jax.ShapeDtypeStruct((targets, BLOCK_TOKENS, head_width), jnp.float32),
    )
    grid_spec = pltpu.PrefetchScalarGridSpec(
        num_scalar_prefetch=3,
        grid=(block_ids,),
        in_specs=in_specs,
        out_specs=(out_row, out_row, acc_spec, acc_spec),
    )
    return pl.pallas_call(
        attention_kernel,
        grid_spec=grid_spec,
        out_shape=out_shape,
        compiler_params=pltpu.CompilerParams(
            dimension_semantics=("arbitrary",),
            vmem_limit_bytes=48 * 1024 * 1024,
        ),
    )(slot_src, query_base, peer_of, table, *([pieces] * 4), key_pos)


def on_device(queries, rotated_keys, value_vectors, block_list, grad_out):
    kv_h = to_heads(rotated_keys, value_vectors)
    size = lax.axis_size("head")
    here = lax.axis_index("head")
    tok, head_count, head_width = queries.shape
    run_len = size * tok
    groups = kv_h.shape[2]
    group_width = head_count // size // groups
    qg = jnp.stack([queries, grad_out]).reshape(2, tok, size, head_count // size * head_width)
    qg = jnp.transpose(qg, (2, 0, 1, 3))
    pieces = []
    for k in range(size):
        piece = lax.dynamic_index_in_dim(qg, (here + k) % size, axis=0, keepdims=False)
        if k:
            piece = lax.ppermute(piece, "head", [(i, (i + k) % size) for i in range(size)])
        pieces.append(piece)
    qg_pieces = jnp.stack(pieces)
    peer_of = (here - jnp.arange(size, dtype=jnp.int32)) % size
    head_count = head_count // size
    block_ids = run_len // BLOCK_TOKENS
    peers = lax.axis_size("blk")
    rank = lax.axis_index("blk")
    head_rank = lax.axis_index("head")
    offsets = jnp.arange(BLOCK_TOKENS, dtype=jnp.int32)
    block_range = jnp.arange(block_ids, dtype=jnp.int32)
    peer_range = jnp.arange(peers, dtype=jnp.int32)

    lists_here = lax.dynamic_slice_in_dim(block_list, head_rank * groups, groups, 0)
    lists_mine = lax.dynamic_slice_in_dim(lists_here, rank * block_ids, block_ids, 1)
    by_run = lists_here.reshape(groups, peers, block_ids * TOPK)
    in_mine = (by_run // block_ids) == rank
    named = jnp.max(jnp.where(in_mine, by_run % block_ids, -1), axis=-1)
    present = (named >= 0) & (peer_range != rank)[None, :]
    pick_send = (named[:, :, None] == block_range).astype(jnp.bfloat16)
    take_back = pick_send * present[..., None].astype(jnp.bfloat16)

    kv_local = jnp.transpose(
        kv_h.reshape(2, block_ids, BLOCK_TOKENS, groups, head_width), (3, 1, 0, 2, 4)
    )
    owner = lists_mine // block_ids
    slot_src = jnp.where(owner == rank, peers + lists_mine % block_ids, owner)
    slot_ids = jnp.arange(TOPK, dtype=jnp.int32)
    earlier = slot_ids[None, :] < slot_ids[:, None]
    repeated = jnp.any((lists_mine[..., :, None] == lists_mine[..., None, :]) & earlier, axis=-1)
    key_pos = lists_mine[..., None] * BLOCK_TOKENS + offsets
    key_pos = jnp.where(repeated[..., None], jnp.int32(2**30), key_pos)
    key_pos = key_pos.reshape(groups, block_ids, 1, TOPK * BLOCK_TOKENS)
    query_base = (rank * block_ids + block_range) * BLOCK_TOKENS

    outs, query_grads, backs, locals_ = [], [], [], []

    def heads_layout(parts):
        return jnp.concatenate(parts, axis=1).reshape(run_len, head_count, head_width)

    for g in range(groups):
        send = jnp.einsum(
            "rb,bktd->rktd", pick_send[g], kv_local[g], preferred_element_type=jnp.float32
        ).astype(jnp.bfloat16)
        recv = lax.all_to_all(send, "blk", split_axis=0, concat_axis=0, tiled=True)
        table = jnp.concatenate([recv, kv_local[g]], axis=0)
        o_g, dq_g, dk_acc, dv_acc = attend(
            slot_src[g].reshape(-1), query_base, peer_of, table, qg_pieces, key_pos[g], g, groups
        )
        outs.append(o_g)
        query_grads.append(dq_g)
        acc = jnp.stack([dk_acc, dv_acc], axis=1)
        remote = acc[:peers].astype(jnp.bfloat16)
        local = acc[peers:].astype(jnp.bfloat16)
        if g == groups - 1:
            attn_all, query_grad_all, remote, backs[0] = lax.optimization_barrier(
                (heads_layout(outs), heads_layout(query_grads), remote, backs[0])
            )
        backs.append(lax.all_to_all(remote, "blk", split_axis=0, concat_axis=0, tiled=True))
        locals_.append(local)

    def group_layout(parts):
        return jnp.stack(parts, axis=2).reshape(run_len, groups, head_width)

    key_grads, value_grads = [], []
    for g in range(groups):
        total = locals_[g].astype(jnp.float32) + jnp.einsum(
            "rl,rktd->lktd", take_back[g], backs[g], preferred_element_type=jnp.float32
        )
        total = total.astype(jnp.bfloat16)
        key_grads.append(total[:, 0])
        value_grads.append(total[:, 1])
    attn_out, grad_queries = from_heads(attn_all, query_grad_all)
    grads = lax.all_to_all(
        jnp.stack([group_layout(key_grads), group_layout(value_grads)]),
        "head", split_axis=1, concat_axis=2, tiled=True,
    )
    key_gradient, value_gradient = grads[0], grads[1]
    return attn_out, grad_queries, key_gradient, value_gradient


def solution(mesh):
    in_specs = (
        P(("blk", "head"), None, None),
        P(("blk", "head"), None, None),
        P(("blk", "head"), None, None),
        P(),
        P(("blk", "head"), None, None),
    )
    out_specs = (
        P(("blk", "head"), None, None),
        P(("blk", "head"), None, None),
        P(("blk", "head"), None, None),
        P(("blk", "head"), None, None),
    )
    return jax.shard_map(
        on_device, mesh=mesh, in_specs=in_specs, out_specs=out_specs, check_vma=False
    )
```

```python
import jax
import jax.numpy as jnp
from jax import lax
from jax.sharding import PartitionSpec as P
from jax.experimental import pallas as pl
from jax.experimental.pallas import tpu as pltpu

BLOCK_TOKENS = 128
TOPK = 8


def exchange(x, part_axis, out_axis):
    size = lax.axis_size("head")
    here = lax.axis_index("head")
    pieces = []
    for k in range(size):
        piece = lax.dynamic_index_in_dim(x, (here + k) % size, axis=part_axis, keepdims=False)
        if k:
            piece = lax.ppermute(piece, "head", [(i, (i + k) % size) for i in range(size)])
        pieces.append(piece)
    ordered = jnp.stack([pieces[(-s) % size] for s in range(size)], axis=out_axis)
    return jnp.roll(ordered, here, axis=out_axis)


def to_heads(*xs):
    size = lax.axis_size("head")
    x = jnp.stack(xs)
    n, tok, heads, d = x.shape
    return lax.all_to_all(x, "head", split_axis=2, concat_axis=1, tiled=True)


def from_heads(*xs):
    size = lax.axis_size("head")
    x = jnp.stack(xs)
    n, run, part, d = x.shape
    x = x.reshape(n, size, run // size, part, d)
    both = exchange(x, 1, 2).reshape(n, run // size, size * part, d)
    return tuple(both[i] for i in range(len(xs)))


def attention_kernel(src_ref, base_ref, peer_ref, *refs):
    recv_ref, local_ref, q_lo, q_hi, do_lo, do_hi, kpos_ref = refs[:7]
    o_ref, dq_ref, dk_ref, dv_ref = refs[7:]
    b = pl.program_id(0)

    @pl.when(b == 0)
    def _():
        dk_ref[...] = jnp.zeros_like(dk_ref)
        dv_ref[...] = jnp.zeros_like(dv_ref)

    head_width = recv_ref.shape[-1]
    group_width = q_lo.shape[-1] // head_width
    scale = head_width ** (-0.5)
    slots = [src_ref[b * TOPK + s] for s in range(TOPK)]
    peers = recv_ref.shape[0]

    def pick(t, kv):
        there = recv_ref[jnp.minimum(t, peers - 1), kv]
        here = local_ref[jnp.maximum(t - peers, 0), kv]
        return jnp.where(t < peers, there, here)

    keys = jnp.concatenate([pick(t, 0) for t in slots], axis=0)
    values = jnp.concatenate([pick(t, 1) for t in slots], axis=0)
    query_pos = base_ref[b] + lax.broadcasted_iota(jnp.int32, (BLOCK_TOKENS, 1), 0)
    allowed = kpos_ref[...] <= query_pos
    nt = (((1,), (1,)), ((), ()))
    tn = (((0,), (0,)), ((), ()))
    dk = None
    dv = None
    for j in range(group_width):
        cols = slice(j * head_width, (j + 1) * head_width)
        qj = jnp.concatenate([q_lo[:, cols], q_hi[:, cols]], axis=0)
        gj = jnp.concatenate([do_lo[:, cols], do_hi[:, cols]], axis=0)
        s = lax.dot_general(qj, keys, nt, preferred_element_type=jnp.float32) * scale
        s = jnp.where(allowed, s, -jnp.inf)
        m = jnp.max(s, axis=-1, keepdims=True)
        lt = m + jnp.log(jnp.sum(jnp.exp(s - m), axis=-1, keepdims=True))
        p = jnp.exp(s - lt)
        pb = p.astype(jnp.bfloat16)
        o = jnp.dot(pb, values, preferred_element_type=jnp.float32).astype(jnp.bfloat16)
        o_ref[:, cols] = o
        rd = jnp.sum(gj.astype(jnp.float32) * o.astype(jnp.float32), axis=-1, keepdims=True)
        dp = lax.dot_general(gj, values, nt, preferred_element_type=jnp.float32)
        ds = (p * (dp - rd)).astype(jnp.bfloat16)
        dq = jnp.dot(ds, keys, preferred_element_type=jnp.float32) * scale
        dq_ref[:, cols] = dq.astype(jnp.bfloat16)
        dkj = lax.dot_general(ds, qj, tn, preferred_element_type=jnp.float32)
        dvj = lax.dot_general(pb, gj, tn, preferred_element_type=jnp.float32)
        dk = dkj if dk is None else dk + dkj
        dv = dvj if dv is None else dv + dvj
    dk = dk * scale
    for s in range(TOPK):
        t = src_ref[b * TOPK + s]
        rows = slice(s * BLOCK_TOKENS, (s + 1) * BLOCK_TOKENS)
        dk_ref[t] = dk_ref[t] + dk[rows]
        dv_ref[t] = dv_ref[t] + dv[rows]


def attend(slot_src, query_base, peer_of, recv, local, pieces, key_pos, group, groups):
    piece_len = pieces.shape[2]
    run_len = pieces.shape[0] * piece_len
    block_ids = run_len // BLOCK_TOKENS
    targets = recv.shape[0] + local.shape[0]
    head_width = recv.shape[-1]
    row_width = pieces.shape[-1] // groups
    half = BLOCK_TOKENS // 2
    per_piece = piece_len // half

    def half_spec(which, part):
        def index(b, src, base, peer):
            i = 2 * b + part
            return (peer[i // per_piece], which, i % per_piece, group)

        return pl.BlockSpec((None, None, half, row_width), index)

    recv_spec = pl.BlockSpec(recv.shape, lambda b, src, base, peer: (0, 0, 0, 0))
    local_spec = pl.BlockSpec(local.shape, lambda b, src, base, peer: (0, 0, 0, 0))

    out_row = pl.BlockSpec((BLOCK_TOKENS, row_width), lambda b, src, base, peer: (b, 0))
    pos_spec = pl.BlockSpec((None, 1, TOPK * BLOCK_TOKENS), lambda b, src, base, peer: (b, 0, 0))
    acc_spec = pl.BlockSpec((targets, BLOCK_TOKENS, head_width), lambda b, src, base, peer: (0, 0, 0))
    in_specs = (
        [recv_spec, local_spec]
        + [half_spec(0, 0), half_spec(0, 1), half_spec(1, 0), half_spec(1, 1), pos_spec]
    )
    out_shape = (
        jax.ShapeDtypeStruct((run_len, row_width), jnp.bfloat16),
        jax.ShapeDtypeStruct((run_len, row_width), jnp.bfloat16),
        jax.ShapeDtypeStruct((targets, BLOCK_TOKENS, head_width), jnp.float32),
        jax.ShapeDtypeStruct((targets, BLOCK_TOKENS, head_width), jnp.float32),
    )
    grid_spec = pltpu.PrefetchScalarGridSpec(
        num_scalar_prefetch=3,
        grid=(block_ids,),
        in_specs=in_specs,
        out_specs=(out_row, out_row, acc_spec, acc_spec),
    )
    return pl.pallas_call(
        attention_kernel,
        grid_spec=grid_spec,
        out_shape=out_shape,
        compiler_params=pltpu.CompilerParams(
            dimension_semantics=("arbitrary",),
            vmem_limit_bytes=48 * 1024 * 1024,
        ),
    )(slot_src, query_base, peer_of, recv, local, *([pieces] * 4), key_pos)


def on_device(queries, rotated_keys, value_vectors, block_list, grad_out):
    kv_h = to_heads(rotated_keys, value_vectors)
    size = lax.axis_size("head")
    here = lax.axis_index("head")
    tok, head_count, head_width = queries.shape
    run_len = size * tok
    groups = kv_h.shape[2]
    group_width = head_count // size // groups
    qg = jnp.stack([queries, grad_out]).reshape(2, tok, size, head_count // size * head_width)
    qg = jnp.transpose(qg, (2, 0, 1, 3))
    pieces = []
    for k in range(size):
        piece = lax.dynamic_index_in_dim(qg, (here + k) % size, axis=0, keepdims=False)
        if k:
            piece = lax.ppermute(piece, "head", [(i, (i + k) % size) for i in range(size)])
        pieces.append(piece)
    qg_pieces = jnp.stack(pieces)
    peer_of = (here - jnp.arange(size, dtype=jnp.int32)) % size
    head_count = head_count // size
    block_ids = run_len // BLOCK_TOKENS
    peers = lax.axis_size("blk")
    rank = lax.axis_index("blk")
    head_rank = lax.axis_index("head")
    offsets = jnp.arange(BLOCK_TOKENS, dtype=jnp.int32)
    block_range = jnp.arange(block_ids, dtype=jnp.int32)
    peer_range = jnp.arange(peers, dtype=jnp.int32)

    lists_here = lax.dynamic_slice_in_dim(block_list, head_rank * groups, groups, 0)
    lists_mine = lax.dynamic_slice_in_dim(lists_here, rank * block_ids, block_ids, 1)
    by_run = lists_here.reshape(groups, peers, block_ids * TOPK)
    in_mine = (by_run // block_ids) == rank
    named = jnp.max(jnp.where(in_mine, by_run % block_ids, -1), axis=-1)
    present = (named >= 0) & (peer_range != rank)[None, :]
    pick_send = (named[:, :, None] == block_range).astype(jnp.bfloat16)
    take_back = pick_send * present[..., None].astype(jnp.bfloat16)

    kv_local = jnp.transpose(
        kv_h.reshape(2, block_ids, BLOCK_TOKENS, groups, head_width), (3, 1, 0, 2, 4)
    )
    owner = lists_mine // block_ids
    slot_src = jnp.where(owner == rank, peers + lists_mine % block_ids, owner)
    slot_ids = jnp.arange(TOPK, dtype=jnp.int32)
    earlier = slot_ids[None, :] < slot_ids[:, None]
    repeated = jnp.any((lists_mine[..., :, None] == lists_mine[..., None, :]) & earlier, axis=-1)
    key_pos = lists_mine[..., None] * BLOCK_TOKENS + offsets
    key_pos = jnp.where(repeated[..., None], jnp.int32(2**30), key_pos)
    key_pos = key_pos.reshape(groups, block_ids, 1, TOPK * BLOCK_TOKENS)
    query_base = (rank * block_ids + block_range) * BLOCK_TOKENS

    outs, query_grads, backs, locals_ = [], [], [], []

    def heads_layout(parts):
        return jnp.concatenate(parts, axis=1).reshape(run_len, head_count, head_width)

    for g in range(groups):
        send = jnp.einsum(
            "rb,bktd->rktd", pick_send[g], kv_local[g], preferred_element_type=jnp.float32
        ).astype(jnp.bfloat16)
        recv = lax.all_to_all(send, "blk", split_axis=0, concat_axis=0, tiled=True)
        o_g, dq_g, dk_acc, dv_acc = attend(
            slot_src[g].reshape(-1), query_base, peer_of, recv, kv_local[g], qg_pieces, key_pos[g], g, groups
        )
        outs.append(o_g)
        query_grads.append(dq_g)
        acc = jnp.stack([dk_acc, dv_acc], axis=1)
        remote = acc[:peers].astype(jnp.bfloat16)
        local = acc[peers:].astype(jnp.bfloat16)
        if g == groups - 1:
            attn_all, query_grad_all, remote, backs[0] = lax.optimization_barrier(
                (heads_layout(outs), heads_layout(query_grads), remote, backs[0])
            )
        backs.append(lax.all_to_all(remote, "blk", split_axis=0, concat_axis=0, tiled=True))
        locals_.append(local)

    def group_layout(parts):
        return jnp.stack(parts, axis=2).reshape(run_len, groups, head_width)

    key_grads, value_grads = [], []
    for g in range(groups):
        total = locals_[g].astype(jnp.float32) + jnp.einsum(
            "rl,rktd->lktd", take_back[g], backs[g], preferred_element_type=jnp.float32
        )
        total = total.astype(jnp.bfloat16)
        key_grads.append(total[:, 0])
        value_grads.append(total[:, 1])
    attn_out, grad_queries = from_heads(attn_all, query_grad_all)
    key_gradient, value_gradient = from_heads(group_layout(key_grads), group_layout(value_grads))
    return attn_out, grad_queries, key_gradient, value_gradient


def solution(mesh):
    in_specs = (
        P(("blk", "head"), None, None),
        P(("blk", "head"), None, None),
        P(("blk", "head"), None, None),
        P(),
        P(("blk", "head"), None, None),
    )
    out_specs = (
        P(("blk", "head"), None, None),
        P(("blk", "head"), None, None),
        P(("blk", "head"), None, None),
        P(("blk", "head"), None, None),
    )
    return jax.shard_map(
        on_device, mesh=mesh, in_specs=in_specs, out_specs=out_specs, check_vma=False
    )
```

```python
import jax
import jax.numpy as jnp
from jax import lax
from jax.sharding import PartitionSpec as P
from jax.experimental import pallas as pl
from jax.experimental.pallas import tpu as pltpu

BLOCK_TOKENS = 128
TOPK = 8


def exchange(x, part_axis, out_axis):
    size = lax.axis_size("head")
    here = lax.axis_index("head")
    pieces = []
    for k in range(size):
        piece = lax.dynamic_index_in_dim(x, (here + k) % size, axis=part_axis, keepdims=False)
        if k:
            piece = lax.ppermute(piece, "head", [(i, (i + k) % size) for i in range(size)])
        pieces.append(piece)
    ordered = jnp.stack([pieces[(-s) % size] for s in range(size)], axis=out_axis)
    return jnp.roll(ordered, here, axis=out_axis)


def to_heads(*xs):
    size = lax.axis_size("head")
    x = jnp.stack(xs)
    n, tok, heads, d = x.shape
    return lax.all_to_all(x, "head", split_axis=2, concat_axis=1, tiled=True)


def from_heads(*xs):
    size = lax.axis_size("head")
    x = jnp.stack(xs)
    n, run, part, d = x.shape
    x = x.reshape(n, size, run // size, part, d)
    both = exchange(x, 1, 2).reshape(n, run // size, size * part, d)
    return tuple(both[i] for i in range(len(xs)))


def attention_kernel(src_ref, base_ref, peer_ref, *refs):
    table_ref, q_lo, q_hi, do_lo, do_hi, kpos_ref = refs[:6]
    o_ref, dq_ref, part_ref, dk_ref, dv_ref = refs[6:]
    b = pl.program_id(0)

    @pl.when(b == 0)
    def _():
        dk_ref[...] = jnp.zeros_like(dk_ref)
        dv_ref[...] = jnp.zeros_like(dv_ref)

    head_width = table_ref.shape[-1]
    group_width = q_lo.shape[-1] // head_width
    scale = head_width ** (-0.5)
    slots = [src_ref[b * TOPK + s] for s in range(TOPK)]
    keys = jnp.concatenate([table_ref[t, 0] for t in slots], axis=0)
    values = jnp.concatenate([table_ref[t, 1] for t in slots], axis=0)
    query_pos = base_ref[b] + lax.broadcasted_iota(jnp.int32, (BLOCK_TOKENS, 1), 0)
    allowed = kpos_ref[...] <= query_pos
    nt = (((1,), (1,)), ((), ()))
    tn = (((0,), (0,)), ((), ()))
    dk = None
    dv = None
    for j in range(group_width):
        cols = slice(j * head_width, (j + 1) * head_width)
        qj = jnp.concatenate([q_lo[:, cols], q_hi[:, cols]], axis=0)
        gj = jnp.concatenate([do_lo[:, cols], do_hi[:, cols]], axis=0)
        s = lax.dot_general(qj, keys, nt, preferred_element_type=jnp.float32) * scale
        s = jnp.where(allowed, s, -jnp.inf)
        m = jnp.max(s, axis=-1, keepdims=True)
        lt = m + jnp.log(jnp.sum(jnp.exp(s - m), axis=-1, keepdims=True))
        p = jnp.exp(s - lt)
        pb = p.astype(jnp.bfloat16)
        o = jnp.dot(pb, values, preferred_element_type=jnp.float32).astype(jnp.bfloat16)
        o_ref[:, cols] = o
        rd = jnp.sum(gj.astype(jnp.float32) * o.astype(jnp.float32), axis=-1, keepdims=True)
        dp = lax.dot_general(gj, values, nt, preferred_element_type=jnp.float32)
        ds = (p * (dp - rd)).astype(jnp.bfloat16)
        dq = jnp.dot(ds, keys, preferred_element_type=jnp.float32) * scale
        dq_ref[:, cols] = dq.astype(jnp.bfloat16)
        dkj = lax.dot_general(ds, qj, tn, preferred_element_type=jnp.float32)
        dvj = lax.dot_general(pb, gj, tn, preferred_element_type=jnp.float32)
        dk = dkj if dk is None else dk + dkj
        dv = dvj if dv is None else dv + dvj
    dk = dk * scale
    for s in range(TOPK):
        t = src_ref[b * TOPK + s]
        rows = slice(s * BLOCK_TOKENS, (s + 1) * BLOCK_TOKENS)
        dk_ref[t] = dk_ref[t] + dk[rows]
        dv_ref[t] = dv_ref[t] + dv[rows]

    @pl.when(b == pl.num_programs(0) - 1)
    def _():
        part_ref[:, 0] = dk_ref[...].astype(part_ref.dtype)
        part_ref[:, 1] = dv_ref[...].astype(part_ref.dtype)


def attend(slot_src, query_base, peer_of, table, pieces, key_pos, group, groups):
    piece_len = pieces.shape[2]
    run_len = pieces.shape[0] * piece_len
    block_ids = run_len // BLOCK_TOKENS
    targets = table.shape[0]
    head_width = table.shape[-1]
    row_width = pieces.shape[-1] // groups
    half = BLOCK_TOKENS // 2
    per_piece = piece_len // half

    def half_spec(which, part):
        def index(b, src, base, peer):
            i = 2 * b + part
            return (peer[i // per_piece], which, i % per_piece, group)

        return pl.BlockSpec((None, None, half, row_width), index)

    table_spec = pl.BlockSpec(table.shape, lambda b, src, base, peer: (0, 0, 0, 0))

    out_row = pl.BlockSpec((BLOCK_TOKENS, row_width), lambda b, src, base, peer: (b, 0))
    pos_spec = pl.BlockSpec((None, 1, TOPK * BLOCK_TOKENS), lambda b, src, base, peer: (b, 0, 0))
    part_spec = pl.BlockSpec(
        (targets, 2, BLOCK_TOKENS, head_width), lambda b, src, base, peer: (0, 0, 0, 0)
    )
    in_specs = (
        [table_spec]
        + [half_spec(0, 0), half_spec(0, 1), half_spec(1, 0), half_spec(1, 1), pos_spec]
    )
    out_shape = (
        jax.ShapeDtypeStruct((run_len, row_width), jnp.bfloat16),
        jax.ShapeDtypeStruct((run_len, row_width), jnp.bfloat16),
        jax.ShapeDtypeStruct((targets, 2, BLOCK_TOKENS, head_width), jnp.bfloat16),
    )
    grid_spec = pltpu.PrefetchScalarGridSpec(
        num_scalar_prefetch=3,
        grid=(block_ids,),
        in_specs=in_specs,
        out_specs=(out_row, out_row, part_spec),
        scratch_shapes=[pltpu.VMEM((targets, BLOCK_TOKENS, head_width), jnp.float32)] * 2,
    )
    return pl.pallas_call(
        attention_kernel,
        grid_spec=grid_spec,
        out_shape=out_shape,
        compiler_params=pltpu.CompilerParams(
            dimension_semantics=("arbitrary",),
            vmem_limit_bytes=48 * 1024 * 1024,
        ),
    )(slot_src, query_base, peer_of, table, *([pieces] * 4), key_pos)


def on_device(queries, rotated_keys, value_vectors, block_list, grad_out):
    kv_h = to_heads(rotated_keys, value_vectors)
    size = lax.axis_size("head")
    here = lax.axis_index("head")
    tok, head_count, head_width = queries.shape
    run_len = size * tok
    groups = kv_h.shape[2]
    group_width = head_count // size // groups
    qg = jnp.stack([queries, grad_out]).reshape(2, tok, size, head_count // size * head_width)
    qg = jnp.transpose(qg, (2, 0, 1, 3))
    pieces = []
    for k in range(size):
        piece = lax.dynamic_index_in_dim(qg, (here + k) % size, axis=0, keepdims=False)
        if k:
            piece = lax.ppermute(piece, "head", [(i, (i + k) % size) for i in range(size)])
        pieces.append(piece)
    qg_pieces = jnp.stack(pieces)
    peer_of = (here - jnp.arange(size, dtype=jnp.int32)) % size
    head_count = head_count // size
    block_ids = run_len // BLOCK_TOKENS
    peers = lax.axis_size("blk")
    rank = lax.axis_index("blk")
    head_rank = lax.axis_index("head")
    offsets = jnp.arange(BLOCK_TOKENS, dtype=jnp.int32)
    block_range = jnp.arange(block_ids, dtype=jnp.int32)
    peer_range = jnp.arange(peers, dtype=jnp.int32)

    lists_here = lax.dynamic_slice_in_dim(block_list, head_rank * groups, groups, 0)
    lists_mine = lax.dynamic_slice_in_dim(lists_here, rank * block_ids, block_ids, 1)
    by_run = lists_here.reshape(groups, peers, block_ids * TOPK)
    in_mine = (by_run // block_ids) == rank
    named = jnp.max(jnp.where(in_mine, by_run % block_ids, -1), axis=-1)
    present = (named >= 0) & (peer_range != rank)[None, :]
    pick_send = (named[:, :, None] == block_range).astype(jnp.bfloat16)
    take_back = pick_send * present[..., None].astype(jnp.bfloat16)

    kv_local = jnp.transpose(
        kv_h.reshape(2, block_ids, BLOCK_TOKENS, groups, head_width), (3, 1, 0, 2, 4)
    )
    owner = lists_mine // block_ids
    slot_src = jnp.where(owner == rank, peers + lists_mine % block_ids, owner)
    slot_ids = jnp.arange(TOPK, dtype=jnp.int32)
    earlier = slot_ids[None, :] < slot_ids[:, None]
    repeated = jnp.any((lists_mine[..., :, None] == lists_mine[..., None, :]) & earlier, axis=-1)
    key_pos = lists_mine[..., None] * BLOCK_TOKENS + offsets
    key_pos = jnp.where(repeated[..., None], jnp.int32(2**30), key_pos)
    key_pos = key_pos.reshape(groups, block_ids, 1, TOPK * BLOCK_TOKENS)
    query_base = (rank * block_ids + block_range) * BLOCK_TOKENS

    outs, query_grads, backs, locals_ = [], [], [], []

    def heads_layout(parts):
        return jnp.concatenate(parts, axis=1).reshape(run_len, head_count, head_width)

    for g in range(groups):
        send = jnp.einsum(
            "rb,bktd->rktd", pick_send[g], kv_local[g], preferred_element_type=jnp.float32
        ).astype(jnp.bfloat16)
        recv = lax.all_to_all(send, "blk", split_axis=0, concat_axis=0, tiled=True)
        table = jnp.concatenate([recv, kv_local[g]], axis=0)
        o_g, dq_g, part = attend(
            slot_src[g].reshape(-1), query_base, peer_of, table, qg_pieces, key_pos[g], g, groups
        )
        outs.append(o_g)
        query_grads.append(dq_g)
        remote = part[:peers]
        local = part[peers:]
        if g == groups - 1:
            attn_all, query_grad_all, remote, backs[0] = lax.optimization_barrier(
                (heads_layout(outs), heads_layout(query_grads), remote, backs[0])
            )
        backs.append(lax.all_to_all(remote, "blk", split_axis=0, concat_axis=0, tiled=True))
        locals_.append(local)

    def group_layout(parts):
        return jnp.stack(parts, axis=2).reshape(run_len, groups, head_width)

    key_grads, value_grads = [], []
    for g in range(groups):
        total = locals_[g].astype(jnp.float32) + jnp.einsum(
            "rl,rktd->lktd", take_back[g], backs[g], preferred_element_type=jnp.float32
        )
        total = total.astype(jnp.bfloat16)
        key_grads.append(total[:, 0])
        value_grads.append(total[:, 1])
    attn_out, grad_queries = from_heads(attn_all, query_grad_all)
    key_gradient, value_gradient = from_heads(group_layout(key_grads), group_layout(value_grads))
    return attn_out, grad_queries, key_gradient, value_gradient


def solution(mesh):
    in_specs = (
        P(("blk", "head"), None, None),
        P(("blk", "head"), None, None),
        P(("blk", "head"), None, None),
        P(),
        P(("blk", "head"), None, None),
    )
    out_specs = (
        P(("blk", "head"), None, None),
        P(("blk", "head"), None, None),
        P(("blk", "head"), None, None),
        P(("blk", "head"), None, None),
    )
    return jax.shard_map(
        on_device, mesh=mesh, in_specs=in_specs, out_specs=out_specs, check_vma=False
    )
```

```python
import jax
import jax.numpy as jnp
from jax import lax
from jax.sharding import PartitionSpec as P
from jax.experimental import pallas as pl
from jax.experimental.pallas import tpu as pltpu

BLOCK_TOKENS = 128
TOPK = 8


def exchange(x, part_axis, out_axis):
    size = lax.axis_size("head")
    here = lax.axis_index("head")
    pieces = []
    for k in range(size):
        piece = lax.dynamic_index_in_dim(x, (here + k) % size, axis=part_axis, keepdims=False)
        if k:
            piece = lax.ppermute(piece, "head", [(i, (i + k) % size) for i in range(size)])
        pieces.append(piece)
    ordered = jnp.stack([pieces[(-s) % size] for s in range(size)], axis=out_axis)
    return jnp.roll(ordered, here, axis=out_axis)


def to_heads(*xs):
    size = lax.axis_size("head")
    x = jnp.stack(xs)
    n, tok, heads, d = x.shape
    return lax.all_to_all(x, "head", split_axis=2, concat_axis=1, tiled=True)


def from_heads(*xs):
    size = lax.axis_size("head")
    x = jnp.stack(xs)
    n, run, part, d = x.shape
    x = x.reshape(n, size, run // size, part, d)
    both = exchange(x, 1, 2).reshape(n, run // size, size * part, d)
    return tuple(both[i] for i in range(len(xs)))


def attention_kernel(src_ref, base_ref, peer_ref, *refs):
    table_ref, q_lo, q_hi, do_lo, do_hi, kpos_ref = refs[:6]
    o_ref, dq_ref, dk_ref, dv_ref = refs[6:]
    b = pl.program_id(0)

    @pl.when(b == 0)
    def _():
        dk_ref[...] = jnp.zeros_like(dk_ref)
        dv_ref[...] = jnp.zeros_like(dv_ref)

    head_width = table_ref.shape[-1]
    group_width = q_lo.shape[-1] // head_width
    scale = head_width ** (-0.5)
    slots = [src_ref[b * TOPK + s] for s in range(TOPK)]
    keys = jnp.concatenate([table_ref[t, 0] for t in slots], axis=0)
    values = jnp.concatenate([table_ref[t, 1] for t in slots], axis=0)
    query_pos = base_ref[b] + lax.broadcasted_iota(jnp.int32, (BLOCK_TOKENS, 1), 0)
    allowed = kpos_ref[...] <= query_pos
    nt = (((1,), (1,)), ((), ()))
    tn = (((0,), (0,)), ((), ()))
    dk = None
    dv = None
    for j in range(group_width):
        cols = slice(j * head_width, (j + 1) * head_width)
        qj = jnp.concatenate([q_lo[:, cols], q_hi[:, cols]], axis=0)
        gj = jnp.concatenate([do_lo[:, cols], do_hi[:, cols]], axis=0)
        s = lax.dot_general(qj, keys, nt, preferred_element_type=jnp.float32) * scale
        s = jnp.where(allowed, s, -jnp.inf)
        m = jnp.max(s, axis=-1, keepdims=True)
        lt = m + jnp.log(jnp.sum(jnp.exp(s - m), axis=-1, keepdims=True))
        p = jnp.exp(s - lt)
        pb = p.astype(jnp.bfloat16)
        o = jnp.dot(pb, values, preferred_element_type=jnp.float32).astype(jnp.bfloat16)
        o_ref[:, cols] = o
        rd = jnp.sum(gj.astype(jnp.float32) * o.astype(jnp.float32), axis=-1, keepdims=True)
        dp = lax.dot_general(gj, values, nt, preferred_element_type=jnp.float32)
        ds = (p * (dp - rd)).astype(jnp.bfloat16)
        dq = jnp.dot(ds, keys, preferred_element_type=jnp.float32) * scale
        dq_ref[:, cols] = dq.astype(jnp.bfloat16)
        dkj = lax.dot_general(ds, qj, tn, preferred_element_type=jnp.float32)
        dvj = lax.dot_general(pb, gj, tn, preferred_element_type=jnp.float32)
        dk = dkj if dk is None else dk + dkj
        dv = dvj if dv is None else dv + dvj
    dk = dk * scale
    for s in range(TOPK):
        t = src_ref[b * TOPK + s]
        rows = slice(s * BLOCK_TOKENS, (s + 1) * BLOCK_TOKENS)
        dk_ref[t] = dk_ref[t] + dk[rows]
        dv_ref[t] = dv_ref[t] + dv[rows]


def attend(slot_src, query_base, peer_of, table, pieces, key_pos, group, groups):
    piece_len = pieces.shape[1]
    run_len = pieces.shape[0] * piece_len
    block_ids = run_len // BLOCK_TOKENS
    targets = table.shape[0]
    head_width = table.shape[-1]
    row_width = pieces.shape[-1] // 2 // groups
    half = BLOCK_TOKENS // 2
    per_piece = piece_len // half

    def half_spec(which, part):
        def index(b, src, base, peer):
            i = 2 * b + part
            return (peer[i // per_piece], i % per_piece, which * groups + group)

        return pl.BlockSpec((None, half, row_width), index)

    table_spec = pl.BlockSpec(table.shape, lambda b, src, base, peer: (0, 0, 0, 0))

    out_row = pl.BlockSpec((BLOCK_TOKENS, row_width), lambda b, src, base, peer: (b, 0))
    pos_spec = pl.BlockSpec((None, 1, TOPK * BLOCK_TOKENS), lambda b, src, base, peer: (b, 0, 0))
    acc_spec = pl.BlockSpec((targets, BLOCK_TOKENS, head_width), lambda b, src, base, peer: (0, 0, 0))
    in_specs = (
        [table_spec]
        + [half_spec(0, 0), half_spec(0, 1), half_spec(1, 0), half_spec(1, 1), pos_spec]
    )
    out_shape = (
        jax.ShapeDtypeStruct((run_len, row_width), jnp.bfloat16),
        jax.ShapeDtypeStruct((run_len, row_width), jnp.bfloat16),
        jax.ShapeDtypeStruct((targets, BLOCK_TOKENS, head_width), jnp.float32),
        jax.ShapeDtypeStruct((targets, BLOCK_TOKENS, head_width), jnp.float32),
    )
    grid_spec = pltpu.PrefetchScalarGridSpec(
        num_scalar_prefetch=3,
        grid=(block_ids,),
        in_specs=in_specs,
        out_specs=(out_row, out_row, acc_spec, acc_spec),
    )
    return pl.pallas_call(
        attention_kernel,
        grid_spec=grid_spec,
        out_shape=out_shape,
        compiler_params=pltpu.CompilerParams(
            dimension_semantics=("arbitrary",),
            vmem_limit_bytes=48 * 1024 * 1024,
        ),
    )(slot_src, query_base, peer_of, table, *([pieces] * 4), key_pos)


def on_device(queries, rotated_keys, value_vectors, block_list, grad_out):
    kv_h = to_heads(rotated_keys, value_vectors)
    size = lax.axis_size("head")
    here = lax.axis_index("head")
    tok, head_count, head_width = queries.shape
    run_len = size * tok
    groups = kv_h.shape[2]
    group_width = head_count // size // groups
    qg = jnp.concatenate(
        [x.reshape(tok, size, head_count // size * head_width) for x in (queries, grad_out)],
        axis=-1,
    )
    qg = jnp.transpose(qg, (1, 0, 2))
    pieces = []
    for k in range(size):
        piece = lax.dynamic_index_in_dim(qg, (here + k) % size, axis=0, keepdims=False)
        if k:
            piece = lax.ppermute(piece, "head", [(i, (i + k) % size) for i in range(size)])
        pieces.append(piece)
    qg_pieces = jnp.stack(pieces)
    peer_of = (here - jnp.arange(size, dtype=jnp.int32)) % size
    head_count = head_count // size
    block_ids = run_len // BLOCK_TOKENS
    peers = lax.axis_size("blk")
    rank = lax.axis_index("blk")
    head_rank = lax.axis_index("head")
    offsets = jnp.arange(BLOCK_TOKENS, dtype=jnp.int32)
    block_range = jnp.arange(block_ids, dtype=jnp.int32)
    peer_range = jnp.arange(peers, dtype=jnp.int32)

    lists_here = lax.dynamic_slice_in_dim(block_list, head_rank * groups, groups, 0)
    lists_mine = lax.dynamic_slice_in_dim(lists_here, rank * block_ids, block_ids, 1)
    by_run = lists_here.reshape(groups, peers, block_ids * TOPK)
    in_mine = (by_run // block_ids) == rank
    named = jnp.max(jnp.where(in_mine, by_run % block_ids, -1), axis=-1)
    present = (named >= 0) & (peer_range != rank)[None, :]
    pick_send = (named[:, :, None] == block_range).astype(jnp.bfloat16)
    take_back = pick_send * present[..., None].astype(jnp.bfloat16)

    kv_local = jnp.transpose(
        kv_h.reshape(2, block_ids, BLOCK_TOKENS, groups, head_width), (3, 1, 0, 2, 4)
    )
    owner = lists_mine // block_ids
    slot_src = jnp.where(owner == rank, peers + lists_mine % block_ids, owner)
    slot_ids = jnp.arange(TOPK, dtype=jnp.int32)
    earlier = slot_ids[None, :] < slot_ids[:, None]
    repeated = jnp.any((lists_mine[..., :, None] == lists_mine[..., None, :]) & earlier, axis=-1)
    key_pos = lists_mine[..., None] * BLOCK_TOKENS + offsets
    key_pos = jnp.where(repeated[..., None], jnp.int32(2**30), key_pos)
    key_pos = key_pos.reshape(groups, block_ids, 1, TOPK * BLOCK_TOKENS)
    query_base = (rank * block_ids + block_range) * BLOCK_TOKENS

    outs, query_grads, backs, locals_ = [], [], [], []

    def heads_layout(parts):
        return jnp.concatenate(parts, axis=1).reshape(run_len, head_count, head_width)

    for g in range(groups):
        send = jnp.einsum(
            "rb,bktd->rktd", pick_send[g], kv_local[g], preferred_element_type=jnp.float32
        ).astype(jnp.bfloat16)
        recv = lax.all_to_all(send, "blk", split_axis=0, concat_axis=0, tiled=True)
        table = jnp.concatenate([recv, kv_local[g]], axis=0)
        o_g, dq_g, dk_acc, dv_acc = attend(
            slot_src[g].reshape(-1), query_base, peer_of, table, qg_pieces, key_pos[g], g, groups
        )
        outs.append(o_g)
        query_grads.append(dq_g)
        acc = jnp.stack([dk_acc, dv_acc], axis=1)
        remote = acc[:peers].astype(jnp.bfloat16)
        local = acc[peers:].astype(jnp.bfloat16)
        if g == groups - 1:
            attn_all, query_grad_all, remote, backs[0] = lax.optimization_barrier(
                (heads_layout(outs), heads_layout(query_grads), remote, backs[0])
            )
        backs.append(lax.all_to_all(remote, "blk", split_axis=0, concat_axis=0, tiled=True))
        locals_.append(local)

    def group_layout(parts):
        return jnp.stack(parts, axis=2).reshape(run_len, groups, head_width)

    key_grads, value_grads = [], []
    for g in range(groups):
        total = locals_[g].astype(jnp.float32) + jnp.einsum(
            "rl,rktd->lktd", take_back[g], backs[g], preferred_element_type=jnp.float32
        )
        total = total.astype(jnp.bfloat16)
        key_grads.append(total[:, 0])
        value_grads.append(total[:, 1])
    attn_out, grad_queries = from_heads(attn_all, query_grad_all)
    key_gradient, value_gradient = from_heads(group_layout(key_grads), group_layout(value_grads))
    return attn_out, grad_queries, key_gradient, value_gradient


def solution(mesh):
    in_specs = (
        P(("blk", "head"), None, None),
        P(("blk", "head"), None, None),
        P(("blk", "head"), None, None),
        P(),
        P(("blk", "head"), None, None),
    )
    out_specs = (
        P(("blk", "head"), None, None),
        P(("blk", "head"), None, None),
        P(("blk", "head"), None, None),
        P(("blk", "head"), None, None),
    )
    return jax.shard_map(
        on_device, mesh=mesh, in_specs=in_specs, out_specs=out_specs, check_vma=False
    )
```

```python
import jax
import jax.numpy as jnp
from jax import lax
from jax.sharding import PartitionSpec as P
from jax.experimental import pallas as pl
from jax.experimental.pallas import tpu as pltpu

BLOCK_TOKENS = 128
TOPK = 8


def exchange(x, part_axis, out_axis):
    size = lax.axis_size("head")
    here = lax.axis_index("head")
    pieces = []
    for k in range(size):
        piece = lax.dynamic_index_in_dim(x, (here + k) % size, axis=part_axis, keepdims=False)
        if k:
            piece = lax.ppermute(piece, "head", [(i, (i + k) % size) for i in range(size)])
        pieces.append(piece)
    ordered = jnp.stack([pieces[(-s) % size] for s in range(size)], axis=out_axis)
    return jnp.roll(ordered, here, axis=out_axis)


def to_heads(*xs):
    size = lax.axis_size("head")
    x = jnp.stack(xs)
    n, tok, heads, d = x.shape
    return lax.all_to_all(x, "head", split_axis=2, concat_axis=1, tiled=True)


def from_heads(*xs):
    size = lax.axis_size("head")
    x = jnp.stack(xs)
    n, run, part, d = x.shape
    x = x.reshape(n, size, run // size, part, d)
    both = exchange(x, 1, 2).reshape(n, run // size, size * part, d)
    return tuple(both[i] for i in range(len(xs)))


def attention_kernel(src_ref, base_ref, peer_ref, *refs):
    table_ref, lo_ref, hi_ref, kpos_ref = refs[:4]
    o_ref, dq_ref, dk_ref, dv_ref = refs[4:]
    b = pl.program_id(0)

    @pl.when(b == 0)
    def _():
        dk_ref[...] = jnp.zeros_like(dk_ref)
        dv_ref[...] = jnp.zeros_like(dv_ref)

    head_width = table_ref.shape[-1]
    width = lo_ref.shape[-1] // 2
    group_width = width // head_width
    scale = head_width ** (-0.5)
    slots = [src_ref[b * TOPK + s] for s in range(TOPK)]
    keys = jnp.concatenate([table_ref[t, 0] for t in slots], axis=0)
    values = jnp.concatenate([table_ref[t, 1] for t in slots], axis=0)
    query_pos = base_ref[b] + lax.broadcasted_iota(jnp.int32, (BLOCK_TOKENS, 1), 0)
    allowed = kpos_ref[...] <= query_pos
    nt = (((1,), (1,)), ((), ()))
    tn = (((0,), (0,)), ((), ()))
    dk = None
    dv = None
    for j in range(group_width):
        cols = slice(j * head_width, (j + 1) * head_width)
        dcols = slice(width + j * head_width, width + (j + 1) * head_width)
        qj = jnp.concatenate([lo_ref[:, cols], hi_ref[:, cols]], axis=0)
        gj = jnp.concatenate([lo_ref[:, dcols], hi_ref[:, dcols]], axis=0)
        s = lax.dot_general(qj, keys, nt, preferred_element_type=jnp.float32) * scale
        s = jnp.where(allowed, s, -jnp.inf)
        m = jnp.max(s, axis=-1, keepdims=True)
        lt = m + jnp.log(jnp.sum(jnp.exp(s - m), axis=-1, keepdims=True))
        p = jnp.exp(s - lt)
        pb = p.astype(jnp.bfloat16)
        o = jnp.dot(pb, values, preferred_element_type=jnp.float32).astype(jnp.bfloat16)
        o_ref[:, cols] = o
        rd = jnp.sum(gj.astype(jnp.float32) * o.astype(jnp.float32), axis=-1, keepdims=True)
        dp = lax.dot_general(gj, values, nt, preferred_element_type=jnp.float32)
        ds = (p * (dp - rd)).astype(jnp.bfloat16)
        dq = jnp.dot(ds, keys, preferred_element_type=jnp.float32) * scale
        dq_ref[:, cols] = dq.astype(jnp.bfloat16)
        dkj = lax.dot_general(ds, qj, tn, preferred_element_type=jnp.float32)
        dvj = lax.dot_general(pb, gj, tn, preferred_element_type=jnp.float32)
        dk = dkj if dk is None else dk + dkj
        dv = dvj if dv is None else dv + dvj
    dk = dk * scale
    for s in range(TOPK):
        t = src_ref[b * TOPK + s]
        rows = slice(s * BLOCK_TOKENS, (s + 1) * BLOCK_TOKENS)
        dk_ref[t] = dk_ref[t] + dk[rows]
        dv_ref[t] = dv_ref[t] + dv[rows]


def attend(slot_src, query_base, peer_of, table, pieces, key_pos, group, groups):
    piece_len = pieces.shape[1]
    run_len = pieces.shape[0] * piece_len
    block_ids = run_len // BLOCK_TOKENS
    targets = table.shape[0]
    head_width = table.shape[-1]
    row_width = pieces.shape[-1] // 2 // groups
    block_width = 2 * row_width
    half = BLOCK_TOKENS // 2
    per_piece = piece_len // half

    def half_spec(part):
        def index(b, src, base, peer):
            i = 2 * b + part
            return (peer[i // per_piece], i % per_piece, group)

        return pl.BlockSpec((None, half, block_width), index)

    table_spec = pl.BlockSpec(table.shape, lambda b, src, base, peer: (0, 0, 0, 0))

    out_row = pl.BlockSpec((BLOCK_TOKENS, row_width), lambda b, src, base, peer: (b, 0))
    pos_spec = pl.BlockSpec((None, 1, TOPK * BLOCK_TOKENS), lambda b, src, base, peer: (b, 0, 0))
    acc_spec = pl.BlockSpec((targets, BLOCK_TOKENS, head_width), lambda b, src, base, peer: (0, 0, 0))
    in_specs = (
        [table_spec]
        + [half_spec(0), half_spec(1), pos_spec]
    )
    out_shape = (
        jax.ShapeDtypeStruct((run_len, row_width), jnp.bfloat16),
        jax.ShapeDtypeStruct((run_len, row_width), jnp.bfloat16),
        jax.ShapeDtypeStruct((targets, BLOCK_TOKENS, head_width), jnp.float32),
        jax.ShapeDtypeStruct((targets, BLOCK_TOKENS, head_width), jnp.float32),
    )
    grid_spec = pltpu.PrefetchScalarGridSpec(
        num_scalar_prefetch=3,
        grid=(block_ids,),
        in_specs=in_specs,
        out_specs=(out_row, out_row, acc_spec, acc_spec),
    )
    return pl.pallas_call(
        attention_kernel,
        grid_spec=grid_spec,
        out_shape=out_shape,
        compiler_params=pltpu.CompilerParams(
            dimension_semantics=("arbitrary",),
            vmem_limit_bytes=48 * 1024 * 1024,
        ),
    )(slot_src, query_base, peer_of, table, pieces, pieces, key_pos)


def on_device(queries, rotated_keys, value_vectors, block_list, grad_out):
    kv_h = to_heads(rotated_keys, value_vectors)
    size = lax.axis_size("head")
    here = lax.axis_index("head")
    tok, head_count, head_width = queries.shape
    run_len = size * tok
    groups = kv_h.shape[2]
    group_width = head_count // size // groups
    qg = jnp.stack(
        [x.reshape(tok, size, groups, group_width * head_width) for x in (queries, grad_out)],
        axis=3,
    ).reshape(tok, size, 2 * head_count // size * head_width)
    qg = jnp.transpose(qg, (1, 0, 2))
    pieces = []
    for k in range(size):
        piece = lax.dynamic_index_in_dim(qg, (here + k) % size, axis=0, keepdims=False)
        if k:
            piece = lax.ppermute(piece, "head", [(i, (i + k) % size) for i in range(size)])
        pieces.append(piece)
    qg_pieces = jnp.stack(pieces)
    peer_of = (here - jnp.arange(size, dtype=jnp.int32)) % size
    head_count = head_count // size
    block_ids = run_len // BLOCK_TOKENS
    peers = lax.axis_size("blk")
    rank = lax.axis_index("blk")
    head_rank = lax.axis_index("head")
    offsets = jnp.arange(BLOCK_TOKENS, dtype=jnp.int32)
    block_range = jnp.arange(block_ids, dtype=jnp.int32)
    peer_range = jnp.arange(peers, dtype=jnp.int32)

    lists_here = lax.dynamic_slice_in_dim(block_list, head_rank * groups, groups, 0)
    lists_mine = lax.dynamic_slice_in_dim(lists_here, rank * block_ids, block_ids, 1)
    by_run = lists_here.reshape(groups, peers, block_ids * TOPK)
    in_mine = (by_run // block_ids) == rank
    named = jnp.max(jnp.where(in_mine, by_run % block_ids, -1), axis=-1)
    present = (named >= 0) & (peer_range != rank)[None, :]
    pick_send = (named[:, :, None] == block_range).astype(jnp.bfloat16)
    take_back = pick_send * present[..., None].astype(jnp.bfloat16)

    kv_local = jnp.transpose(
        kv_h.reshape(2, block_ids, BLOCK_TOKENS, groups, head_width), (3, 1, 0, 2, 4)
    )
    owner = lists_mine // block_ids
    slot_src = jnp.where(owner == rank, peers + lists_mine % block_ids, owner)
    slot_ids = jnp.arange(TOPK, dtype=jnp.int32)
    earlier = slot_ids[None, :] < slot_ids[:, None]
    repeated = jnp.any((lists_mine[..., :, None] == lists_mine[..., None, :]) & earlier, axis=-1)
    key_pos = lists_mine[..., None] * BLOCK_TOKENS + offsets
    key_pos = jnp.where(repeated[..., None], jnp.int32(2**30), key_pos)
    key_pos = key_pos.reshape(groups, block_ids, 1, TOPK * BLOCK_TOKENS)
    query_base = (rank * block_ids + block_range) * BLOCK_TOKENS

    outs, query_grads, backs, locals_ = [], [], [], []

    def heads_layout(parts):
        return jnp.concatenate(parts, axis=1).reshape(run_len, head_count, head_width)

    for g in range(groups):
        send = jnp.einsum(
            "rb,bktd->rktd", pick_send[g], kv_local[g], preferred_element_type=jnp.float32
        ).astype(jnp.bfloat16)
        recv = lax.all_to_all(send, "blk", split_axis=0, concat_axis=0, tiled=True)
        table = jnp.concatenate([recv, kv_local[g]], axis=0)
        o_g, dq_g, dk_acc, dv_acc = attend(
            slot_src[g].reshape(-1), query_base, peer_of, table, qg_pieces, key_pos[g], g, groups
        )
        outs.append(o_g)
        query_grads.append(dq_g)
        acc = jnp.stack([dk_acc, dv_acc], axis=1)
        remote = acc[:peers].astype(jnp.bfloat16)
        local = acc[peers:].astype(jnp.bfloat16)
        if g == groups - 1:
            attn_all, query_grad_all, remote, backs[0] = lax.optimization_barrier(
                (heads_layout(outs), heads_layout(query_grads), remote, backs[0])
            )
        backs.append(lax.all_to_all(remote, "blk", split_axis=0, concat_axis=0, tiled=True))
        locals_.append(local)

    def group_layout(parts):
        return jnp.stack(parts, axis=2).reshape(run_len, groups, head_width)

    key_grads, value_grads = [], []
    for g in range(groups):
        total = locals_[g].astype(jnp.float32) + jnp.einsum(
            "rl,rktd->lktd", take_back[g], backs[g], preferred_element_type=jnp.float32
        )
        total = total.astype(jnp.bfloat16)
        key_grads.append(total[:, 0])
        value_grads.append(total[:, 1])
    attn_out, grad_queries = from_heads(attn_all, query_grad_all)
    key_gradient, value_gradient = from_heads(group_layout(key_grads), group_layout(value_grads))
    return attn_out, grad_queries, key_gradient, value_gradient


def solution(mesh):
    in_specs = (
        P(("blk", "head"), None, None),
        P(("blk", "head"), None, None),
        P(("blk", "head"), None, None),
        P(),
        P(("blk", "head"), None, None),
    )
    out_specs = (
        P(("blk", "head"), None, None),
        P(("blk", "head"), None, None),
        P(("blk", "head"), None, None),
        P(("blk", "head"), None, None),
    )
    return jax.shard_map(
        on_device, mesh=mesh, in_specs=in_specs, out_specs=out_specs, check_vma=False
    )
```
